128 devices in a mesh: dom: 32 (over x, z, core), feat: 4 (over y).
Axes of the slice: x: 4, y: 4, z: 4, core: 2. Of those that a mesh axis runs over, the one named last changes fastest.
Arguments:
- features: bfloat16 [128, 131072], P('feat', 'dom'), may hold values from -6 to 6
- neighbours: int32 [8, 131072], P(None, 'dom'), may hold values from 0 to 27647, as said below
- hub_rows: int32 [20480], P('dom'), may hold values from 0 to 4095, as said below
- send_rows: int32 [96, 1024], P('dom'), may hold values from 0 to 4095
- labels: int32 [131072], P('dom'), may hold values from 0 to 171
- inner_self: bfloat16 [256, 128], P('feat'), may hold values from -0.375 to 0.375
- inner_neighbour: bfloat16 [256, 128], P('feat'), may hold values from -0.375 to 0.375
- outer_self: bfloat16 [172, 256], replicated, may hold values from -1.796875 to 1.796875
- outer_neighbour: bfloat16 [172, 256], replicated, may hold values from -1.796875 to 1.796875
Outputs:
- grad_inner_self: float32 [256, 128], P('feat')
- grad_inner_neighbour: float32 [256, 128], P('feat')
- grad_outer_self: float32 [172, 256], P(None, 'feat')
- grad_outer_neighbour: float32 [172, 256], P(None, 'feat')
The draws below stay inside these ranges and needn't reach their ends.
Inputs may be any that keep to these rules, and one draw needn't show every extreme that they name: `hub_rows`: within each owner's block of 640 entries the rows are distinct; each block holds rows 0 and 4095. `neighbours`: entries below 4096 are own rows, the next 20480 are hubs, the rest are rows received in rounds.
All inputs are finite; a program needn't handle non-finite values.
Results may differ from the reference program's by a relative error of at most 0.004.
The reference program's roundings to bfloat16 on the way count: a program that leaves them out, or rounds other values in their place, can miss the bound.
Values may be sent and summed in bfloat16 or wider, within the bound.
No kernel may reach another device: no remote copies, remote signals or barrier semaphores. Data moves between devices by JAX's collectives and lax.ppermute only.
A program may use at most 128 MiB of HBM per device.

```python
import jax
import jax.numpy as jnp
from jax import lax

F_IN = 128
H = 256
C = 172
DEG = 8
ROUNDS = 3
NODE_DEV = 4096
HUB_DEV = 640
BND = 1024
NODES = 131072
HUBS = 20480
PAIRS = 96
N_DOM = 32


def draw_hub_rows(key, part):
    owners = HUBS // HUB_DEV

    def one_owner(owner_key):
        first_key, second_key = jax.random.split(owner_key)
        middle = jax.random.permutation(first_key, NODE_DEV - 2)[:HUB_DEV - 2] + 1
        chosen = jnp.concatenate([middle.astype(jnp.int32), jnp.array([0, NODE_DEV - 1], jnp.int32)])
        shuffle = jax.random.permutation(second_key, HUB_DEV)
        return chosen[shuffle]
    return jax.vmap(one_owner)(jax.random.split(key, owners)).reshape(-1).astype(jnp.int32)


def draw_neighbours(key, part):
    category_key, local_key, hub_key, band_key = jax.random.split(key, 4)
    layout = (DEG, NODES)
    category = jax.random.randint(category_key, layout, 0, 4)
    local_pick = jax.random.randint(local_key, layout, 0, NODE_DEV)
    hub_pick = NODE_DEV + jax.random.randint(hub_key, layout, 0, HUBS)
    band_pick = NODE_DEV + HUBS + jax.random.randint(band_key, layout, 0, ROUNDS * BND)
    chosen = jnp.where(category < 2, local_pick, jnp.where(category == 2, hub_pick, band_pick))
    chosen = chosen.at[0, 0].set(0)
    chosen = chosen.at[DEG - 1, NODES - 1].set(NODE_DEV + HUBS + ROUNDS * BND - 1)
    return chosen.astype(jnp.int32)


def with_ends(drawn, rng, low, largest):
    extent = drawn.shape
    index_at = [jax.random.randint(jax.random.fold_in(rng, axis), (), 0, extent[axis]) for axis in range(len(extent))]
    drawn = drawn.at[tuple(index_at)].set(low)
    longest = extent.index(max(extent))
    index_at[longest] = (index_at[longest] + 1) % extent[longest]
    return drawn.at[tuple(index_at)].set(largest)


def block_levels(own_key, extent, cuts, least, top_value):
    factor_of = 1.0
    for dim, shards_of in cuts:
        heights = jax.random.uniform(jax.random.fold_in(jax.random.fold_in(own_key, 6), dim), (shards_of,), jnp.float32, least / len(cuts), top_value / len(cuts))
        factor_of = factor_of * jnp.repeat(jnp.exp(heights), extent[dim] // shards_of).reshape((-1,) + (1,) * (len(extent) - 1 - dim))
    return factor_of


def gaussian(own_key, dims, scale, bound, pieces=(), kind=jnp.bfloat16):
    values = jax.random.normal(own_key, dims, jnp.float32) * scale
    if len(pieces) > 0:
        values = block_levels(own_key, dims, pieces, -0.22, 0.18) * values
    return jnp.clip(values, min=-bound, max=bound).astype(kind)


def setup_inputs(seed: int = 0) -> dict:
    splits = jax.random.split(jax.random.key(seed), 10)
    features = gaussian(splits[0], (F_IN, NODES), 1.0, 6.0, ((0, 4), (1, 32)))
    neighbours = draw_neighbours(jax.random.fold_in(splits[9], 71), 0)
    hub_rows = draw_hub_rows(jax.random.fold_in(splits[9], 71), 0)
    send_rows = with_ends(jax.random.randint(splits[3], (PAIRS, BND), 0, NODE_DEV), jax.random.fold_in(splits[3], 1), 0, NODE_DEV - 1).astype(jnp.int32)
    labels = with_ends(jax.random.randint(splits[4], (NODES,), 0, C), jax.random.fold_in(splits[4], 1), 0, C - 1).astype(jnp.int32)
    inner_self = gaussian(splits[5], (H, F_IN), (2 * F_IN) ** -0.5, 0.375, ((0, 4),))
    inner_neighbour = gaussian(splits[6], (H, F_IN), (2 * F_IN) ** -0.5, 0.375, ((0, 4),))
    outer_self = gaussian(splits[7], (C, H), 0.3, 1.796875)
    outer_neighbour = gaussian(splits[8], (C, H), 0.3, 1.796875)
    return dict(features=features, neighbours=neighbours, hub_rows=hub_rows, send_rows=send_rows, labels=labels, inner_self=inner_self, inner_neighbour=inner_neighbour, outer_self=outer_self, outer_neighbour=outer_neighbour)


loss_scale = 4096.0


def reference(features, neighbours, hub_rows, send_rows, labels, inner_self, inner_neighbour, outer_self, outer_neighbour):
    def blocks(matrix):
        return matrix.reshape(matrix.shape[0], N_DOM, NODE_DEV).transpose(1, 0, 2)

    neigh_blocks = blocks(neighbours)
    hub_blocks = hub_rows.reshape(N_DOM, HUB_DEV)
    send_blocks = send_rows.reshape(N_DOM, ROUNDS, BND)
    label_blocks = labels.reshape(N_DOM, NODE_DEV)
    owners = jnp.arange(N_DOM, dtype=jnp.int32)
    partners = [jnp.bitwise_xor(owners, jnp.int32(1 << bit_index)) for bit_index in range(ROUNDS)]

    def take_cols(block_rows, index_rows):
        return jnp.take(block_rows, index_rows, axis=1)

    def aggregate(local):
        width = local.shape[1]
        hub_part = jax.vmap(take_cols)(local, hub_blocks)
        hub_all = hub_part.transpose(1, 0, 2).reshape(width, HUBS)
        sent = jax.vmap(take_cols)(local, send_blocks)
        received = jnp.stack([sent[partners[bit_index], :, bit_index, :] for bit_index in range(ROUNDS)], axis=2)
        received = received.reshape(N_DOM, width, ROUNDS * BND)

        def one_part(packed):
            block_rows, got_rows, index_rows = packed
            table = jnp.concatenate([block_rows, hub_all, got_rows], axis=1)
            picked = jnp.take(table, index_rows, axis=1).astype(jnp.float32)
            return (jnp.sum(picked, axis=1) / DEG).astype(jnp.bfloat16)

        return lax.map(one_part, (local, received, neigh_blocks))

    feat_blocks = blocks(features)
    mean_one = aggregate(feat_blocks)
    pre_act = jnp.einsum('hf,dfn->dhn', inner_self.astype(jnp.float32), feat_blocks.astype(jnp.float32))
    pre_act = pre_act + jnp.einsum('hf,dfn->dhn', inner_neighbour.astype(jnp.float32), mean_one.astype(jnp.float32))
    hidden = jnp.maximum(pre_act, 0.0).astype(jnp.bfloat16)
    mean_two = aggregate(hidden)
    logits = jnp.einsum('ch,dhn->dcn', outer_self.astype(jnp.float32), hidden.astype(jnp.float32))
    logits = logits + jnp.einsum('ch,dhn->dcn', outer_neighbour.astype(jnp.float32), mean_two.astype(jnp.float32))
    expd = jnp.exp(logits)
    probs = expd / jnp.sum(expd, axis=1, keepdims=True)
    classes = jnp.arange(C, dtype=jnp.int32)
    onehot = (classes[None, :, None] == label_blocks[:, None, :]).astype(jnp.float32)
    logit_grad = ((probs - onehot) * (loss_scale / NODES)).astype(jnp.bfloat16)
    grad_outer_self = jnp.einsum('dcn,dhn->ch', logit_grad.astype(jnp.float32), hidden.astype(jnp.float32))
    grad_outer_neighbour = jnp.einsum('dcn,dhn->ch', logit_grad.astype(jnp.float32), mean_two.astype(jnp.float32))
    direct = jnp.einsum('ch,dcn->dhn', outer_self.astype(jnp.float32), logit_grad.astype(jnp.float32))
    back_mean = jnp.einsum('ch,dcn->dhn', outer_neighbour.astype(jnp.float32), logit_grad.astype(jnp.float32)).astype(jnp.bfloat16)
    span = NODE_DEV + HUBS + ROUNDS * BND

    def spread_one(carry, packed):
        grad_rows, index_rows = packed
        updates = jnp.broadcast_to(grad_rows[:, None, :], (H, DEG, NODE_DEV)).reshape(H, DEG * NODE_DEV).astype(jnp.float32)
        table = jnp.zeros((H, span), jnp.float32).at[:, index_rows.reshape(-1)].add(updates) * (1.0 / DEG)
        band = table[:, NODE_DEV + HUBS:].reshape(H, ROUNDS, BND).astype(jnp.bfloat16)
        return carry + table[:, NODE_DEV:NODE_DEV + HUBS], (table[:, :NODE_DEV], band)

    hub_total, (local_grad, band_grad) = lax.scan(spread_one, jnp.zeros((H, HUBS), jnp.float32), (back_mean, neigh_blocks))
    hub_back = hub_total.reshape(H, N_DOM, HUB_DEV).transpose(1, 0, 2)
    returned = jnp.stack([band_grad[partners[bit_index], :, bit_index, :] for bit_index in range(ROUNDS)], axis=2)

    def land(grad_rows, hub_grad, hub_index, back_rows, send_index):
        grad_rows = grad_rows.at[:, hub_index].add(hub_grad)
        for bit_index in range(ROUNDS):
            grad_rows = grad_rows.at[:, send_index[bit_index]].add(back_rows[:, bit_index, :].astype(jnp.float32))
        return grad_rows

    grad_hidden = jax.vmap(land)(direct + local_grad, hub_back, hub_blocks, returned, send_blocks)
    grad_pre = jnp.where(hidden > 0, grad_hidden, 0.0).astype(jnp.bfloat16)
    grad_inner_self = jnp.einsum('dhn,dfn->hf', grad_pre.astype(jnp.float32), feat_blocks.astype(jnp.float32))
    grad_inner_neighbour = jnp.einsum('dhn,dfn->hf', grad_pre.astype(jnp.float32), mean_one.astype(jnp.float32))
    return (grad_inner_self, grad_inner_neighbour, grad_outer_self, grad_outer_neighbour)
```

```python
import jax
import jax.numpy as jnp
from jax import lax
from jax.sharding import PartitionSpec as P

from jax.experimental import pallas as pl
from jax.experimental.pallas import tpu as pltpu

loss_scale = 4096.0


def gather_mean(table, neighbours, block=512):
    size, width = table.shape
    degree, nodes = neighbours.shape

    def kernel(nb_ref, tab_ref, out_ref):
        base = pl.program_id(0) * block

        def group(g, carry):
            picked = []
            for r in range(8):
                n = base + g * 8 + r
                acc = tab_ref[pl.ds(nb_ref[0, n], 1), :]
                for k in range(1, degree):
                    acc = acc + tab_ref[pl.ds(nb_ref[k, n], 1), :]
                picked.append(acc)
            start = pl.multiple_of(g * 8, 8)
            out_ref[pl.ds(start, 8), :] = jnp.concatenate(picked, axis=0) / degree
            return carry

        lax.fori_loop(0, block // 8, group, 0, unroll=2)

    return pl.pallas_call(
        kernel,
        grid_spec=pltpu.PrefetchScalarGridSpec(
            num_scalar_prefetch=1,
            grid=(nodes // block,),
            in_specs=[pl.BlockSpec((size, width), lambda j, nb: (0, 0))],
            out_specs=pl.BlockSpec((block, width), lambda j, nb: (j, 0)),
        ),
        out_shape=jax.ShapeDtypeStruct((nodes, width), jnp.float32),
    )(neighbours, table)


def scatter_mean(rows, neighbours, size, block=512):
    nodes, width = rows.shape
    degree = neighbours.shape[0]

    def kernel(nb_ref, rows_ref, out_ref):
        j = pl.program_id(0)

        @pl.when(j == 0)
        def _():
            out_ref[...] = jnp.zeros_like(out_ref)

        base = j * block

        def step(i, carry):
            n = base + i
            x = rows_ref[pl.ds(i, 1), :]
            for k in range(degree):
                s = nb_ref[k, n]
                out_ref[pl.ds(s, 1), :] = out_ref[pl.ds(s, 1), :] + x
            return carry

        lax.fori_loop(0, block, step, 0, unroll=8)

        @pl.when(j == pl.num_programs(0) - 1)
        def _():
            out_ref[...] = out_ref[...] * (1.0 / degree)

    return pl.pallas_call(
        kernel,
        grid_spec=pltpu.PrefetchScalarGridSpec(
            num_scalar_prefetch=1,
            grid=(nodes // block,),
            in_specs=[pl.BlockSpec((block, width), lambda j, nb: (j, 0))],
            out_specs=pl.BlockSpec((size, width), lambda j, nb: (0, 0)),
        ),
        out_shape=jax.ShapeDtypeStruct((size, width), jnp.float32),
        compiler_params=pltpu.CompilerParams(dimension_semantics=("arbitrary",)),
    )(neighbours, rows)


def partner(value, axis, stride):
    mask = 2**stride
    pairs = [(source, source ^ mask) for source in range(lax.axis_size(axis))]
    return lax.ppermute(value, axis, pairs)


def trade(piece, bit_index):
    return partner(piece, "dom", bit_index)


def widen(first_rows, second_rows):
    return (
        lax.all_gather(first_rows, "feat", axis=0, tiled=True),
        lax.all_gather(second_rows, "feat", axis=0, tiled=True),
    )


def average(table_rows, neighbours):
    summed = gather_mean(table_rows.astype(jnp.float32), neighbours)
    return summed.T.astype(jnp.bfloat16)


def source_table(local, hub_rows, send_rows):
    local_rows = local.T
    hub_local = jnp.take(local_rows, hub_rows, axis=0)
    hub_all = lax.all_gather(hub_local, "dom", axis=0, tiled=True)
    received = [
        trade(jnp.take(local_rows, send_rows[bit_index], axis=0), bit_index)
        for bit_index in range(send_rows.shape[0])
    ]
    return jnp.concatenate([local_rows, hub_all] + received, axis=0)


def contract(left, right):
    return lax.dot_general(
        left, right, (((1,), (1,)), ((), ())), preferred_element_type=jnp.float32
    )


def transpose_times(left, right):
    return lax.dot_general(
        left, right, (((0,), (0,)), ((), ())), preferred_element_type=jnp.float32
    )


def class_gradient(logits, labels, nodes_all):
    expd = jnp.exp(logits)
    probs = expd / jnp.sum(expd, axis=0, keepdims=True)
    classes = lax.broadcasted_iota(jnp.int32, logits.shape, 0)
    onehot = (classes == labels[None, :]).astype(jnp.float32)
    return ((probs - onehot) * (loss_scale / nodes_all)).astype(jnp.bfloat16)


def body(
    features,
    neighbours,
    hub_rows,
    send_rows,
    labels,
    inner_self,
    inner_neighbour,
    outer_self,
    outer_neighbour,
):
    rows = features.shape[1]
    nodes_all = rows * lax.axis_size("dom")
    mean_one = average(source_table(features, hub_rows, send_rows), neighbours)
    full_input, full_mean = widen(features, mean_one)
    pre_act = jnp.dot(inner_self, full_input, preferred_element_type=jnp.float32)
    pre_act = pre_act + jnp.dot(inner_neighbour, full_mean, preferred_element_type=jnp.float32)
    hidden = jnp.maximum(pre_act, 0.0).astype(jnp.bfloat16)
    mean_two = average(source_table(hidden, hub_rows, send_rows), neighbours)
    width = hidden.shape[0]
    offset = lax.axis_index("feat") * width
    self_cols = lax.dynamic_slice_in_dim(outer_self, offset, width, 1)
    neigh_cols = lax.dynamic_slice_in_dim(outer_neighbour, offset, width, 1)
    full_hidden, full_two = widen(hidden, mean_two)
    logits = jnp.dot(outer_self, full_hidden, preferred_element_type=jnp.float32)
    logits = logits + jnp.dot(outer_neighbour, full_two, preferred_element_type=jnp.float32)
    logit_grad = class_gradient(logits, labels, nodes_all)
    grad_outer_self = contract(logit_grad, hidden)
    grad_outer_neighbour = contract(logit_grad, mean_two)
    grad_outer_self, grad_outer_neighbour = lax.psum((grad_outer_self, grad_outer_neighbour), "dom")
    direct = transpose_times(self_cols, logit_grad)
    back_mean = transpose_times(neigh_cols, logit_grad).astype(jnp.bfloat16)
    degree = neighbours.shape[0]
    hub_count = lax.axis_size("dom") * hub_rows.shape[0]
    band = send_rows.shape[1]
    span = rows + hub_count + send_rows.shape[0] * band
    back_rows = back_mean.T.astype(jnp.float32)
    spread = scatter_mean(back_rows, neighbours, span)
    grad_rows = direct.T + spread[:rows]
    hub_back = lax.psum_scatter(
        spread[rows : rows + hub_count], "dom", scatter_dimension=0, tiled=True
    )
    grad_rows = grad_rows.at[hub_rows].add(hub_back)
    base = rows + hub_count
    for bit_index in range(send_rows.shape[0]):
        outgoing = spread[base + bit_index * band : base + (bit_index + 1) * band].astype(
            jnp.bfloat16
        )
        returned = trade(outgoing, bit_index)
        grad_rows = grad_rows.at[send_rows[bit_index]].add(returned.astype(jnp.float32))
    grad_hidden = grad_rows.T
    grad_pre = jnp.where(hidden > 0, grad_hidden, 0.0).astype(jnp.bfloat16)
    grad_inner_self = contract(grad_pre, full_input)
    grad_inner_neighbour = contract(grad_pre, full_mean)
    summed = lax.psum((grad_inner_self, grad_inner_neighbour), "dom")
    return (summed[0], summed[1], grad_outer_self, grad_outer_neighbour)


def solution(mesh):
    return jax.shard_map(
        body,
        mesh=mesh,
        in_specs=(
            P("feat", "dom"),
            P(None, "dom"),
            P("dom"),
            P("dom", None),
            P("dom"),
            P("feat", None),
            P("feat", None),
            P(),
            P(),
        ),
        out_specs=(P("feat", None), P("feat", None), P(None, "feat"), P(None, "feat")),
        check_vma=False,
    )
```

```python
import jax
import jax.numpy as jnp
from jax import lax
from jax.sharding import PartitionSpec as P

from jax.experimental import pallas as pl
from jax.experimental.pallas import tpu as pltpu

loss_scale = 4096.0


def gather_mean(table, neighbours, block=512):
    size, width = table.shape
    degree, nodes = neighbours.shape

    def kernel(nb_ref, tab_ref, out_ref):
        base = pl.program_id(0) * block

        def group(g, carry):
            picked = []
            for r in range(8):
                n = base + g * 8 + r
                acc = tab_ref[pl.ds(nb_ref[0, n], 1), :]
                for k in range(1, degree):
                    acc = acc + tab_ref[pl.ds(nb_ref[k, n], 1), :]
                picked.append(acc)
            start = pl.multiple_of(g * 8, 8)
            out_ref[pl.ds(start, 8), :] = jnp.concatenate(picked, axis=0) / degree
            return carry

        lax.fori_loop(0, block // 8, group, 0, unroll=2)

    return pl.pallas_call(
        kernel,
        grid_spec=pltpu.PrefetchScalarGridSpec(
            num_scalar_prefetch=1,
            grid=(nodes // block,),
            in_specs=[pl.BlockSpec((size, width), lambda j, nb: (0, 0))],
            out_specs=pl.BlockSpec((block, width), lambda j, nb: (j, 0)),
        ),
        out_shape=jax.ShapeDtypeStruct((nodes, width), jnp.float32),
    )(neighbours, table)


def scatter_mean(rows, neighbours, size):
    nodes, width = rows.shape
    degree = neighbours.shape[0]
    half = degree // 2

    def kernel(nb_ref, rows_ref, first_ref, second_ref):
        first_ref[...] = jnp.zeros_like(first_ref)
        second_ref[...] = jnp.zeros_like(second_ref)

        def step(n, carry):
            x = rows_ref[pl.ds(n, 1), :]
            for k in range(half):
                s = nb_ref[k, n]
                t = nb_ref[k + half, n]
                first_ref[pl.ds(s, 1), :] = first_ref[pl.ds(s, 1), :] + x
                second_ref[pl.ds(t, 1), :] = second_ref[pl.ds(t, 1), :] + x
            return carry

        lax.fori_loop(0, nodes, step, 0, unroll=4)

    first, second = pl.pallas_call(
        kernel,
        in_specs=[
            pl.BlockSpec(memory_space=pltpu.SMEM),
            pl.BlockSpec(memory_space=pltpu.VMEM),
        ],
        out_specs=(
            pl.BlockSpec(memory_space=pltpu.VMEM),
            pl.BlockSpec(memory_space=pltpu.VMEM),
        ),
        out_shape=(
            jax.ShapeDtypeStruct((size, width), jnp.float32),
            jax.ShapeDtypeStruct((size, width), jnp.float32),
        ),
    )(neighbours, rows)
    return (first + second) * (1.0 / degree)


def tree_sum(value, axis):
    count = lax.axis_size(axis)
    stride = 1
    while stride < count:
        pairs = [(source, source ^ stride) for source in range(count)]
        value = value + lax.ppermute(value, axis, pairs)
        stride *= 2
    return value


def partner(value, axis, stride):
    mask = 2**stride
    pairs = [(source, source ^ mask) for source in range(lax.axis_size(axis))]
    return lax.ppermute(value, axis, pairs)


def trade(piece, bit_index):
    return partner(piece, "dom", bit_index)


def widen(first_rows, second_rows):
    return (
        lax.all_gather(first_rows, "feat", axis=0, tiled=True),
        lax.all_gather(second_rows, "feat", axis=0, tiled=True),
    )


def average(table_rows, neighbours):
    summed = gather_mean(table_rows.astype(jnp.float32), neighbours)
    return summed.T.astype(jnp.bfloat16)


def source_table(local, hub_rows, send_rows):
    local_rows = local.T
    hub_local = jnp.take(local_rows, hub_rows, axis=0)
    hub_all = lax.all_gather(hub_local, "dom", axis=0, tiled=True)
    received = [
        trade(jnp.take(local_rows, send_rows[bit_index], axis=0), bit_index)
        for bit_index in range(send_rows.shape[0])
    ]
    return jnp.concatenate([local_rows, hub_all] + received, axis=0)


def contract(left, right):
    return lax.dot_general(
        left, right, (((1,), (1,)), ((), ())), preferred_element_type=jnp.float32
    )


def transpose_times(left, right):
    return lax.dot_general(
        left, right, (((0,), (0,)), ((), ())), preferred_element_type=jnp.float32
    )


def class_gradient(logits, labels, nodes_all):
    expd = jnp.exp(logits)
    probs = expd / jnp.sum(expd, axis=0, keepdims=True)
    classes = lax.broadcasted_iota(jnp.int32, logits.shape, 0)
    onehot = (classes == labels[None, :]).astype(jnp.float32)
    return ((probs - onehot) * (loss_scale / nodes_all)).astype(jnp.bfloat16)


def body(
    features,
    neighbours,
    hub_rows,
    send_rows,
    labels,
    inner_self,
    inner_neighbour,
    outer_self,
    outer_neighbour,
):
    rows = features.shape[1]
    nodes_all = rows * lax.axis_size("dom")
    mean_one = average(source_table(features, hub_rows, send_rows), neighbours)
    full_input, full_mean = widen(features, mean_one)
    pre_act = jnp.dot(inner_self, full_input, preferred_element_type=jnp.float32)
    pre_act = pre_act + jnp.dot(inner_neighbour, full_mean, preferred_element_type=jnp.float32)
    hidden = jnp.maximum(pre_act, 0.0).astype(jnp.bfloat16)
    mean_two = average(source_table(hidden, hub_rows, send_rows), neighbours)
    width = hidden.shape[0]
    offset = lax.axis_index("feat") * width
    self_cols = lax.dynamic_slice_in_dim(outer_self, offset, width, 1)
    neigh_cols = lax.dynamic_slice_in_dim(outer_neighbour, offset, width, 1)
    full_hidden, full_two = widen(hidden, mean_two)
    logits = jnp.dot(outer_self, full_hidden, preferred_element_type=jnp.float32)
    logits = logits + jnp.dot(outer_neighbour, full_two, preferred_element_type=jnp.float32)
    logit_grad = class_gradient(logits, labels, nodes_all)
    grad_outer_self = contract(logit_grad, hidden)
    grad_outer_neighbour = contract(logit_grad, mean_two)
    outer_both = tree_sum(jnp.concatenate([grad_outer_self, grad_outer_neighbour], axis=0), "dom")
    direct = transpose_times(self_cols, logit_grad)
    back_mean = transpose_times(neigh_cols, logit_grad).astype(jnp.bfloat16)
    degree = neighbours.shape[0]
    hub_count = lax.axis_size("dom") * hub_rows.shape[0]
    band = send_rows.shape[1]
    span = rows + hub_count + send_rows.shape[0] * band
    back_rows = back_mean.T.astype(jnp.float32)
    spread = scatter_mean(back_rows, neighbours, span)
    grad_rows = direct.T + spread[:rows]
    hub_back = lax.psum_scatter(
        spread[rows : rows + hub_count], "dom", scatter_dimension=0, tiled=True
    )
    grad_rows = grad_rows.at[hub_rows].add(hub_back)
    base = rows + hub_count
    for bit_index in range(send_rows.shape[0]):
        outgoing = spread[base + bit_index * band : base + (bit_index + 1) * band].astype(
            jnp.bfloat16
        )
        returned = trade(outgoing, bit_index)
        grad_rows = grad_rows.at[send_rows[bit_index]].add(returned.astype(jnp.float32))
    grad_hidden = grad_rows.T
    grad_pre = jnp.where(hidden > 0, grad_hidden, 0.0).astype(jnp.bfloat16)
    grad_inner_self = contract(grad_pre, full_input)
    grad_inner_neighbour = contract(grad_pre, full_mean)
    inner_both = tree_sum(jnp.concatenate([grad_inner_self, grad_inner_neighbour], axis=0), "dom")
    classes = outer_self.shape[0]
    return (inner_both[:width], inner_both[width:], outer_both[:classes], outer_both[classes:])


def solution(mesh):
    return jax.shard_map(
        body,
        mesh=mesh,
        in_specs=(
            P("feat", "dom"),
            P(None, "dom"),
            P("dom"),
            P("dom", None),
            P("dom"),
            P("feat", None),
            P("feat", None),
            P(),
            P(),
        ),
        out_specs=(P("feat", None), P("feat", None), P(None, "feat"), P(None, "feat")),
        check_vma=False,
    )
```

```python
import jax
import jax.numpy as jnp
from jax import lax
from jax.sharding import PartitionSpec as P

from jax.experimental import pallas as pl
from jax.experimental.pallas import tpu as pltpu

loss_scale = 4096.0


def gather_mean(table, neighbours, block=512):
    size, width = table.shape
    degree, nodes = neighbours.shape

    def kernel(nb_ref, tab_ref, out_ref):
        base = pl.program_id(0) * block

        def group(g, carry):
            picked = []
            for r in range(8):
                n = base + g * 8 + r
                acc = tab_ref[pl.ds(nb_ref[0, n], 1), :]
                for k in range(1, degree):
                    acc = acc + tab_ref[pl.ds(nb_ref[k, n], 1), :]
                picked.append(acc)
            start = pl.multiple_of(g * 8, 8)
            out_ref[pl.ds(start, 8), :] = jnp.concatenate(picked, axis=0) / degree
            return carry

        lax.fori_loop(0, block // 8, group, 0, unroll=2)

    return pl.pallas_call(
        kernel,
        grid_spec=pltpu.PrefetchScalarGridSpec(
            num_scalar_prefetch=1,
            grid=(nodes // block,),
            in_specs=[pl.BlockSpec((size, width), lambda j, nb: (0, 0))],
            out_specs=pl.BlockSpec((block, width), lambda j, nb: (j, 0)),
        ),
        out_shape=jax.ShapeDtypeStruct((nodes, width), jnp.float32),
    )(neighbours, table)


def scatter_mean(rows, neighbours, size):
    nodes, width = rows.shape
    degree = neighbours.shape[0]
    half = degree // 2

    def kernel(nb_ref, rows_ref, first_ref, second_ref):
        first_ref[...] = jnp.zeros_like(first_ref)
        second_ref[...] = jnp.zeros_like(second_ref)

        def step(n, carry):
            x = rows_ref[pl.ds(n, 1), :]
            for k in range(half):
                s = nb_ref[k, n]
                t = nb_ref[k + half, n]
                first_ref[pl.ds(s, 1), :] = first_ref[pl.ds(s, 1), :] + x
                second_ref[pl.ds(t, 1), :] = second_ref[pl.ds(t, 1), :] + x
            return carry

        lax.fori_loop(0, nodes, step, 0, unroll=4)

    first, second = pl.pallas_call(
        kernel,
        in_specs=[
            pl.BlockSpec(memory_space=pltpu.SMEM),
            pl.BlockSpec(memory_space=pltpu.VMEM),
        ],
        out_specs=(
            pl.BlockSpec(memory_space=pltpu.VMEM),
            pl.BlockSpec(memory_space=pltpu.VMEM),
        ),
        out_shape=(
            jax.ShapeDtypeStruct((size, width), jnp.float32),
            jax.ShapeDtypeStruct((size, width), jnp.float32),
        ),
    )(neighbours, rows)
    return (first + second) * (1.0 / degree)


def tree_sum(value, axis):
    count = lax.axis_size(axis)
    stride = 1
    while stride < count:
        pairs = [(source, source ^ stride) for source in range(count)]
        value = value + lax.ppermute(value, axis, pairs)
        stride *= 2
    return value


def tree_scatter(value, axis):
    count = lax.axis_size(axis)
    index = lax.axis_index(axis)
    width = value.shape[1]
    parts = value.reshape(count, -1, width)
    rows = parts.shape[1]
    stride = 1
    while stride < count:
        bit = (index // stride) % 2
        paired = parts.reshape(parts.shape[0] // 2, 2, rows, width)
        keep = lax.dynamic_index_in_dim(paired, bit, axis=1, keepdims=False)
        send = lax.dynamic_index_in_dim(paired, 1 - bit, axis=1, keepdims=False)
        pairs = [(source, source ^ stride) for source in range(count)]
        parts = keep + lax.ppermute(send, axis, pairs)
        stride *= 2
    return parts.reshape(rows, width)


def partner(value, axis, stride):
    mask = 2**stride
    pairs = [(source, source ^ mask) for source in range(lax.axis_size(axis))]
    return lax.ppermute(value, axis, pairs)


def trade(piece, bit_index):
    return partner(piece, "dom", bit_index)


def widen(first_rows, second_rows):
    return (
        lax.all_gather(first_rows, "feat", axis=0, tiled=True),
        lax.all_gather(second_rows, "feat", axis=0, tiled=True),
    )


def average(table_rows, neighbours):
    summed = gather_mean(table_rows.astype(jnp.float32), neighbours)
    return summed.T.astype(jnp.bfloat16)


def source_table(local, hub_rows, send_rows):
    local_rows = local.T
    hub_local = jnp.take(local_rows, hub_rows, axis=0)
    hub_all = lax.all_gather(hub_local, "dom", axis=0, tiled=True)
    received = [
        trade(jnp.take(local_rows, send_rows[bit_index], axis=0), bit_index)
        for bit_index in range(send_rows.shape[0])
    ]
    return jnp.concatenate([local_rows, hub_all] + received, axis=0)


def contract(left, right):
    return lax.dot_general(
        left, right, (((1,), (1,)), ((), ())), preferred_element_type=jnp.float32
    )


def transpose_times(left, right):
    return lax.dot_general(
        left, right, (((0,), (0,)), ((), ())), preferred_element_type=jnp.float32
    )


def class_gradient(logits, labels, nodes_all):
    expd = jnp.exp(logits)
    probs = expd / jnp.sum(expd, axis=0, keepdims=True)
    classes = lax.broadcasted_iota(jnp.int32, logits.shape, 0)
    onehot = (classes == labels[None, :]).astype(jnp.float32)
    return ((probs - onehot) * (loss_scale / nodes_all)).astype(jnp.bfloat16)


def body(
    features,
    neighbours,
    hub_rows,
    send_rows,
    labels,
    inner_self,
    inner_neighbour,
    outer_self,
    outer_neighbour,
):
    rows = features.shape[1]
    nodes_all = rows * lax.axis_size("dom")
    mean_one = average(source_table(features, hub_rows, send_rows), neighbours)
    full_input, full_mean = widen(features, mean_one)
    pre_act = jnp.dot(inner_self, full_input, preferred_element_type=jnp.float32)
    pre_act = pre_act + jnp.dot(inner_neighbour, full_mean, preferred_element_type=jnp.float32)
    hidden = jnp.maximum(pre_act, 0.0).astype(jnp.bfloat16)
    mean_two = average(source_table(hidden, hub_rows, send_rows), neighbours)
    width = hidden.shape[0]
    offset = lax.axis_index("feat") * width
    self_cols = lax.dynamic_slice_in_dim(outer_self, offset, width, 1)
    neigh_cols = lax.dynamic_slice_in_dim(outer_neighbour, offset, width, 1)
    full_hidden, full_two = widen(hidden, mean_two)
    logits = jnp.dot(outer_self, full_hidden, preferred_element_type=jnp.float32)
    logits = logits + jnp.dot(outer_neighbour, full_two, preferred_element_type=jnp.float32)
    logit_grad = class_gradient(logits, labels, nodes_all)
    grad_outer_self = contract(logit_grad, hidden)
    grad_outer_neighbour = contract(logit_grad, mean_two)
    outer_both = tree_sum(jnp.concatenate([grad_outer_self, grad_outer_neighbour], axis=0), "dom")
    direct = transpose_times(self_cols, logit_grad)
    back_mean = transpose_times(neigh_cols, logit_grad).astype(jnp.bfloat16)
    degree = neighbours.shape[0]
    hub_count = lax.axis_size("dom") * hub_rows.shape[0]
    band = send_rows.shape[1]
    span = rows + hub_count + send_rows.shape[0] * band
    back_rows = back_mean.T.astype(jnp.float32)
    spread = scatter_mean(back_rows, neighbours, span)
    grad_rows = direct.T + spread[:rows]
    hub_back = tree_scatter(spread[rows : rows + hub_count], "dom")
    grad_rows = grad_rows.at[hub_rows].add(hub_back)
    base = rows + hub_count
    for bit_index in range(send_rows.shape[0]):
        outgoing = spread[base + bit_index * band : base + (bit_index + 1) * band].astype(
            jnp.bfloat16
        )
        returned = trade(outgoing, bit_index)
        grad_rows = grad_rows.at[send_rows[bit_index]].add(returned.astype(jnp.float32))
    grad_hidden = grad_rows.T
    grad_pre = jnp.where(hidden > 0, grad_hidden, 0.0).astype(jnp.bfloat16)
    grad_inner_self = contract(grad_pre, full_input)
    grad_inner_neighbour = contract(grad_pre, full_mean)
    inner_both = tree_sum(jnp.concatenate([grad_inner_self, grad_inner_neighbour], axis=0), "dom")
    classes = outer_self.shape[0]
    return (inner_both[:width], inner_both[width:], outer_both[:classes], outer_both[classes:])


def solution(mesh):
    return jax.shard_map(
        body,
        mesh=mesh,
        in_specs=(
            P("feat", "dom"),
            P(None, "dom"),
            P("dom"),
            P("dom", None),
            P("dom"),
            P("feat", None),
            P("feat", None),
            P(),
            P(),
        ),
        out_specs=(P("feat", None), P("feat", None), P(None, "feat"), P(None, "feat")),
        check_vma=False,
    )
```

```python
import jax
import jax.numpy as jnp
from jax import lax
from jax.sharding import PartitionSpec as P

from jax.experimental import pallas as pl
from jax.experimental.pallas import tpu as pltpu

loss_scale = 4096.0


def gather_mean(table, neighbours, block=512):
    size, width = table.shape
    degree, nodes = neighbours.shape

    def kernel(nb_ref, tab_ref, out_ref):
        base = pl.program_id(0) * block

        def group(g, carry):
            picked = []
            for r in range(8):
                n = base + g * 8 + r
                acc = tab_ref[pl.ds(nb_ref[0, n], 1), :]
                for k in range(1, degree):
                    acc = acc + tab_ref[pl.ds(nb_ref[k, n], 1), :]
                picked.append(acc)
            start = pl.multiple_of(g * 8, 8)
            out_ref[pl.ds(start, 8), :] = jnp.concatenate(picked, axis=0) / degree
            return carry

        lax.fori_loop(0, block // 8, group, 0)

    return pl.pallas_call(
        kernel,
        grid_spec=pltpu.PrefetchScalarGridSpec(
            num_scalar_prefetch=1,
            grid=(nodes // block,),
            in_specs=[pl.BlockSpec((size, width), lambda j, nb: (0, 0))],
            out_specs=pl.BlockSpec((block, width), lambda j, nb: (j, 0)),
        ),
        out_shape=jax.ShapeDtypeStruct((nodes, width), jnp.float32),
    )(neighbours, table)


def scatter_mean(rows, neighbours, size):
    nodes, width = rows.shape
    degree = neighbours.shape[0]
    half = degree // 2

    def kernel(nb_ref, rows_ref, first_ref, second_ref):
        first_ref[...] = jnp.zeros_like(first_ref)
        second_ref[...] = jnp.zeros_like(second_ref)

        def step(n, carry):
            x = rows_ref[pl.ds(n, 1), :]
            for k in range(half):
                s = nb_ref[k, n]
                t = nb_ref[k + half, n]
                first_ref[pl.ds(s, 1), :] = first_ref[pl.ds(s, 1), :] + x
                second_ref[pl.ds(t, 1), :] = second_ref[pl.ds(t, 1), :] + x
            return carry

        lax.fori_loop(0, nodes, step, 0, unroll=4)
        first_ref[...] = (first_ref[...] + second_ref[...]) * (1.0 / degree)

    return pl.pallas_call(
        kernel,
        in_specs=[
            pl.BlockSpec(memory_space=pltpu.SMEM),
            pl.BlockSpec(memory_space=pltpu.VMEM),
        ],
        out_specs=pl.BlockSpec(memory_space=pltpu.VMEM),
        out_shape=jax.ShapeDtypeStruct((size, width), jnp.float32),
        scratch_shapes=[pltpu.VMEM((size, width), jnp.float32)],
    )(neighbours, rows)


def tree_sum(value, axis):
    count = lax.axis_size(axis)
    stride = 1
    while stride < count:
        pairs = [(source, source ^ stride) for source in range(count)]
        value = value + lax.ppermute(value, axis, pairs)
        stride *= 2
    return value


def tree_scatter(value, axis):
    count = lax.axis_size(axis)
    index = lax.axis_index(axis)
    width = value.shape[1]
    parts = value.reshape(count, -1, width)
    rows = parts.shape[1]
    stride = 1
    while stride < count:
        bit = (index // stride) % 2
        paired = parts.reshape(parts.shape[0] // 2, 2, rows, width)
        keep = lax.dynamic_index_in_dim(paired, bit, axis=1, keepdims=False)
        send = lax.dynamic_index_in_dim(paired, 1 - bit, axis=1, keepdims=False)
        pairs = [(source, source ^ stride) for source in range(count)]
        parts = keep + lax.ppermute(send, axis, pairs)
        stride *= 2
    return parts.reshape(rows, width)


def partner(value, axis, stride):
    mask = 2**stride
    pairs = [(source, source ^ mask) for source in range(lax.axis_size(axis))]
    return lax.ppermute(value, axis, pairs)


def trade(piece, bit_index):
    return partner(piece, "dom", bit_index)


def widen(first_rows, second_rows):
    return (
        lax.all_gather(first_rows, "feat", axis=0, tiled=True),
        lax.all_gather(second_rows, "feat", axis=0, tiled=True),
    )


def average(table_rows, neighbours):
    summed = gather_mean(table_rows.astype(jnp.float32), neighbours)
    return summed.T.astype(jnp.bfloat16)


def source_table(local, hub_rows, send_rows):
    local_rows = local.T
    hub_local = jnp.take(local_rows, hub_rows, axis=0)
    hub_all = lax.all_gather(hub_local, "dom", axis=0, tiled=True)
    received = [
        trade(jnp.take(local_rows, send_rows[bit_index], axis=0), bit_index)
        for bit_index in range(send_rows.shape[0])
    ]
    return jnp.concatenate([local_rows, hub_all] + received, axis=0)


def contract(left, right):
    return lax.dot_general(
        left, right, (((1,), (1,)), ((), ())), preferred_element_type=jnp.float32
    )


def transpose_times(left, right):
    return lax.dot_general(
        left, right, (((0,), (0,)), ((), ())), preferred_element_type=jnp.float32
    )


def class_gradient(logits, labels, nodes_all):
    expd = jnp.exp(logits)
    probs = expd / jnp.sum(expd, axis=0, keepdims=True)
    classes = lax.broadcasted_iota(jnp.int32, logits.shape, 0)
    onehot = (classes == labels[None, :]).astype(jnp.float32)
    return ((probs - onehot) * (loss_scale / nodes_all)).astype(jnp.bfloat16)


def body(
    features,
    neighbours,
    hub_rows,
    send_rows,
    labels,
    inner_self,
    inner_neighbour,
    outer_self,
    outer_neighbour,
):
    rows = features.shape[1]
    nodes_all = rows * lax.axis_size("dom")
    mean_one = average(source_table(features, hub_rows, send_rows), neighbours)
    full_input, full_mean = widen(features, mean_one)
    pre_act = jnp.dot(inner_self, full_input, preferred_element_type=jnp.float32)
    pre_act = pre_act + jnp.dot(inner_neighbour, full_mean, preferred_element_type=jnp.float32)
    hidden = jnp.maximum(pre_act, 0.0).astype(jnp.bfloat16)
    mean_two = average(source_table(hidden, hub_rows, send_rows), neighbours)
    width = hidden.shape[0]
    offset = lax.axis_index("feat") * width
    self_cols = lax.dynamic_slice_in_dim(outer_self, offset, width, 1)
    neigh_cols = lax.dynamic_slice_in_dim(outer_neighbour, offset, width, 1)
    full_hidden, full_two = widen(hidden, mean_two)
    logits = jnp.dot(outer_self, full_hidden, preferred_element_type=jnp.float32)
    logits = logits + jnp.dot(outer_neighbour, full_two, preferred_element_type=jnp.float32)
    logit_grad = class_gradient(logits, labels, nodes_all)
    grad_outer_self = contract(logit_grad, hidden)
    grad_outer_neighbour = contract(logit_grad, mean_two)
    outer_both = tree_sum(jnp.concatenate([grad_outer_self, grad_outer_neighbour], axis=0), "dom")
    direct = transpose_times(self_cols, logit_grad)
    back_mean = transpose_times(neigh_cols, logit_grad).astype(jnp.bfloat16)
    degree = neighbours.shape[0]
    hub_count = lax.axis_size("dom") * hub_rows.shape[0]
    band = send_rows.shape[1]
    span = rows + hub_count + send_rows.shape[0] * band
    back_rows = back_mean.T.astype(jnp.float32)
    spread = scatter_mean(back_rows, neighbours, span)
    grad_rows = direct.T + spread[:rows]
    owners = lax.axis_size("dom")
    hub_parts = spread[rows : rows + hub_count].reshape(owners, hub_count // owners, width)
    hub_back = jnp.sum(
        lax.all_to_all(hub_parts, "dom", split_axis=0, concat_axis=0, tiled=True), axis=0
    )
    grad_rows = grad_rows.at[hub_rows].add(hub_back)
    base = rows + hub_count
    for bit_index in range(send_rows.shape[0]):
        outgoing = spread[base + bit_index * band : base + (bit_index + 1) * band].astype(
            jnp.bfloat16
        )
        returned = trade(outgoing, bit_index)
        grad_rows = grad_rows.at[send_rows[bit_index]].add(returned.astype(jnp.float32))
    grad_hidden = grad_rows.T
    grad_pre = jnp.where(hidden > 0, grad_hidden, 0.0).astype(jnp.bfloat16)
    grad_inner_self = contract(grad_pre, full_input)
    grad_inner_neighbour = contract(grad_pre, full_mean)
    inner_both = tree_sum(jnp.concatenate([grad_inner_self, grad_inner_neighbour], axis=0), "dom")
    classes = outer_self.shape[0]
    return (inner_both[:width], inner_both[width:], outer_both[:classes], outer_both[classes:])


def solution(mesh):
    return jax.shard_map(
        body,
        mesh=mesh,
        in_specs=(
            P("feat", "dom"),
            P(None, "dom"),
            P("dom"),
            P("dom", None),
            P("dom"),
            P("feat", None),
            P("feat", None),
            P(),
            P(),
        ),
        out_specs=(P("feat", None), P("feat", None), P(None, "feat"), P(None, "feat")),
        check_vma=False,
    )
```

```python
import jax
import jax.numpy as jnp
from jax import lax
from jax.sharding import PartitionSpec as P

from jax.experimental import pallas as pl
from jax.experimental.pallas import tpu as pltpu

loss_scale = 4096.0


def gather_mean(table, neighbours, block=512):
    size, width = table.shape
    degree, nodes = neighbours.shape

    def kernel(nb_ref, tab_ref, out_ref):
        base = pl.program_id(0) * block

        def group(g, carry):
            picked = []
            for r in range(8):
                n = base + g * 8 + r
                acc = tab_ref[pl.ds(nb_ref[0, n], 1), :]
                for k in range(1, degree):
                    acc = acc + tab_ref[pl.ds(nb_ref[k, n], 1), :]
                picked.append(acc)
            start = pl.multiple_of(g * 8, 8)
            out_ref[pl.ds(start, 8), :] = jnp.concatenate(picked, axis=0) / degree
            return carry

        lax.fori_loop(0, block // 8, group, 0)

    return pl.pallas_call(
        kernel,
        grid_spec=pltpu.PrefetchScalarGridSpec(
            num_scalar_prefetch=1,
            grid=(nodes // block,),
            in_specs=[pl.BlockSpec((size, width), lambda j, nb: (0, 0))],
            out_specs=pl.BlockSpec((block, width), lambda j, nb: (j, 0)),
        ),
        out_shape=jax.ShapeDtypeStruct((nodes, width), jnp.float32),
    )(neighbours, table)


def scatter_mean(rows, neighbours, size):
    nodes, width = rows.shape
    degree = neighbours.shape[0]
    half = degree // 2

    def kernel(nb_ref, rows_ref, first_ref, second_ref):
        first_ref[...] = jnp.zeros_like(first_ref)
        second_ref[...] = jnp.zeros_like(second_ref)

        def step(n, carry):
            x = rows_ref[pl.ds(n, 1), :]
            for k in range(half):
                s = nb_ref[k, n]
                t = nb_ref[k + half, n]
                first_ref[pl.ds(s, 1), :] = first_ref[pl.ds(s, 1), :] + x
                second_ref[pl.ds(t, 1), :] = second_ref[pl.ds(t, 1), :] + x
            return carry

        lax.fori_loop(0, nodes, step, 0, unroll=4)
        first_ref[...] = (first_ref[...] + second_ref[...]) * (1.0 / degree)

    return pl.pallas_call(
        kernel,
        in_specs=[
            pl.BlockSpec(memory_space=pltpu.SMEM),
            pl.BlockSpec(memory_space=pltpu.VMEM),
        ],
        out_specs=pl.BlockSpec(memory_space=pltpu.VMEM),
        out_shape=jax.ShapeDtypeStruct((size, width), jnp.float32),
        scratch_shapes=[pltpu.VMEM((size, width), jnp.float32)],
    )(neighbours, rows)


def tree_sum(value, axis):
    count = lax.axis_size(axis)
    stride = 1
    while stride < count:
        pairs = [(source, source ^ stride) for source in range(count)]
        value = value + lax.ppermute(value, axis, pairs)
        stride *= 2
    return value


def tree_scatter(value, axis):
    count = lax.axis_size(axis)
    index = lax.axis_index(axis)
    width = value.shape[1]
    parts = value.reshape(count, -1, width)
    rows = parts.shape[1]
    stride = 1
    while stride < count:
        bit = (index // stride) % 2
        paired = parts.reshape(parts.shape[0] // 2, 2, rows, width)
        keep = lax.dynamic_index_in_dim(paired, bit, axis=1, keepdims=False)
        send = lax.dynamic_index_in_dim(paired, 1 - bit, axis=1, keepdims=False)
        pairs = [(source, source ^ stride) for source in range(count)]
        parts = keep + lax.ppermute(send, axis, pairs)
        stride *= 2
    return parts.reshape(rows, width)


def partner(value, axis, stride):
    mask = 2**stride
    pairs = [(source, source ^ mask) for source in range(lax.axis_size(axis))]
    return lax.ppermute(value, axis, pairs)


def trade(piece, bit_index):
    return partner(piece, "dom", bit_index)


def widen(first_rows, second_rows):
    return (
        lax.all_gather(first_rows, "feat", axis=0, tiled=True),
        lax.all_gather(second_rows, "feat", axis=0, tiled=True),
    )


def average(table_rows, neighbours):
    summed = gather_mean(table_rows.astype(jnp.float32), neighbours)
    return summed.T.astype(jnp.bfloat16)


def source_table(local, hub_rows, send_rows):
    local_rows = local.T
    hub_local = jnp.take(local_rows, hub_rows, axis=0)
    hub_all = lax.all_gather(hub_local, "dom", axis=0, tiled=True)
    received = [
        trade(jnp.take(local_rows, send_rows[bit_index], axis=0), bit_index)
        for bit_index in range(send_rows.shape[0])
    ]
    return jnp.concatenate([local_rows, hub_all] + received, axis=0)


def contract(left, right):
    return lax.dot_general(
        left, right, (((1,), (1,)), ((), ())), preferred_element_type=jnp.float32
    )


def transpose_times(left, right):
    return lax.dot_general(
        left, right, (((0,), (0,)), ((), ())), preferred_element_type=jnp.float32
    )


def class_gradient(logits, labels, nodes_all):
    expd = jnp.exp(logits)
    probs = expd / jnp.sum(expd, axis=0, keepdims=True)
    classes = lax.broadcasted_iota(jnp.int32, logits.shape, 0)
    onehot = (classes == labels[None, :]).astype(jnp.float32)
    return ((probs - onehot) * (loss_scale / nodes_all)).astype(jnp.bfloat16)


def body(
    features,
    neighbours,
    hub_rows,
    send_rows,
    labels,
    inner_self,
    inner_neighbour,
    outer_self,
    outer_neighbour,
):
    rows = features.shape[1]
    nodes_all = rows * lax.axis_size("dom")
    mean_one = average(source_table(features, hub_rows, send_rows), neighbours)
    full_input, full_mean = widen(features, mean_one)
    pre_act = jnp.dot(inner_self, full_input, preferred_element_type=jnp.float32)
    pre_act = pre_act + jnp.dot(inner_neighbour, full_mean, preferred_element_type=jnp.float32)
    hidden = jnp.maximum(pre_act, 0.0).astype(jnp.bfloat16)
    mean_two = average(source_table(hidden, hub_rows, send_rows), neighbours)
    width = hidden.shape[0]
    offset = lax.axis_index("feat") * width
    self_cols = lax.dynamic_slice_in_dim(outer_self, offset, width, 1)
    neigh_cols = lax.dynamic_slice_in_dim(outer_neighbour, offset, width, 1)
    full_hidden, full_two = widen(hidden, mean_two)
    logits = jnp.dot(outer_self, full_hidden, preferred_element_type=jnp.float32)
    logits = logits + jnp.dot(outer_neighbour, full_two, preferred_element_type=jnp.float32)
    logit_grad = class_gradient(logits, labels, nodes_all)
    grad_outer_self = contract(logit_grad, hidden)
    grad_outer_neighbour = contract(logit_grad, mean_two)
    direct = transpose_times(self_cols, logit_grad)
    back_mean = transpose_times(neigh_cols, logit_grad).astype(jnp.bfloat16)
    degree = neighbours.shape[0]
    hub_count = lax.axis_size("dom") * hub_rows.shape[0]
    band = send_rows.shape[1]
    span = rows + hub_count + send_rows.shape[0] * band
    back_rows = back_mean.T.astype(jnp.float32)
    spread = scatter_mean(back_rows, neighbours, span)
    grad_rows = direct.T + spread[:rows]
    owners = lax.axis_size("dom")
    hub_parts = spread[rows : rows + hub_count].reshape(owners, hub_count // owners, width)
    hub_back = jnp.sum(
        lax.all_to_all(
            hub_parts.astype(jnp.bfloat16), "dom", split_axis=0, concat_axis=0, tiled=True
        ).astype(jnp.float32),
        axis=0,
    )
    base = rows + hub_count
    landed = [hub_back]
    for bit_index in range(send_rows.shape[0]):
        outgoing = spread[base + bit_index * band : base + (bit_index + 1) * band].astype(
            jnp.bfloat16
        )
        landed.append(trade(outgoing, bit_index).astype(jnp.float32))
    targets = jnp.concatenate([hub_rows, send_rows.reshape(-1)])
    grad_rows = grad_rows.at[targets].add(jnp.concatenate(landed, axis=0))
    grad_hidden = grad_rows.T
    grad_pre = jnp.where(hidden > 0, grad_hidden, 0.0).astype(jnp.bfloat16)
    grad_inner_self = contract(grad_pre, full_input)
    grad_inner_neighbour = contract(grad_pre, full_mean)
    pieces = (grad_inner_self, grad_inner_neighbour, grad_outer_self, grad_outer_neighbour)
    summed = tree_sum(jnp.concatenate([piece.reshape(-1) for piece in pieces]), "dom")
    results = []
    offset = 0
    for piece in pieces:
        results.append(summed[offset : offset + piece.size].reshape(piece.shape))
        offset += piece.size
    return tuple(results)


def solution(mesh):
    return jax.shard_map(
        body,
        mesh=mesh,
        in_specs=(
            P("feat", "dom"),
            P(None, "dom"),
            P("dom"),
            P("dom", None),
            P("dom"),
            P("feat", None),
            P("feat", None),
            P(),
            P(),
        ),
        out_specs=(P("feat", None), P("feat", None), P(None, "feat"), P(None, "feat")),
        check_vma=False,
    )
```

```python
import jax
import jax.numpy as jnp
from jax import lax
from jax.sharding import PartitionSpec as P

from jax.experimental import pallas as pl
from jax.experimental.pallas import tpu as pltpu

loss_scale = 4096.0


def gather_mean(table, neighbours, block=512):
    size, width = table.shape
    degree, nodes = neighbours.shape

    def kernel(nb_ref, tab_ref, out_ref):
        base = pl.program_id(0) * block

        def group(g, carry):
            picked = []
            for r in range(8):
                n = base + g * 8 + r
                acc = tab_ref[pl.ds(nb_ref[0, n], 1), :]
                for k in range(1, degree):
                    acc = acc + tab_ref[pl.ds(nb_ref[k, n], 1), :]
                picked.append(acc)
            start = pl.multiple_of(g * 8, 8)
            out_ref[pl.ds(start, 8), :] = jnp.concatenate(picked, axis=0) / degree
            return carry

        lax.fori_loop(0, block // 8, group, 0)

    return pl.pallas_call(
        kernel,
        grid_spec=pltpu.PrefetchScalarGridSpec(
            num_scalar_prefetch=1,
            grid=(nodes // block,),
            in_specs=[pl.BlockSpec((size, width), lambda j, nb: (0, 0))],
            out_specs=pl.BlockSpec((block, width), lambda j, nb: (j, 0)),
        ),
        out_shape=jax.ShapeDtypeStruct((nodes, width), jnp.float32),
    )(neighbours, table)


def scatter_mean(rows, neighbours, size):
    nodes, width = rows.shape
    degree = neighbours.shape[0]
    half = degree // 2

    def kernel(nb_ref, rows_ref, first_ref, second_ref):
        first_ref[...] = jnp.zeros_like(first_ref)
        second_ref[...] = jnp.zeros_like(second_ref)

        def step(n, carry):
            x = rows_ref[pl.ds(n, 1), :]
            for k in range(half):
                s = nb_ref[k, n]
                t = nb_ref[k + half, n]
                first_ref[pl.ds(s, 1), :] = first_ref[pl.ds(s, 1), :] + x
                second_ref[pl.ds(t, 1), :] = second_ref[pl.ds(t, 1), :] + x
            return carry

        lax.fori_loop(0, nodes, step, 0, unroll=4)
        first_ref[...] = (first_ref[...] + second_ref[...]) * (1.0 / degree)

    return pl.pallas_call(
        kernel,
        in_specs=[
            pl.BlockSpec(memory_space=pltpu.SMEM),
            pl.BlockSpec(memory_space=pltpu.VMEM),
        ],
        out_specs=pl.BlockSpec(memory_space=pltpu.VMEM),
        out_shape=jax.ShapeDtypeStruct((size, width), jnp.float32),
        scratch_shapes=[pltpu.VMEM((size, width), jnp.float32)],
    )(neighbours, rows)


def land_rows(base, targets, updates):
    count, width = updates.shape
    half = count // 2

    def kernel(t_ref, base_ref, upd_ref, out_ref, extra_ref):
        out_ref[...] = base_ref[...]
        extra_ref[...] = jnp.zeros_like(extra_ref)

        def step(i, carry):
            s = t_ref[i]
            t = t_ref[i + half]
            out_ref[pl.ds(s, 1), :] = out_ref[pl.ds(s, 1), :] + upd_ref[pl.ds(i, 1), :]
            extra_ref[pl.ds(t, 1), :] = extra_ref[pl.ds(t, 1), :] + upd_ref[pl.ds(i + half, 1), :]
            return carry

        lax.fori_loop(0, half, step, 0, unroll=4)
        for i in range(2 * half, count):
            s = t_ref[i]
            out_ref[pl.ds(s, 1), :] = out_ref[pl.ds(s, 1), :] + upd_ref[pl.ds(i, 1), :]
        out_ref[...] = out_ref[...] + extra_ref[...]

    return pl.pallas_call(
        kernel,
        in_specs=[
            pl.BlockSpec(memory_space=pltpu.SMEM),
            pl.BlockSpec(memory_space=pltpu.VMEM),
            pl.BlockSpec(memory_space=pltpu.VMEM),
        ],
        out_specs=pl.BlockSpec(memory_space=pltpu.VMEM),
        out_shape=jax.ShapeDtypeStruct(base.shape, jnp.float32),
        scratch_shapes=[pltpu.VMEM(base.shape, jnp.float32)],
    )(targets, base, updates)


def tree_gather(value, axis):
    count = lax.axis_size(axis)
    index = lax.axis_index(axis)
    block = value
    stride = 1
    while stride < count:
        pairs = [(source, source ^ stride) for source in range(count)]
        other = lax.ppermute(block, axis, pairs)
        low = (index // stride) % 2 == 0
        block = jnp.where(
            low, jnp.concatenate([block, other], axis=0), jnp.concatenate([other, block], axis=0)
        )
        stride *= 2
    return block


def tree_sum(value, axis):
    count = lax.axis_size(axis)
    stride = 1
    while stride < count:
        pairs = [(source, source ^ stride) for source in range(count)]
        value = value + lax.ppermute(value, axis, pairs)
        stride *= 2
    return value


def tree_scatter(value, axis):
    count = lax.axis_size(axis)
    index = lax.axis_index(axis)
    width = value.shape[1]
    parts = value.reshape(count, -1, width)
    rows = parts.shape[1]
    stride = 1
    while stride < count:
        bit = (index // stride) % 2
        paired = parts.reshape(parts.shape[0] // 2, 2, rows, width)
        keep = lax.dynamic_index_in_dim(paired, bit, axis=1, keepdims=False)
        send = lax.dynamic_index_in_dim(paired, 1 - bit, axis=1, keepdims=False)
        pairs = [(source, source ^ stride) for source in range(count)]
        parts = keep + lax.ppermute(send, axis, pairs)
        stride *= 2
    return parts.reshape(rows, width)


def partner(value, axis, stride):
    mask = 2**stride
    pairs = [(source, source ^ mask) for source in range(lax.axis_size(axis))]
    return lax.ppermute(value, axis, pairs)


def trade(piece, bit_index):
    return partner(piece, "dom", bit_index)


def widen(first_rows, second_rows):
    return (
        lax.all_gather(first_rows, "feat", axis=0, tiled=True),
        lax.all_gather(second_rows, "feat", axis=0, tiled=True),
    )


def average(table_rows, neighbours):
    summed = gather_mean(table_rows.astype(jnp.float32), neighbours)
    return summed.T.astype(jnp.bfloat16)


def source_table(local, hub_rows, send_rows):
    local_rows = local.T
    hub_local = jnp.take(local_rows, hub_rows, axis=0)
    hub_all = tree_gather(hub_local, "dom")
    received = [
        trade(jnp.take(local_rows, send_rows[bit_index], axis=0), bit_index)
        for bit_index in range(send_rows.shape[0])
    ]
    return jnp.concatenate([local_rows, hub_all] + received, axis=0)


def contract(left, right):
    return lax.dot_general(
        left, right, (((1,), (1,)), ((), ())), preferred_element_type=jnp.float32
    )


def transpose_times(left, right):
    return lax.dot_general(
        left, right, (((0,), (0,)), ((), ())), preferred_element_type=jnp.float32
    )


def class_gradient(logits, labels, nodes_all):
    expd = jnp.exp(logits)
    probs = expd / jnp.sum(expd, axis=0, keepdims=True)
    classes = lax.broadcasted_iota(jnp.int32, logits.shape, 0)
    onehot = (classes == labels[None, :]).astype(jnp.float32)
    return ((probs - onehot) * (loss_scale / nodes_all)).astype(jnp.bfloat16)


def body(
    features,
    neighbours,
    hub_rows,
    send_rows,
    labels,
    inner_self,
    inner_neighbour,
    outer_self,
    outer_neighbour,
):
    rows = features.shape[1]
    nodes_all = rows * lax.axis_size("dom")
    mean_one = average(source_table(features, hub_rows, send_rows), neighbours)
    full_input, full_mean = widen(features, mean_one)
    pre_act = jnp.dot(inner_self, full_input, preferred_element_type=jnp.float32)
    pre_act = pre_act + jnp.dot(inner_neighbour, full_mean, preferred_element_type=jnp.float32)
    hidden = jnp.maximum(pre_act, 0.0).astype(jnp.bfloat16)
    mean_two = average(source_table(hidden, hub_rows, send_rows), neighbours)
    width = hidden.shape[0]
    offset = lax.axis_index("feat") * width
    self_cols = lax.dynamic_slice_in_dim(outer_self, offset, width, 1)
    neigh_cols = lax.dynamic_slice_in_dim(outer_neighbour, offset, width, 1)
    full_hidden, full_two = widen(hidden, mean_two)
    logits = jnp.dot(outer_self, full_hidden, preferred_element_type=jnp.float32)
    logits = logits + jnp.dot(outer_neighbour, full_two, preferred_element_type=jnp.float32)
    logit_grad = class_gradient(logits, labels, nodes_all)
    grad_outer_self = contract(logit_grad, hidden)
    grad_outer_neighbour = contract(logit_grad, mean_two)
    direct = transpose_times(self_cols, logit_grad)
    back_mean = transpose_times(neigh_cols, logit_grad).astype(jnp.bfloat16)
    degree = neighbours.shape[0]
    hub_count = lax.axis_size("dom") * hub_rows.shape[0]
    band = send_rows.shape[1]
    span = rows + hub_count + send_rows.shape[0] * band
    back_rows = back_mean.T.astype(jnp.float32)
    spread = scatter_mean(back_rows, neighbours, span)
    grad_rows = direct.T + spread[:rows]
    owners = lax.axis_size("dom")
    hub_parts = spread[rows : rows + hub_count].reshape(owners, hub_count // owners, width)
    hub_back = jnp.sum(
        lax.all_to_all(
            hub_parts.astype(jnp.bfloat16), "dom", split_axis=0, concat_axis=0, tiled=True
        ).astype(jnp.float32),
        axis=0,
    )
    base = rows + hub_count
    landed = [hub_back]
    for bit_index in range(send_rows.shape[0]):
        outgoing = spread[base + bit_index * band : base + (bit_index + 1) * band].astype(
            jnp.bfloat16
        )
        landed.append(trade(outgoing, bit_index).astype(jnp.float32))
    targets = jnp.concatenate([hub_rows, send_rows.reshape(-1)])
    grad_rows = land_rows(grad_rows, targets, jnp.concatenate(landed, axis=0))
    grad_hidden = grad_rows.T
    grad_pre = jnp.where(hidden > 0, grad_hidden, 0.0).astype(jnp.bfloat16)
    grad_inner_self = contract(grad_pre, full_input)
    grad_inner_neighbour = contract(grad_pre, full_mean)
    pieces = (grad_inner_self, grad_inner_neighbour, grad_outer_self, grad_outer_neighbour)
    summed = tree_sum(jnp.concatenate([piece.reshape(-1) for piece in pieces]), "dom")
    results = []
    offset = 0
    for piece in pieces:
        results.append(summed[offset : offset + piece.size].reshape(piece.shape))
        offset += piece.size
    return tuple(results)


def solution(mesh):
    return jax.shard_map(
        body,
        mesh=mesh,
        in_specs=(
            P("feat", "dom"),
            P(None, "dom"),
            P("dom"),
            P("dom", None),
            P("dom"),
            P("feat", None),
            P("feat", None),
            P(),
            P(),
        ),
        out_specs=(P("feat", None), P("feat", None), P(None, "feat"), P(None, "feat")),
        check_vma=False,
    )
```

```python
import jax
import jax.numpy as jnp
from jax import lax
from jax.sharding import PartitionSpec as P

from jax.experimental import pallas as pl
from jax.experimental.pallas import tpu as pltpu

loss_scale = 4096.0


def gather_mean(table, neighbours, after, block=512):
    size, width = table.shape
    degree, nodes = neighbours.shape

    def kernel(nb_ref, tab_ref, after_ref, out_ref):
        base = pl.program_id(0) * block

        def group(g, carry):
            picked = []
            for r in range(8):
                n = base + g * 8 + r
                acc = tab_ref[pl.ds(nb_ref[0, n], 1), :]
                for k in range(1, degree):
                    acc = acc + tab_ref[pl.ds(nb_ref[k, n], 1), :]
                picked.append(acc)
            start = pl.multiple_of(g * 8, 8)
            out_ref[pl.ds(start, 8), :] = jnp.concatenate(picked, axis=0) / degree
            return carry

        lax.fori_loop(0, block // 8, group, 0)

    return pl.pallas_call(
        kernel,
        grid_spec=pltpu.PrefetchScalarGridSpec(
            num_scalar_prefetch=1,
            grid=(nodes // block,),
            in_specs=[
                pl.BlockSpec((size, width), lambda j, nb: (0, 0)),
                pl.BlockSpec(memory_space=pl.ANY),
            ],
            out_specs=pl.BlockSpec((block, width), lambda j, nb: (j, 0)),
        ),
        out_shape=jax.ShapeDtypeStruct((nodes, width), jnp.float32),
    )(neighbours, table, after)


def scatter_mean(rows, neighbours, size):
    nodes, width = rows.shape
    degree = neighbours.shape[0]
    half = degree // 2

    def kernel(nb_ref, rows_ref, first_ref, second_ref):
        first_ref[...] = jnp.zeros_like(first_ref)
        second_ref[...] = jnp.zeros_like(second_ref)

        def step(n, carry):
            x = rows_ref[pl.ds(n, 1), :]
            for k in range(half):
                s = nb_ref[k, n]
                t = nb_ref[k + half, n]
                first_ref[pl.ds(s, 1), :] = first_ref[pl.ds(s, 1), :] + x
                second_ref[pl.ds(t, 1), :] = second_ref[pl.ds(t, 1), :] + x
            return carry

        lax.fori_loop(0, nodes, step, 0, unroll=4)
        first_ref[...] = (first_ref[...] + second_ref[...]) * (1.0 / degree)

    return pl.pallas_call(
        kernel,
        in_specs=[
            pl.BlockSpec(memory_space=pltpu.SMEM),
            pl.BlockSpec(memory_space=pltpu.VMEM),
        ],
        out_specs=pl.BlockSpec(memory_space=pltpu.VMEM),
        out_shape=jax.ShapeDtypeStruct((size, width), jnp.float32),
        scratch_shapes=[pltpu.VMEM((size, width), jnp.float32)],
    )(neighbours, rows)


def land_rows(base, targets, updates):
    count, width = updates.shape
    half = count // 2

    def kernel(t_ref, base_ref, upd_ref, out_ref, extra_ref):
        out_ref[...] = base_ref[...]
        extra_ref[...] = jnp.zeros_like(extra_ref)

        def step(i, carry):
            s = t_ref[i]
            t = t_ref[i + half]
            out_ref[pl.ds(s, 1), :] = out_ref[pl.ds(s, 1), :] + upd_ref[pl.ds(i, 1), :]
            extra_ref[pl.ds(t, 1), :] = extra_ref[pl.ds(t, 1), :] + upd_ref[pl.ds(i + half, 1), :]
            return carry

        lax.fori_loop(0, half, step, 0, unroll=4)
        for i in range(2 * half, count):
            s = t_ref[i]
            out_ref[pl.ds(s, 1), :] = out_ref[pl.ds(s, 1), :] + upd_ref[pl.ds(i, 1), :]
        out_ref[...] = out_ref[...] + extra_ref[...]

    return pl.pallas_call(
        kernel,
        in_specs=[
            pl.BlockSpec(memory_space=pltpu.SMEM),
            pl.BlockSpec(memory_space=pltpu.VMEM),
            pl.BlockSpec(memory_space=pltpu.VMEM),
        ],
        out_specs=pl.BlockSpec(memory_space=pltpu.VMEM),
        out_shape=jax.ShapeDtypeStruct(base.shape, jnp.float32),
        scratch_shapes=[pltpu.VMEM(base.shape, jnp.float32)],
    )(targets, base, updates)


def tree_gather(value, axis):
    count = lax.axis_size(axis)
    index = lax.axis_index(axis)
    block = value
    stride = 1
    while stride < count:
        pairs = [(source, source ^ stride) for source in range(count)]
        other = lax.ppermute(block, axis, pairs)
        low = (index // stride) % 2 == 0
        block = jnp.where(
            low, jnp.concatenate([block, other], axis=0), jnp.concatenate([other, block], axis=0)
        )
        stride *= 2
    return block


def tree_sum(value, axis):
    count = lax.axis_size(axis)
    stride = 1
    while stride < count:
        pairs = [(source, source ^ stride) for source in range(count)]
        value = value + lax.ppermute(value, axis, pairs)
        stride *= 2
    return value


def tree_scatter(value, axis):
    count = lax.axis_size(axis)
    index = lax.axis_index(axis)
    width = value.shape[1]
    parts = value.reshape(count, -1, width)
    rows = parts.shape[1]
    stride = 1
    while stride < count:
        bit = (index // stride) % 2
        paired = parts.reshape(parts.shape[0] // 2, 2, rows, width)
        keep = lax.dynamic_index_in_dim(paired, bit, axis=1, keepdims=False)
        send = lax.dynamic_index_in_dim(paired, 1 - bit, axis=1, keepdims=False)
        pairs = [(source, source ^ stride) for source in range(count)]
        parts = keep + lax.ppermute(send, axis, pairs)
        stride *= 2
    return parts.reshape(rows, width)


def partner(value, axis, stride):
    mask = 2**stride
    pairs = [(source, source ^ mask) for source in range(lax.axis_size(axis))]
    return lax.ppermute(value, axis, pairs)


def trade(piece, bit_index):
    return partner(piece, "dom", bit_index)


def widen(first_rows, second_rows):
    return (
        lax.all_gather(first_rows, "feat", axis=0, tiled=True),
        lax.all_gather(second_rows, "feat", axis=0, tiled=True),
    )


def average(table_rows, neighbours, after):
    summed = gather_mean(table_rows.astype(jnp.float32), neighbours, after)
    return summed.T.astype(jnp.bfloat16)


def source_table(local, hub_rows, send_rows):
    local_rows = local.T
    hub_local = jnp.take(local_rows, hub_rows, axis=0)
    hub_all = lax.all_gather(hub_local, "dom", axis=0, tiled=True)
    received = [
        trade(jnp.take(local_rows, send_rows[bit_index], axis=0), bit_index)
        for bit_index in range(send_rows.shape[0])
    ]
    return jnp.concatenate([local_rows, hub_all] + received, axis=0)


def contract(left, right):
    return lax.dot_general(
        left, right, (((1,), (1,)), ((), ())), preferred_element_type=jnp.float32
    )


def transpose_times(left, right):
    return lax.dot_general(
        left, right, (((0,), (0,)), ((), ())), preferred_element_type=jnp.float32
    )


def class_gradient(logits, labels, nodes_all):
    expd = jnp.exp(logits)
    probs = expd / jnp.sum(expd, axis=0, keepdims=True)
    classes = lax.broadcasted_iota(jnp.int32, logits.shape, 0)
    onehot = (classes == labels[None, :]).astype(jnp.float32)
    return ((probs - onehot) * (loss_scale / nodes_all)).astype(jnp.bfloat16)


def body(
    features,
    neighbours,
    hub_rows,
    send_rows,
    labels,
    inner_self,
    inner_neighbour,
    outer_self,
    outer_neighbour,
):
    rows = features.shape[1]
    nodes_all = rows * lax.axis_size("dom")
    full_input = lax.all_gather(features, "feat", axis=0, tiled=True)
    mean_one = average(source_table(features, hub_rows, send_rows), neighbours, full_input)
    full_mean = lax.all_gather(mean_one, "feat", axis=0, tiled=True)
    pre_act = jnp.dot(inner_self, full_input, preferred_element_type=jnp.float32)
    pre_act = pre_act + jnp.dot(inner_neighbour, full_mean, preferred_element_type=jnp.float32)
    hidden = jnp.maximum(pre_act, 0.0).astype(jnp.bfloat16)
    mean_two = average(source_table(hidden, hub_rows, send_rows), neighbours, hidden)
    width = hidden.shape[0]
    offset = lax.axis_index("feat") * width
    self_cols = lax.dynamic_slice_in_dim(outer_self, offset, width, 1)
    neigh_cols = lax.dynamic_slice_in_dim(outer_neighbour, offset, width, 1)
    full_hidden, full_two = widen(hidden, mean_two)
    logits = jnp.dot(outer_self, full_hidden, preferred_element_type=jnp.float32)
    logits = logits + jnp.dot(outer_neighbour, full_two, preferred_element_type=jnp.float32)
    logit_grad = class_gradient(logits, labels, nodes_all)
    grad_outer_self = contract(logit_grad, hidden)
    grad_outer_neighbour = contract(logit_grad, mean_two)
    direct = transpose_times(self_cols, logit_grad)
    back_mean = transpose_times(neigh_cols, logit_grad).astype(jnp.bfloat16)
    degree = neighbours.shape[0]
    hub_count = lax.axis_size("dom") * hub_rows.shape[0]
    band = send_rows.shape[1]
    span = rows + hub_count + send_rows.shape[0] * band
    back_rows = back_mean.T.astype(jnp.float32)
    spread = scatter_mean(back_rows, neighbours, span)
    grad_rows = direct.T + spread[:rows]
    owners = lax.axis_size("dom")
    hub_parts = spread[rows : rows + hub_count].reshape(owners, hub_count // owners, width)
    hub_back = jnp.sum(
        lax.all_to_all(
            hub_parts.astype(jnp.bfloat16), "dom", split_axis=0, concat_axis=0, tiled=True
        ).astype(jnp.float32),
        axis=0,
    )
    base = rows + hub_count
    landed = [hub_back]
    for bit_index in range(send_rows.shape[0]):
        outgoing = spread[base + bit_index * band : base + (bit_index + 1) * band].astype(
            jnp.bfloat16
        )
        landed.append(trade(outgoing, bit_index).astype(jnp.float32))
    targets = jnp.concatenate([hub_rows, send_rows.reshape(-1)])
    grad_rows = land_rows(grad_rows, targets, jnp.concatenate(landed, axis=0))
    grad_hidden = grad_rows.T
    grad_pre = jnp.where(hidden > 0, grad_hidden, 0.0).astype(jnp.bfloat16)
    grad_inner_self = contract(grad_pre, full_input)
    grad_inner_neighbour = contract(grad_pre, full_mean)
    pieces = (grad_inner_self, grad_inner_neighbour, grad_outer_self, grad_outer_neighbour)
    summed = tree_sum(jnp.concatenate([piece.reshape(-1) for piece in pieces]), "dom")
    results = []
    offset = 0
    for piece in pieces:
        results.append(summed[offset : offset + piece.size].reshape(piece.shape))
        offset += piece.size
    return tuple(results)


def solution(mesh):
    return jax.shard_map(
        body,
        mesh=mesh,
        in_specs=(
            P("feat", "dom"),
            P(None, "dom"),
            P("dom"),
            P("dom", None),
            P("dom"),
            P("feat", None),
            P("feat", None),
            P(),
            P(),
        ),
        out_specs=(P("feat", None), P("feat", None), P(None, "feat"), P(None, "feat")),
        check_vma=False,
    )
```

```python
import jax
import jax.numpy as jnp
from jax import lax
from jax.sharding import PartitionSpec as P

from jax.experimental import pallas as pl
from jax.experimental.pallas import tpu as pltpu

loss_scale = 4096.0


def gather_mean(table, neighbours, after, block=512):
    size, width = table.shape
    degree, nodes = neighbours.shape

    def kernel(nb_ref, tab_ref, after_ref, out_ref):
        base = pl.program_id(0) * block

        def group(g, carry):
            picked = []
            for r in range(8):
                n = base + g * 8 + r
                acc = tab_ref[pl.ds(nb_ref[0, n], 1), :]
                for k in range(1, degree):
                    acc = acc + tab_ref[pl.ds(nb_ref[k, n], 1), :]
                picked.append(acc)
            start = pl.multiple_of(g * 8, 8)
            out_ref[pl.ds(start, 8), :] = jnp.concatenate(picked, axis=0) / degree
            return carry

        lax.fori_loop(0, block // 8, group, 0)

    return pl.pallas_call(
        kernel,
        grid_spec=pltpu.PrefetchScalarGridSpec(
            num_scalar_prefetch=1,
            grid=(nodes // block,),
            in_specs=[
                pl.BlockSpec((size, width), lambda j, nb: (0, 0)),
                pl.BlockSpec(memory_space=pl.ANY),
            ],
            out_specs=pl.BlockSpec((block, width), lambda j, nb: (j, 0)),
        ),
        out_shape=jax.ShapeDtypeStruct((nodes, width), jnp.float32),
    )(neighbours, table, after)


def scatter_mean(rows, neighbours, own, hubs, bands, chunk=512):
    nodes, width = rows.shape
    degree = neighbours.shape[0]
    half = degree // 2
    size = own + hubs + bands

    def kernel(nb_ref, rows_ref, own_ref, hub_ref, band_ref, first_ref, second_ref):
        first_ref[...] = jnp.zeros_like(first_ref)
        second_ref[...] = jnp.zeros_like(second_ref)

        def step(n, carry):
            x = rows_ref[pl.ds(n, 1), :]
            for k in range(half):
                s = nb_ref[k, n]
                t = nb_ref[k + half, n]
                first_ref[pl.ds(s, 1), :] = first_ref[pl.ds(s, 1), :] + x
                second_ref[pl.ds(t, 1), :] = second_ref[pl.ds(t, 1), :] + x
            return carry

        lax.fori_loop(0, nodes, step, 0, unroll=4)

        for out_ref, start, count in ((own_ref, 0, own), (hub_ref, own, hubs), (band_ref, own + hubs, bands)):

            def finish(c, carry, out_ref=out_ref, start=start):
                r = pl.multiple_of(c * chunk, chunk)
                total = first_ref[pl.ds(start + r, chunk), :] + second_ref[pl.ds(start + r, chunk), :]
                out_ref[pl.ds(r, chunk), :] = (total * (1.0 / degree)).astype(out_ref.dtype)
                return carry

            lax.fori_loop(0, count // chunk, finish, 0)

    return pl.pallas_call(
        kernel,
        in_specs=[
            pl.BlockSpec(memory_space=pltpu.SMEM),
            pl.BlockSpec(memory_space=pltpu.VMEM),
        ],
        out_specs=(
            pl.BlockSpec(memory_space=pltpu.VMEM),
            pl.BlockSpec(memory_space=pltpu.VMEM),
            pl.BlockSpec(memory_space=pltpu.VMEM),
        ),
        out_shape=(
            jax.ShapeDtypeStruct((own, width), jnp.float32),
            jax.ShapeDtypeStruct((hubs, width), jnp.bfloat16),
            jax.ShapeDtypeStruct((bands, width), jnp.bfloat16),
        ),
        scratch_shapes=[
            pltpu.VMEM((size, width), jnp.float32),
            pltpu.VMEM((size, width), jnp.float32),
        ],
    )(neighbours, rows)


def feat_gather(value, axis):
    count = lax.axis_size(axis)
    index = lax.axis_index(axis)
    got = [value] + [
        lax.ppermute(value, axis, [(source, (source + shift) % count) for source in range(count)])
        for shift in range(1, count)
    ]
    stacked = jnp.stack(got[::-1] * 2)
    full = lax.dynamic_slice_in_dim(stacked, (count - 1 - index) % count, count, axis=0)
    return full.reshape(count * value.shape[0], value.shape[1])


def land_rows(base, targets, updates):
    count, width = updates.shape
    half = count // 2

    def kernel(t_ref, base_ref, upd_ref, out_ref, extra_ref):
        out_ref[...] = base_ref[...]
        extra_ref[...] = jnp.zeros_like(extra_ref)

        def step(i, carry):
            s = t_ref[i]
            t = t_ref[i + half]
            out_ref[pl.ds(s, 1), :] = out_ref[pl.ds(s, 1), :] + upd_ref[pl.ds(i, 1), :]
            extra_ref[pl.ds(t, 1), :] = extra_ref[pl.ds(t, 1), :] + upd_ref[pl.ds(i + half, 1), :]
            return carry

        lax.fori_loop(0, half, step, 0, unroll=4)
        for i in range(2 * half, count):
            s = t_ref[i]
            out_ref[pl.ds(s, 1), :] = out_ref[pl.ds(s, 1), :] + upd_ref[pl.ds(i, 1), :]
        out_ref[...] = out_ref[...] + extra_ref[...]

    return pl.pallas_call(
        kernel,
        in_specs=[
            pl.BlockSpec(memory_space=pltpu.SMEM),
            pl.BlockSpec(memory_space=pltpu.VMEM),
            pl.BlockSpec(memory_space=pltpu.VMEM),
        ],
        out_specs=pl.BlockSpec(memory_space=pltpu.VMEM),
        out_shape=jax.ShapeDtypeStruct(base.shape, jnp.float32),
        scratch_shapes=[pltpu.VMEM(base.shape, jnp.float32)],
    )(targets, base, updates)


def tree_gather(value, axis):
    count = lax.axis_size(axis)
    index = lax.axis_index(axis)
    block = value
    stride = 1
    while stride < count:
        pairs = [(source, source ^ stride) for source in range(count)]
        other = lax.ppermute(block, axis, pairs)
        low = (index // stride) % 2 == 0
        block = jnp.where(
            low, jnp.concatenate([block, other], axis=0), jnp.concatenate([other, block], axis=0)
        )
        stride *= 2
    return block


def tree_sum(value, axis):
    count = lax.axis_size(axis)
    stride = 1
    while stride < count:
        pairs = [(source, source ^ stride) for source in range(count)]
        value = value + lax.ppermute(value, axis, pairs)
        stride *= 2
    return value


def tree_scatter(value, axis):
    count = lax.axis_size(axis)
    index = lax.axis_index(axis)
    width = value.shape[1]
    parts = value.reshape(count, -1, width)
    rows = parts.shape[1]
    stride = 1
    while stride < count:
        bit = (index // stride) % 2
        paired = parts.reshape(parts.shape[0] // 2, 2, rows, width)
        keep = lax.dynamic_index_in_dim(paired, bit, axis=1, keepdims=False)
        send = lax.dynamic_index_in_dim(paired, 1 - bit, axis=1, keepdims=False)
        pairs = [(source, source ^ stride) for source in range(count)]
        parts = keep + lax.ppermute(send, axis, pairs)
        stride *= 2
    return parts.reshape(rows, width)


def partner(value, axis, stride):
    mask = 2**stride
    pairs = [(source, source ^ mask) for source in range(lax.axis_size(axis))]
    return lax.ppermute(value, axis, pairs)


def trade(piece, bit_index):
    return partner(piece, "dom", bit_index)


def widen(first_rows, second_rows):
    return (
        lax.all_gather(first_rows, "feat", axis=0, tiled=True),
        lax.all_gather(second_rows, "feat", axis=0, tiled=True),
    )


def average(table_rows, neighbours, after):
    summed = gather_mean(table_rows.astype(jnp.float32), neighbours, after)
    return summed.T.astype(jnp.bfloat16)


def source_table(local, hub_rows, send_rows):
    local_rows = local.T
    hub_local = jnp.take(local_rows, hub_rows, axis=0)
    hub_all = lax.all_gather(hub_local, "dom", axis=0, tiled=True)
    received = [
        trade(jnp.take(local_rows, send_rows[bit_index], axis=0), bit_index)
        for bit_index in range(send_rows.shape[0])
    ]
    return jnp.concatenate([local_rows, hub_all] + received, axis=0)


def contract(left, right):
    return lax.dot_general(
        left, right, (((1,), (1,)), ((), ())), preferred_element_type=jnp.float32
    )


def transpose_times(left, right):
    return lax.dot_general(
        left, right, (((0,), (0,)), ((), ())), preferred_element_type=jnp.float32
    )


def class_gradient(logits, labels, nodes_all):
    expd = jnp.exp(logits)
    probs = expd / jnp.sum(expd, axis=0, keepdims=True)
    classes = lax.broadcasted_iota(jnp.int32, logits.shape, 0)
    onehot = (classes == labels[None, :]).astype(jnp.float32)
    return ((probs - onehot) * (loss_scale / nodes_all)).astype(jnp.bfloat16)


def body(
    features,
    neighbours,
    hub_rows,
    send_rows,
    labels,
    inner_self,
    inner_neighbour,
    outer_self,
    outer_neighbour,
):
    rows = features.shape[1]
    nodes_all = rows * lax.axis_size("dom")
    full_input = lax.all_gather(features, "feat", axis=0, tiled=True)
    mean_one = average(source_table(features, hub_rows, send_rows), neighbours, full_input)
    full_mean = feat_gather(mean_one, "feat")
    pre_act = jnp.dot(inner_self, full_input, preferred_element_type=jnp.float32)
    pre_act = pre_act + jnp.dot(inner_neighbour, full_mean, preferred_element_type=jnp.float32)
    hidden = jnp.maximum(pre_act, 0.0).astype(jnp.bfloat16)
    mean_two = average(source_table(hidden, hub_rows, send_rows), neighbours, hidden)
    width = hidden.shape[0]
    offset = lax.axis_index("feat") * width
    self_cols = lax.dynamic_slice_in_dim(outer_self, offset, width, 1)
    neigh_cols = lax.dynamic_slice_in_dim(outer_neighbour, offset, width, 1)
    full_hidden = lax.all_gather(hidden, "feat", axis=0, tiled=True)
    full_two = feat_gather(mean_two, "feat")
    logits = jnp.dot(outer_self, full_hidden, preferred_element_type=jnp.float32)
    logits = logits + jnp.dot(outer_neighbour, full_two, preferred_element_type=jnp.float32)
    logit_grad = class_gradient(logits, labels, nodes_all)
    grad_outer_self = contract(logit_grad, hidden)
    grad_outer_neighbour = contract(logit_grad, mean_two)
    direct = transpose_times(self_cols, logit_grad)
    back_mean = transpose_times(neigh_cols, logit_grad).astype(jnp.bfloat16)
    degree = neighbours.shape[0]
    hub_count = lax.axis_size("dom") * hub_rows.shape[0]
    band = send_rows.shape[1]
    span = rows + hub_count + send_rows.shape[0] * band
    back_rows = back_mean.T.astype(jnp.float32)
    own_grad, hub_grad, band_grad = scatter_mean(
        back_rows, neighbours, rows, hub_count, send_rows.shape[0] * band
    )
    grad_rows = direct.T + own_grad
    owners = lax.axis_size("dom")
    hub_parts = hub_grad.reshape(owners, hub_count // owners, width)
    hub_back = jnp.sum(
        lax.all_to_all(hub_parts, "dom", split_axis=0, concat_axis=0, tiled=True).astype(
            jnp.float32
        ),
        axis=0,
    )
    landed = [hub_back]
    for bit_index in range(send_rows.shape[0]):
        outgoing = band_grad[bit_index * band : (bit_index + 1) * band]
        landed.append(trade(outgoing, bit_index).astype(jnp.float32))
    targets = jnp.concatenate([hub_rows, send_rows.reshape(-1)])
    grad_rows = land_rows(grad_rows, targets, jnp.concatenate(landed, axis=0))
    grad_hidden = grad_rows.T
    grad_pre = jnp.where(hidden > 0, grad_hidden, 0.0).astype(jnp.bfloat16)
    grad_inner_self = contract(grad_pre, full_input)
    grad_inner_neighbour = contract(grad_pre, full_mean)
    pieces = (grad_inner_self, grad_inner_neighbour, grad_outer_self, grad_outer_neighbour)
    summed = tree_sum(jnp.concatenate([piece.reshape(-1) for piece in pieces]), "dom")
    results = []
    offset = 0
    for piece in pieces:
        results.append(summed[offset : offset + piece.size].reshape(piece.shape))
        offset += piece.size
    return tuple(results)


def solution(mesh):
    return jax.shard_map(
        body,
        mesh=mesh,
        in_specs=(
            P("feat", "dom"),
            P(None, "dom"),
            P("dom"),
            P("dom", None),
            P("dom"),
            P("feat", None),
            P("feat", None),
            P(),
            P(),
        ),
        out_specs=(P("feat", None), P("feat", None), P(None, "feat"), P(None, "feat")),
        check_vma=False,
    )
```

```python
import jax
import jax.numpy as jnp
from jax import lax
from jax.sharding import PartitionSpec as P

from jax.experimental import pallas as pl
from jax.experimental.pallas import tpu as pltpu

loss_scale = 4096.0


def gather_mean(table, neighbours, after, block=512):
    size, width = table.shape
    degree, nodes = neighbours.shape

    def kernel(nb_ref, tab_ref, after_ref, out_ref):
        base = pl.program_id(0) * block

        def group(g, carry):
            picked = []
            for r in range(8):
                n = base + g * 8 + r
                acc = tab_ref[pl.ds(nb_ref[0, n], 1), :]
                for k in range(1, degree):
                    acc = acc + tab_ref[pl.ds(nb_ref[k, n], 1), :]
                picked.append(acc)
            start = pl.multiple_of(g * 8, 8)
            out_ref[pl.ds(start, 8), :] = jnp.concatenate(picked, axis=0) / degree
            return carry

        lax.fori_loop(0, block // 8, group, 0)

    return pl.pallas_call(
        kernel,
        grid_spec=pltpu.PrefetchScalarGridSpec(
            num_scalar_prefetch=1,
            grid=(nodes // block,),
            in_specs=[
                pl.BlockSpec((size, width), lambda j, nb: (0, 0)),
                pl.BlockSpec(memory_space=pl.ANY),
            ],
            out_specs=pl.BlockSpec((block, width), lambda j, nb: (j, 0)),
        ),
        out_shape=jax.ShapeDtypeStruct((nodes, width), jnp.float32),
    )(neighbours, table, after)


def scatter_mean(rows, neighbours, size, chains=4):
    nodes, width = rows.shape
    degree = neighbours.shape[0]
    per_chain = degree // chains

    def kernel(nb_ref, rows_ref, out_ref, *extra_refs):
        accumulators = (out_ref,) + extra_refs
        for acc_ref in accumulators:
            acc_ref[...] = jnp.zeros_like(acc_ref)

        def step(n, carry):
            x = rows_ref[pl.ds(n, 1), :]
            for k in range(per_chain):
                for chain, acc_ref in enumerate(accumulators):
                    s = nb_ref[chain * per_chain + k, n]
                    acc_ref[pl.ds(s, 1), :] = acc_ref[pl.ds(s, 1), :] + x
            return carry

        lax.fori_loop(0, nodes, step, 0, unroll=2)
        total = out_ref[...]
        for acc_ref in extra_refs:
            total = total + acc_ref[...]
        out_ref[...] = total * (1.0 / degree)

    return pl.pallas_call(
        kernel,
        in_specs=[
            pl.BlockSpec(memory_space=pltpu.SMEM),
            pl.BlockSpec(memory_space=pltpu.VMEM),
        ],
        out_specs=pl.BlockSpec(memory_space=pltpu.VMEM),
        out_shape=jax.ShapeDtypeStruct((size, width), jnp.float32),
        scratch_shapes=[pltpu.VMEM((size, width), jnp.float32) for _ in range(chains - 1)],
        compiler_params=pltpu.CompilerParams(vmem_limit_bytes=63 * 1024 * 1024),
    )(neighbours, rows)


def land_rows(base, targets, updates):
    count, width = updates.shape
    half = count // 2

    def kernel(t_ref, base_ref, upd_ref, out_ref, extra_ref):
        out_ref[...] = base_ref[...]
        extra_ref[...] = jnp.zeros_like(extra_ref)

        def step(i, carry):
            s = t_ref[i]
            t = t_ref[i + half]
            out_ref[pl.ds(s, 1), :] = out_ref[pl.ds(s, 1), :] + upd_ref[pl.ds(i, 1), :]
            extra_ref[pl.ds(t, 1), :] = extra_ref[pl.ds(t, 1), :] + upd_ref[pl.ds(i + half, 1), :]
            return carry

        lax.fori_loop(0, half, step, 0, unroll=4)
        for i in range(2 * half, count):
            s = t_ref[i]
            out_ref[pl.ds(s, 1), :] = out_ref[pl.ds(s, 1), :] + upd_ref[pl.ds(i, 1), :]
        out_ref[...] = out_ref[...] + extra_ref[...]

    return pl.pallas_call(
        kernel,
        in_specs=[
            pl.BlockSpec(memory_space=pltpu.SMEM),
            pl.BlockSpec(memory_space=pltpu.VMEM),
            pl.BlockSpec(memory_space=pltpu.VMEM),
        ],
        out_specs=pl.BlockSpec(memory_space=pltpu.VMEM),
        out_shape=jax.ShapeDtypeStruct(base.shape, jnp.float32),
        scratch_shapes=[pltpu.VMEM(base.shape, jnp.float32)],
    )(targets, base, updates)


def tree_gather(value, axis):
    count = lax.axis_size(axis)
    index = lax.axis_index(axis)
    block = value
    stride = 1
    while stride < count:
        pairs = [(source, source ^ stride) for source in range(count)]
        other = lax.ppermute(block, axis, pairs)
        low = (index // stride) % 2 == 0
        block = jnp.where(
            low, jnp.concatenate([block, other], axis=0), jnp.concatenate([other, block], axis=0)
        )
        stride *= 2
    return block


def tree_sum(value, axis):
    count = lax.axis_size(axis)
    stride = 1
    while stride < count:
        pairs = [(source, source ^ stride) for source in range(count)]
        value = value + lax.ppermute(value, axis, pairs)
        stride *= 2
    return value


def tree_scatter(value, axis):
    count = lax.axis_size(axis)
    index = lax.axis_index(axis)
    width = value.shape[1]
    parts = value.reshape(count, -1, width)
    rows = parts.shape[1]
    stride = 1
    while stride < count:
        bit = (index // stride) % 2
        paired = parts.reshape(parts.shape[0] // 2, 2, rows, width)
        keep = lax.dynamic_index_in_dim(paired, bit, axis=1, keepdims=False)
        send = lax.dynamic_index_in_dim(paired, 1 - bit, axis=1, keepdims=False)
        pairs = [(source, source ^ stride) for source in range(count)]
        parts = keep + lax.ppermute(send, axis, pairs)
        stride *= 2
    return parts.reshape(rows, width)


def partner(value, axis, stride):
    mask = 2**stride
    pairs = [(source, source ^ mask) for source in range(lax.axis_size(axis))]
    return lax.ppermute(value, axis, pairs)


def trade(piece, bit_index):
    return partner(piece, "dom", bit_index)


def widen(first_rows, second_rows):
    return (
        lax.all_gather(first_rows, "feat", axis=0, tiled=True),
        lax.all_gather(second_rows, "feat", axis=0, tiled=True),
    )


def average(table_rows, neighbours, after):
    summed = gather_mean(table_rows.astype(jnp.float32), neighbours, after)
    return summed.T.astype(jnp.bfloat16)


def source_table(local, hub_rows, send_rows):
    local_rows = local.T
    hub_local = jnp.take(local_rows, hub_rows, axis=0)
    hub_all = lax.all_gather(hub_local, "dom", axis=0, tiled=True)
    received = [
        trade(jnp.take(local_rows, send_rows[bit_index], axis=0), bit_index)
        for bit_index in range(send_rows.shape[0])
    ]
    return jnp.concatenate([local_rows, hub_all] + received, axis=0)


def contract(left, right):
    return lax.dot_general(
        left, right, (((1,), (1,)), ((), ())), preferred_element_type=jnp.float32
    )


def transpose_times(left, right):
    return lax.dot_general(
        left, right, (((0,), (0,)), ((), ())), preferred_element_type=jnp.float32
    )


def class_gradient(logits, labels, nodes_all):
    expd = jnp.exp(logits)
    probs = expd / jnp.sum(expd, axis=0, keepdims=True)
    classes = lax.broadcasted_iota(jnp.int32, logits.shape, 0)
    onehot = (classes == labels[None, :]).astype(jnp.float32)
    return ((probs - onehot) * (loss_scale / nodes_all)).astype(jnp.bfloat16)


def body(
    features,
    neighbours,
    hub_rows,
    send_rows,
    labels,
    inner_self,
    inner_neighbour,
    outer_self,
    outer_neighbour,
):
    rows = features.shape[1]
    nodes_all = rows * lax.axis_size("dom")
    full_input = lax.all_gather(features, "feat", axis=0, tiled=True)
    mean_one = average(source_table(features, hub_rows, send_rows), neighbours, full_input)
    full_mean = lax.all_gather(mean_one, "feat", axis=0, tiled=True)
    pre_act = jnp.dot(inner_self, full_input, preferred_element_type=jnp.float32)
    pre_act = pre_act + jnp.dot(inner_neighbour, full_mean, preferred_element_type=jnp.float32)
    hidden = jnp.maximum(pre_act, 0.0).astype(jnp.bfloat16)
    mean_two = average(source_table(hidden, hub_rows, send_rows), neighbours, hidden)
    width = hidden.shape[0]
    offset = lax.axis_index("feat") * width
    self_cols = lax.dynamic_slice_in_dim(outer_self, offset, width, 1)
    neigh_cols = lax.dynamic_slice_in_dim(outer_neighbour, offset, width, 1)
    full_hidden, full_two = widen(hidden, mean_two)
    logits = jnp.dot(outer_self, full_hidden, preferred_element_type=jnp.float32)
    logits = logits + jnp.dot(outer_neighbour, full_two, preferred_element_type=jnp.float32)
    logit_grad = class_gradient(logits, labels, nodes_all)
    grad_outer_self = contract(logit_grad, hidden)
    grad_outer_neighbour = contract(logit_grad, mean_two)
    direct = transpose_times(self_cols, logit_grad)
    back_mean = transpose_times(neigh_cols, logit_grad).astype(jnp.bfloat16)
    degree = neighbours.shape[0]
    hub_count = lax.axis_size("dom") * hub_rows.shape[0]
    band = send_rows.shape[1]
    span = rows + hub_count + send_rows.shape[0] * band
    back_rows = back_mean.T.astype(jnp.float32)
    spread = scatter_mean(back_rows, neighbours, span)
    grad_rows = direct.T + spread[:rows]
    owners = lax.axis_size("dom")
    hub_parts = spread[rows : rows + hub_count].reshape(owners, hub_count // owners, width)
    hub_back = jnp.sum(
        lax.all_to_all(
            hub_parts.astype(jnp.bfloat16), "dom", split_axis=0, concat_axis=0, tiled=True
        ).astype(jnp.float32),
        axis=0,
    )
    base = rows + hub_count
    landed = [hub_back]
    for bit_index in range(send_rows.shape[0]):
        outgoing = spread[base + bit_index * band : base + (bit_index + 1) * band].astype(
            jnp.bfloat16
        )
        landed.append(trade(outgoing, bit_index).astype(jnp.float32))
    targets = jnp.concatenate([hub_rows, send_rows.reshape(-1)])
    grad_rows = land_rows(grad_rows, targets, jnp.concatenate(landed, axis=0))
    grad_hidden = grad_rows.T
    grad_pre = jnp.where(hidden > 0, grad_hidden, 0.0).astype(jnp.bfloat16)
    grad_inner_self = contract(grad_pre, full_input)
    grad_inner_neighbour = contract(grad_pre, full_mean)
    pieces = (grad_inner_self, grad_inner_neighbour, grad_outer_self, grad_outer_neighbour)
    summed = tree_sum(jnp.concatenate([piece.reshape(-1) for piece in pieces]), "dom")
    results = []
    offset = 0
    for piece in pieces:
        results.append(summed[offset : offset + piece.size].reshape(piece.shape))
        offset += piece.size
    return tuple(results)


def solution(mesh):
    return jax.shard_map(
        body,
        mesh=mesh,
        in_specs=(
            P("feat", "dom"),
            P(None, "dom"),
            P("dom"),
            P("dom", None),
            P("dom"),
            P("feat", None),
            P("feat", None),
            P(),
            P(),
        ),
        out_specs=(P("feat", None), P("feat", None), P(None, "feat"), P(None, "feat")),
        check_vma=False,
    )
```

```python
import math

import jax
import jax.numpy as jnp
from jax import lax
from jax.sharding import PartitionSpec as P

from jax.experimental import pallas as pl
from jax.experimental.pallas import tpu as pltpu

loss_scale = 4096.0


def gather_mean(pieces, neighbours, after):
    width = pieces[0].shape[1]
    degree, nodes = neighbours.shape
    size = sum(piece.shape[0] for piece in pieces)
    chunk = 512
    for piece in pieces:
        chunk = math.gcd(chunk, piece.shape[0])

    def kernel(nb_ref, *refs):
        piece_refs = refs[: len(pieces)]
        out_ref = refs[len(pieces) + 1]
        tab_ref = refs[len(pieces) + 2]
        start = 0
        for piece_ref, piece in zip(piece_refs, pieces):

            def fill(c, carry, piece_ref=piece_ref, start=start):
                r = pl.multiple_of(c * chunk, chunk)
                tab_ref[pl.ds(start + r, chunk), :] = piece_ref[pl.ds(r, chunk), :].astype(jnp.float32)
                return carry

            lax.fori_loop(0, piece.shape[0] // chunk, fill, 0)
            start += piece.shape[0]

        def body(n, carry):
            acc = tab_ref[pl.ds(nb_ref[0, n], 1), :]
            for k in range(1, degree):
                acc = acc + tab_ref[pl.ds(nb_ref[k, n], 1), :]
            out_ref[pl.ds(n, 1), :] = acc / degree
            return carry

        lax.fori_loop(0, nodes, body, 0, unroll=8)

    return pl.pallas_call(
        kernel,
        in_specs=[pl.BlockSpec(memory_space=pltpu.SMEM)]
        + [pl.BlockSpec(memory_space=pltpu.VMEM) for _ in pieces]
        + [pl.BlockSpec(memory_space=pl.ANY)],
        out_specs=pl.BlockSpec(memory_space=pltpu.VMEM),
        out_shape=jax.ShapeDtypeStruct((nodes, width), jnp.float32),
        scratch_shapes=[pltpu.VMEM((size, width), jnp.float32)],
    )(neighbours, *pieces, after)


def scatter_mean(rows, neighbours, size, chains=4):
    nodes, width = rows.shape
    degree = neighbours.shape[0]
    per_chain = degree // chains

    def kernel(nb_ref, rows_ref, out_ref, *extra_refs):
        accumulators = (out_ref,) + extra_refs
        for acc_ref in accumulators:
            acc_ref[...] = jnp.zeros_like(acc_ref)

        def step(n, carry):
            x = rows_ref[pl.ds(n, 1), :]
            for k in range(per_chain):
                for chain, acc_ref in enumerate(accumulators):
                    s = nb_ref[chain * per_chain + k, n]
                    acc_ref[pl.ds(s, 1), :] = acc_ref[pl.ds(s, 1), :] + x
            return carry

        lax.fori_loop(0, nodes, step, 0, unroll=2)
        total = out_ref[...]
        for acc_ref in extra_refs:
            total = total + acc_ref[...]
        out_ref[...] = total * (1.0 / degree)

    return pl.pallas_call(
        kernel,
        in_specs=[
            pl.BlockSpec(memory_space=pltpu.SMEM),
            pl.BlockSpec(memory_space=pltpu.VMEM),
        ],
        out_specs=pl.BlockSpec(memory_space=pltpu.VMEM),
        out_shape=jax.ShapeDtypeStruct((size, width), jnp.float32),
        scratch_shapes=[pltpu.VMEM((size, width), jnp.float32) for _ in range(chains - 1)],
        compiler_params=pltpu.CompilerParams(vmem_limit_bytes=63 * 1024 * 1024),
    )(neighbours, rows)


def land_rows(base, targets, updates):
    count, width = updates.shape
    half = count // 2

    def kernel(t_ref, base_ref, upd_ref, out_ref, extra_ref):
        out_ref[...] = base_ref[...]
        extra_ref[...] = jnp.zeros_like(extra_ref)

        def step(i, carry):
            s = t_ref[i]
            t = t_ref[i + half]
            out_ref[pl.ds(s, 1), :] = out_ref[pl.ds(s, 1), :] + upd_ref[pl.ds(i, 1), :]
            extra_ref[pl.ds(t, 1), :] = extra_ref[pl.ds(t, 1), :] + upd_ref[pl.ds(i + half, 1), :]
            return carry

        lax.fori_loop(0, half, step, 0, unroll=4)
        for i in range(2 * half, count):
            s = t_ref[i]
            out_ref[pl.ds(s, 1), :] = out_ref[pl.ds(s, 1), :] + upd_ref[pl.ds(i, 1), :]
        out_ref[...] = out_ref[...] + extra_ref[...]

    return pl.pallas_call(
        kernel,
        in_specs=[
            pl.BlockSpec(memory_space=pltpu.SMEM),
            pl.BlockSpec(memory_space=pltpu.VMEM),
            pl.BlockSpec(memory_space=pltpu.VMEM),
        ],
        out_specs=pl.BlockSpec(memory_space=pltpu.VMEM),
        out_shape=jax.ShapeDtypeStruct(base.shape, jnp.float32),
        scratch_shapes=[pltpu.VMEM(base.shape, jnp.float32)],
    )(targets, base, updates)


def tree_gather(value, axis):
    count = lax.axis_size(axis)
    index = lax.axis_index(axis)
    block = value
    stride = 1
    while stride < count:
        pairs = [(source, source ^ stride) for source in range(count)]
        other = lax.ppermute(block, axis, pairs)
        low = (index // stride) % 2 == 0
        block = jnp.where(
            low, jnp.concatenate([block, other], axis=0), jnp.concatenate([other, block], axis=0)
        )
        stride *= 2
    return block


def tree_sum(value, axis):
    count = lax.axis_size(axis)
    stride = 1
    while stride < count:
        pairs = [(source, source ^ stride) for source in range(count)]
        value = value + lax.ppermute(value, axis, pairs)
        stride *= 2
    return value


def tree_scatter(value, axis):
    count = lax.axis_size(axis)
    index = lax.axis_index(axis)
    width = value.shape[1]
    parts = value.reshape(count, -1, width)
    rows = parts.shape[1]
    stride = 1
    while stride < count:
        bit = (index // stride) % 2
        paired = parts.reshape(parts.shape[0] // 2, 2, rows, width)
        keep = lax.dynamic_index_in_dim(paired, bit, axis=1, keepdims=False)
        send = lax.dynamic_index_in_dim(paired, 1 - bit, axis=1, keepdims=False)
        pairs = [(source, source ^ stride) for source in range(count)]
        parts = keep + lax.ppermute(send, axis, pairs)
        stride *= 2
    return parts.reshape(rows, width)


def partner(value, axis, stride):
    mask = 2**stride
    pairs = [(source, source ^ mask) for source in range(lax.axis_size(axis))]
    return lax.ppermute(value, axis, pairs)


def trade(piece, bit_index):
    return partner(piece, "dom", bit_index)


def widen(first_rows, second_rows):
    return (
        lax.all_gather(first_rows, "feat", axis=0, tiled=True),
        lax.all_gather(second_rows, "feat", axis=0, tiled=True),
    )


def average(pieces, neighbours, after):
    summed = gather_mean(pieces, neighbours, after)
    return summed.T.astype(jnp.bfloat16)


def source_table(local, hub_rows, send_rows):
    local_rows = local.T
    hub_local = jnp.take(local_rows, hub_rows, axis=0)
    hub_all = lax.all_gather(hub_local, "dom", axis=0, tiled=True)
    received = [
        trade(jnp.take(local_rows, send_rows[bit_index], axis=0), bit_index)
        for bit_index in range(send_rows.shape[0])
    ]
    return [local_rows, hub_all] + received


def contract(left, right):
    return lax.dot_general(
        left, right, (((1,), (1,)), ((), ())), preferred_element_type=jnp.float32
    )


def transpose_times(left, right):
    return lax.dot_general(
        left, right, (((0,), (0,)), ((), ())), preferred_element_type=jnp.float32
    )


def class_gradient(logits, labels, nodes_all):
    expd = jnp.exp(logits)
    probs = expd / jnp.sum(expd, axis=0, keepdims=True)
    classes = lax.broadcasted_iota(jnp.int32, logits.shape, 0)
    onehot = (classes == labels[None, :]).astype(jnp.float32)
    return ((probs - onehot) * (loss_scale / nodes_all)).astype(jnp.bfloat16)


def body(
    features,
    neighbours,
    hub_rows,
    send_rows,
    labels,
    inner_self,
    inner_neighbour,
    outer_self,
    outer_neighbour,
):
    rows = features.shape[1]
    nodes_all = rows * lax.axis_size("dom")
    full_input = lax.all_gather(features, "feat", axis=0, tiled=True)
    mean_one = average(source_table(features, hub_rows, send_rows), neighbours, full_input)
    full_mean = lax.all_gather(mean_one, "feat", axis=0, tiled=True)
    pre_act = jnp.dot(inner_self, full_input, preferred_element_type=jnp.float32)
    pre_act = pre_act + jnp.dot(inner_neighbour, full_mean, preferred_element_type=jnp.float32)
    hidden = jnp.maximum(pre_act, 0.0).astype(jnp.bfloat16)
    mean_two = average(source_table(hidden, hub_rows, send_rows), neighbours, hidden)
    width = hidden.shape[0]
    offset = lax.axis_index("feat") * width
    self_cols = lax.dynamic_slice_in_dim(outer_self, offset, width, 1)
    neigh_cols = lax.dynamic_slice_in_dim(outer_neighbour, offset, width, 1)
    full_hidden, full_two = widen(hidden, mean_two)
    logits = jnp.dot(outer_self, full_hidden, preferred_element_type=jnp.float32)
    logits = logits + jnp.dot(outer_neighbour, full_two, preferred_element_type=jnp.float32)
    logit_grad = class_gradient(logits, labels, nodes_all)
    grad_outer_self = contract(logit_grad, hidden)
    grad_outer_neighbour = contract(logit_grad, mean_two)
    direct = transpose_times(self_cols, logit_grad)
    back_mean = transpose_times(neigh_cols, logit_grad).astype(jnp.bfloat16)
    degree = neighbours.shape[0]
    hub_count = lax.axis_size("dom") * hub_rows.shape[0]
    band = send_rows.shape[1]
    span = rows + hub_count + send_rows.shape[0] * band
    back_rows = back_mean.T.astype(jnp.float32)
    spread = scatter_mean(back_rows, neighbours, span)
    grad_rows = direct.T + spread[:rows]
    owners = lax.axis_size("dom")
    hub_parts = spread[rows : rows + hub_count].reshape(owners, hub_count // owners, width)
    hub_back = jnp.sum(
        lax.all_to_all(
            hub_parts.astype(jnp.bfloat16), "dom", split_axis=0, concat_axis=0, tiled=True
        ).astype(jnp.float32),
        axis=0,
    )
    base = rows + hub_count
    landed = [hub_back]
    for bit_index in range(send_rows.shape[0]):
        outgoing = spread[base + bit_index * band : base + (bit_index + 1) * band].astype(
            jnp.bfloat16
        )
        landed.append(trade(outgoing, bit_index).astype(jnp.float32))
    targets = jnp.concatenate([hub_rows, send_rows.reshape(-1)])
    grad_rows = land_rows(grad_rows, targets, jnp.concatenate(landed, axis=0))
    grad_hidden = grad_rows.T
    grad_pre = jnp.where(hidden > 0, grad_hidden, 0.0).astype(jnp.bfloat16)
    grad_inner_self = contract(grad_pre, full_input)
    grad_inner_neighbour = contract(grad_pre, full_mean)
    pieces = (grad_inner_self, grad_inner_neighbour, grad_outer_self, grad_outer_neighbour)
    summed = tree_sum(jnp.concatenate([piece.reshape(-1) for piece in pieces]), "dom")
    results = []
    offset = 0
    for piece in pieces:
        results.append(summed[offset : offset + piece.size].reshape(piece.shape))
        offset += piece.size
    return tuple(results)


def solution(mesh):
    return jax.shard_map(
        body,
        mesh=mesh,
        in_specs=(
            P("feat", "dom"),
            P(None, "dom"),
            P("dom"),
            P("dom", None),
            P("dom"),
            P("feat", None),
            P("feat", None),
            P(),
            P(),
        ),
        out_specs=(P("feat", None), P("feat", None), P(None, "feat"), P(None, "feat")),
        check_vma=False,
    )
```

```python
import math

import jax
import jax.numpy as jnp
from jax import lax
from jax.sharding import PartitionSpec as P

from jax.experimental import pallas as pl
from jax.experimental.pallas import tpu as pltpu

loss_scale = 4096.0


def gather_mean(pieces, neighbours, after):
    width = pieces[0].shape[1]
    degree, nodes = neighbours.shape
    size = sum(piece.shape[0] for piece in pieces)
    chunk = 512
    for piece in pieces:
        chunk = math.gcd(chunk, piece.shape[0])

    def kernel(nb_ref, *refs):
        piece_refs = refs[: len(pieces)]
        out_ref = refs[len(pieces) + 1]
        tab_ref = refs[len(pieces) + 2]
        start = 0
        for piece_ref, piece in zip(piece_refs, pieces):

            def fill(c, carry, piece_ref=piece_ref, start=start):
                r = pl.multiple_of(c * chunk, chunk)
                tab_ref[pl.ds(start + r, chunk), :] = piece_ref[pl.ds(r, chunk), :].astype(jnp.float32)
                return carry

            lax.fori_loop(0, piece.shape[0] // chunk, fill, 0)
            start += piece.shape[0]

        def body(n, carry):
            acc = tab_ref[pl.ds(nb_ref[0, n], 1), :]
            for k in range(1, degree):
                acc = acc + tab_ref[pl.ds(nb_ref[k, n], 1), :]
            out_ref[pl.ds(n, 1), :] = acc / degree
            return carry

        lax.fori_loop(0, nodes, body, 0, unroll=8)

    return pl.pallas_call(
        kernel,
        in_specs=[pl.BlockSpec(memory_space=pltpu.SMEM)]
        + [pl.BlockSpec(memory_space=pltpu.VMEM) for _ in pieces]
        + [pl.BlockSpec(memory_space=pl.ANY)],
        out_specs=pl.BlockSpec(memory_space=pltpu.VMEM),
        out_shape=jax.ShapeDtypeStruct((nodes, width), jnp.float32),
        scratch_shapes=[pltpu.VMEM((size, width), jnp.float32)],
    )(neighbours, *pieces, after)


def scatter_mean(rows, neighbours, size, chains=4):
    nodes, width = rows.shape
    degree = neighbours.shape[0]
    per_chain = degree // chains

    def kernel(nb_ref, rows_ref, out_ref, *extra_refs):
        accumulators = (out_ref,) + extra_refs
        for acc_ref in accumulators:
            acc_ref[...] = jnp.zeros_like(acc_ref)

        def step(n, carry):
            x = rows_ref[pl.ds(n, 1), :]
            for k in range(per_chain):
                for chain, acc_ref in enumerate(accumulators):
                    s = nb_ref[chain * per_chain + k, n]
                    acc_ref[pl.ds(s, 1), :] = acc_ref[pl.ds(s, 1), :] + x
            return carry

        lax.fori_loop(0, nodes, step, 0, unroll=2)
        total = out_ref[...]
        for acc_ref in extra_refs:
            total = total + acc_ref[...]
        out_ref[...] = total * (1.0 / degree)

    return pl.pallas_call(
        kernel,
        in_specs=[
            pl.BlockSpec(memory_space=pltpu.SMEM),
            pl.BlockSpec(memory_space=pltpu.VMEM),
        ],
        out_specs=pl.BlockSpec(memory_space=pltpu.VMEM),
        out_shape=jax.ShapeDtypeStruct((size, width), jnp.float32),
        scratch_shapes=[pltpu.VMEM((size, width), jnp.float32) for _ in range(chains - 1)],
        compiler_params=pltpu.CompilerParams(vmem_limit_bytes=63 * 1024 * 1024),
    )(neighbours, rows)


def feat_gather(value, axis):
    count = lax.axis_size(axis)
    index = lax.axis_index(axis)
    got = [value] + [
        lax.ppermute(value, axis, [(source, (source + shift) % count) for source in range(count)])
        for shift in range(1, count)
    ]
    stacked = jnp.stack(got[::-1] * 2)
    full = lax.dynamic_slice_in_dim(stacked, (count - 1 - index) % count, count, axis=0)
    return full.reshape(count * value.shape[0], value.shape[1])


def land_rows(base, targets, updates):
    count, width = updates.shape
    half = count // 2

    def kernel(t_ref, base_ref, upd_ref, out_ref, extra_ref):
        out_ref[...] = base_ref[...]
        extra_ref[...] = jnp.zeros_like(extra_ref)

        def step(i, carry):
            s = t_ref[i]
            t = t_ref[i + half]
            out_ref[pl.ds(s, 1), :] = out_ref[pl.ds(s, 1), :] + upd_ref[pl.ds(i, 1), :]
            extra_ref[pl.ds(t, 1), :] = extra_ref[pl.ds(t, 1), :] + upd_ref[pl.ds(i + half, 1), :]
            return carry

        lax.fori_loop(0, half, step, 0, unroll=4)
        for i in range(2 * half, count):
            s = t_ref[i]
            out_ref[pl.ds(s, 1), :] = out_ref[pl.ds(s, 1), :] + upd_ref[pl.ds(i, 1), :]
        out_ref[...] = out_ref[...] + extra_ref[...]

    return pl.pallas_call(
        kernel,
        in_specs=[
            pl.BlockSpec(memory_space=pltpu.SMEM),
            pl.BlockSpec(memory_space=pltpu.VMEM),
            pl.BlockSpec(memory_space=pltpu.VMEM),
        ],
        out_specs=pl.BlockSpec(memory_space=pltpu.VMEM),
        out_shape=jax.ShapeDtypeStruct(base.shape, jnp.float32),
        scratch_shapes=[pltpu.VMEM(base.shape, jnp.float32)],
    )(targets, base, updates)


def tree_gather(value, axis):
    count = lax.axis_size(axis)
    index = lax.axis_index(axis)
    block = value
    stride = 1
    while stride < count:
        pairs = [(source, source ^ stride) for source in range(count)]
        other = lax.ppermute(block, axis, pairs)
        low = (index // stride) % 2 == 0
        block = jnp.where(
            low, jnp.concatenate([block, other], axis=0), jnp.concatenate([other, block], axis=0)
        )
        stride *= 2
    return block


def tree_sum(value, axis):
    count = lax.axis_size(axis)
    stride = 1
    while stride < count:
        pairs = [(source, source ^ stride) for source in range(count)]
        value = value + lax.ppermute(value, axis, pairs)
        stride *= 2
    return value


def tree_scatter(value, axis):
    count = lax.axis_size(axis)
    index = lax.axis_index(axis)
    width = value.shape[1]
    parts = value.reshape(count, -1, width)
    rows = parts.shape[1]
    stride = 1
    while stride < count:
        bit = (index // stride) % 2
        paired = parts.reshape(parts.shape[0] // 2, 2, rows, width)
        keep = lax.dynamic_index_in_dim(paired, bit, axis=1, keepdims=False)
        send = lax.dynamic_index_in_dim(paired, 1 - bit, axis=1, keepdims=False)
        pairs = [(source, source ^ stride) for source in range(count)]
        parts = keep + lax.ppermute(send, axis, pairs)
        stride *= 2
    return parts.reshape(rows, width)


def partner(value, axis, stride):
    mask = 2**stride
    pairs = [(source, source ^ mask) for source in range(lax.axis_size(axis))]
    return lax.ppermute(value, axis, pairs)


def trade(piece, bit_index):
    return partner(piece, "dom", bit_index)


def widen(first_rows, second_rows):
    return (
        lax.all_gather(first_rows, "feat", axis=0, tiled=True),
        lax.all_gather(second_rows, "feat", axis=0, tiled=True),
    )


def average(pieces, neighbours, after):
    summed = gather_mean(pieces, neighbours, after)
    return summed.T.astype(jnp.bfloat16)


def source_table(local, hub_rows, send_rows):
    local_rows = local.T
    hub_local = jnp.take(local_rows, hub_rows, axis=0)
    hub_all = lax.all_gather(hub_local, "dom", axis=0, tiled=True)
    received = [
        trade(jnp.take(local_rows, send_rows[bit_index], axis=0), bit_index)
        for bit_index in range(send_rows.shape[0])
    ]
    return [local_rows, hub_all] + received


def contract(left, right):
    return lax.dot_general(
        left, right, (((1,), (1,)), ((), ())), preferred_element_type=jnp.float32
    )


def transpose_times(left, right):
    return lax.dot_general(
        left, right, (((0,), (0,)), ((), ())), preferred_element_type=jnp.float32
    )


def class_gradient(logits, labels, nodes_all):
    expd = jnp.exp(logits)
    probs = expd / jnp.sum(expd, axis=0, keepdims=True)
    classes = lax.broadcasted_iota(jnp.int32, logits.shape, 0)
    onehot = (classes == labels[None, :]).astype(jnp.float32)
    return ((probs - onehot) * (loss_scale / nodes_all)).astype(jnp.bfloat16)


def body(
    features,
    neighbours,
    hub_rows,
    send_rows,
    labels,
    inner_self,
    inner_neighbour,
    outer_self,
    outer_neighbour,
):
    rows = features.shape[1]
    nodes_all = rows * lax.axis_size("dom")
    full_input = feat_gather(features, "feat")
    mean_one = average(source_table(features, hub_rows, send_rows), neighbours, full_input)
    full_mean = lax.all_gather(mean_one, "feat", axis=0, tiled=True)
    pre_act = jnp.dot(inner_self, full_input, preferred_element_type=jnp.float32)
    pre_act = pre_act + jnp.dot(inner_neighbour, full_mean, preferred_element_type=jnp.float32)
    hidden = jnp.maximum(pre_act, 0.0).astype(jnp.bfloat16)
    mean_two = average(source_table(hidden, hub_rows, send_rows), neighbours, hidden)
    width = hidden.shape[0]
    offset = lax.axis_index("feat") * width
    self_cols = lax.dynamic_slice_in_dim(outer_self, offset, width, 1)
    neigh_cols = lax.dynamic_slice_in_dim(outer_neighbour, offset, width, 1)
    full_hidden, full_two = widen(hidden, mean_two)
    logits = jnp.dot(outer_self, full_hidden, preferred_element_type=jnp.float32)
    logits = logits + jnp.dot(outer_neighbour, full_two, preferred_element_type=jnp.float32)
    logit_grad = class_gradient(logits, labels, nodes_all)
    grad_outer_self = contract(logit_grad, hidden)
    grad_outer_neighbour = contract(logit_grad, mean_two)
    direct = transpose_times(self_cols, logit_grad)
    back_mean = transpose_times(neigh_cols, logit_grad).astype(jnp.bfloat16)
    degree = neighbours.shape[0]
    hub_count = lax.axis_size("dom") * hub_rows.shape[0]
    band = send_rows.shape[1]
    span = rows + hub_count + send_rows.shape[0] * band
    back_rows = back_mean.T.astype(jnp.float32)
    spread = scatter_mean(back_rows, neighbours, span)
    grad_rows = direct.T + spread[:rows]
    owners = lax.axis_size("dom")
    hub_parts = spread[rows : rows + hub_count].reshape(owners, hub_count // owners, width)
    hub_back = jnp.sum(
        lax.all_to_all(
            hub_parts.astype(jnp.bfloat16), "dom", split_axis=0, concat_axis=0, tiled=True
        ).astype(jnp.float32),
        axis=0,
    )
    base = rows + hub_count
    landed = [hub_back]
    for bit_index in range(send_rows.shape[0]):
        outgoing = spread[base + bit_index * band : base + (bit_index + 1) * band].astype(
            jnp.bfloat16
        )
        landed.append(trade(outgoing, bit_index).astype(jnp.float32))
    targets = jnp.concatenate([hub_rows, send_rows.reshape(-1)])
    grad_rows = land_rows(grad_rows, targets, jnp.concatenate(landed, axis=0))
    grad_hidden = grad_rows.T
    grad_pre = jnp.where(hidden > 0, grad_hidden, 0.0).astype(jnp.bfloat16)
    grad_inner_self = contract(grad_pre, full_input)
    grad_inner_neighbour = contract(grad_pre, full_mean)
    pieces = (grad_inner_self, grad_inner_neighbour, grad_outer_self, grad_outer_neighbour)
    summed = tree_sum(jnp.concatenate([piece.reshape(-1) for piece in pieces]), "dom")
    results = []
    offset = 0
    for piece in pieces:
        results.append(summed[offset : offset + piece.size].reshape(piece.shape))
        offset += piece.size
    return tuple(results)


def solution(mesh):
    return jax.shard_map(
        body,
        mesh=mesh,
        in_specs=(
            P("feat", "dom"),
            P(None, "dom"),
            P("dom"),
            P("dom", None),
            P("dom"),
            P("feat", None),
            P("feat", None),
            P(),
            P(),
        ),
        out_specs=(P("feat", None), P("feat", None), P(None, "feat"), P(None, "feat")),
        check_vma=False,
    )
```

```python
import math

import jax
import jax.numpy as jnp
from jax import lax
from jax.sharding import PartitionSpec as P

from jax.experimental import pallas as pl
from jax.experimental.pallas import tpu as pltpu

loss_scale = 4096.0


def gather_mean(pieces, neighbours, after):
    width = pieces[0].shape[1]
    degree, nodes = neighbours.shape
    size = sum(piece.shape[0] for piece in pieces)
    chunk = 512
    for piece in pieces:
        chunk = math.gcd(chunk, piece.shape[0])

    def kernel(nb_ref, *refs):
        piece_refs = refs[: len(pieces)]
        out_ref = refs[len(pieces) + 1]
        tab_ref = refs[len(pieces) + 2]
        start = 0
        for piece_ref, piece in zip(piece_refs, pieces):

            def fill(c, carry, piece_ref=piece_ref, start=start):
                r = pl.multiple_of(c * chunk, chunk)
                tab_ref[pl.ds(start + r, chunk), :] = piece_ref[pl.ds(r, chunk), :].astype(jnp.float32)
                return carry

            lax.fori_loop(0, piece.shape[0] // chunk, fill, 0)
            start += piece.shape[0]

        def body(n, carry):
            acc = tab_ref[pl.ds(nb_ref[0, n], 1), :]
            for k in range(1, degree):
                acc = acc + tab_ref[pl.ds(nb_ref[k, n], 1), :]
            out_ref[pl.ds(n, 1), :] = acc / degree
            return carry

        lax.fori_loop(0, nodes, body, 0, unroll=8)

    return pl.pallas_call(
        kernel,
        in_specs=[pl.BlockSpec(memory_space=pltpu.SMEM)]
        + [pl.BlockSpec(memory_space=pltpu.VMEM) for _ in pieces]
        + [pl.BlockSpec(memory_space=pl.ANY)],
        out_specs=pl.BlockSpec(memory_space=pltpu.VMEM),
        out_shape=jax.ShapeDtypeStruct((nodes, width), jnp.float32),
        scratch_shapes=[pltpu.VMEM((size, width), jnp.float32)],
    )(neighbours, *pieces, after)


def scatter_mean(rows, neighbours, size, chains=4):
    nodes, width = rows.shape
    degree = neighbours.shape[0]
    per_chain = degree // chains

    def kernel(nb_ref, rows_ref, out_ref, *extra_refs):
        accumulators = (out_ref,) + extra_refs
        for acc_ref in accumulators:
            acc_ref[...] = jnp.zeros_like(acc_ref)

        def step(n, carry):
            x = rows_ref[pl.ds(n, 1), :]
            for k in range(per_chain):
                for chain, acc_ref in enumerate(accumulators):
                    s = nb_ref[chain * per_chain + k, n]
                    acc_ref[pl.ds(s, 1), :] = acc_ref[pl.ds(s, 1), :] + x
            return carry

        lax.fori_loop(0, nodes, step, 0, unroll=2)
        total = out_ref[...]
        for acc_ref in extra_refs:
            total = total + acc_ref[...]
        out_ref[...] = total * (1.0 / degree)

    return pl.pallas_call(
        kernel,
        in_specs=[
            pl.BlockSpec(memory_space=pltpu.SMEM),
            pl.BlockSpec(memory_space=pltpu.VMEM),
        ],
        out_specs=pl.BlockSpec(memory_space=pltpu.VMEM),
        out_shape=jax.ShapeDtypeStruct((size, width), jnp.float32),
        scratch_shapes=[pltpu.VMEM((size, width), jnp.float32) for _ in range(chains - 1)],
        compiler_params=pltpu.CompilerParams(vmem_limit_bytes=63 * 1024 * 1024),
    )(neighbours, rows)


def feat_gather(value, axis):
    count = lax.axis_size(axis)
    index = lax.axis_index(axis)
    got = [value] + [
        lax.ppermute(value, axis, [(source, (source + shift) % count) for source in range(count)])
        for shift in range(1, count)
    ]
    stacked = jnp.stack(got[::-1] * 2)
    full = lax.dynamic_slice_in_dim(stacked, (count - 1 - index) % count, count, axis=0)
    return full.reshape(count * value.shape[0], value.shape[1])


def land_rows(base, targets, updates):
    count, width = updates.shape
    half = count // 2

    def kernel(t_ref, base_ref, upd_ref, out_ref, extra_ref):
        out_ref[...] = base_ref[...]
        extra_ref[...] = jnp.zeros_like(extra_ref)

        def step(i, carry):
            s = t_ref[i]
            t = t_ref[i + half]
            out_ref[pl.ds(s, 1), :] = out_ref[pl.ds(s, 1), :] + upd_ref[pl.ds(i, 1), :]
            extra_ref[pl.ds(t, 1), :] = extra_ref[pl.ds(t, 1), :] + upd_ref[pl.ds(i + half, 1), :]
            return carry

        lax.fori_loop(0, half, step, 0, unroll=4)
        for i in range(2 * half, count):
            s = t_ref[i]
            out_ref[pl.ds(s, 1), :] = out_ref[pl.ds(s, 1), :] + upd_ref[pl.ds(i, 1), :]
        out_ref[...] = out_ref[...] + extra_ref[...]

    return pl.pallas_call(
        kernel,
        in_specs=[
            pl.BlockSpec(memory_space=pltpu.SMEM),
            pl.BlockSpec(memory_space=pltpu.VMEM),
            pl.BlockSpec(memory_space=pltpu.VMEM),
        ],
        out_specs=pl.BlockSpec(memory_space=pltpu.VMEM),
        out_shape=jax.ShapeDtypeStruct(base.shape, jnp.float32),
        scratch_shapes=[pltpu.VMEM(base.shape, jnp.float32)],
    )(targets, base, updates)


def tree_gather(value, axis):
    count = lax.axis_size(axis)
    index = lax.axis_index(axis)
    block = value
    stride = 1
    while stride < count:
        pairs = [(source, source ^ stride) for source in range(count)]
        other = lax.ppermute(block, axis, pairs)
        low = (index // stride) % 2 == 0
        block = jnp.where(
            low, jnp.concatenate([block, other], axis=0), jnp.concatenate([other, block], axis=0)
        )
        stride *= 2
    return block


def exchange_sum(flat, axis):
    count = lax.axis_size(axis)
    length = flat.shape[0]
    padded = jnp.pad(flat, (0, (-length) % count)).reshape(count, -1)
    reduced = jnp.sum(lax.all_to_all(padded, axis, 0, 0, tiled=True), axis=0)
    spread = jnp.broadcast_to(reduced[None], (count, reduced.shape[0]))
    return lax.all_to_all(spread, axis, 0, 0, tiled=True).reshape(-1)[:length]


def tree_sum(value, axis):
    count = lax.axis_size(axis)
    stride = 1
    while stride < count:
        pairs = [(source, source ^ stride) for source in range(count)]
        value = value + lax.ppermute(value, axis, pairs)
        stride *= 2
    return value


def tree_scatter(value, axis):
    count = lax.axis_size(axis)
    index = lax.axis_index(axis)
    width = value.shape[1]
    parts = value.reshape(count, -1, width)
    rows = parts.shape[1]
    stride = 1
    while stride < count:
        bit = (index // stride) % 2
        paired = parts.reshape(parts.shape[0] // 2, 2, rows, width)
        keep = lax.dynamic_index_in_dim(paired, bit, axis=1, keepdims=False)
        send = lax.dynamic_index_in_dim(paired, 1 - bit, axis=1, keepdims=False)
        pairs = [(source, source ^ stride) for source in range(count)]
        parts = keep + lax.ppermute(send, axis, pairs)
        stride *= 2
    return parts.reshape(rows, width)


def partner(value, axis, stride):
    mask = 2**stride
    pairs = [(source, source ^ mask) for source in range(lax.axis_size(axis))]
    return lax.ppermute(value, axis, pairs)


def trade(piece, bit_index):
    return partner(piece, "dom", bit_index)


def widen(first_rows, second_rows):
    return (
        lax.all_gather(first_rows, "feat", axis=0, tiled=True),
        lax.all_gather(second_rows, "feat", axis=0, tiled=True),
    )


def average(pieces, neighbours, after):
    summed = gather_mean(pieces, neighbours, after)
    return summed.T.astype(jnp.bfloat16)


def source_table(local, hub_rows, send_rows):
    local_rows = local.T
    hub_local = jnp.take(local_rows, hub_rows, axis=0)
    hub_all = lax.all_gather(hub_local, "dom", axis=0, tiled=True)
    received = [
        trade(jnp.take(local_rows, send_rows[bit_index], axis=0), bit_index)
        for bit_index in range(send_rows.shape[0])
    ]
    return [local_rows, hub_all] + received


def contract(left, right):
    return lax.dot_general(
        left, right, (((1,), (1,)), ((), ())), preferred_element_type=jnp.float32
    )


def transpose_times(left, right):
    return lax.dot_general(
        left, right, (((0,), (0,)), ((), ())), preferred_element_type=jnp.float32
    )


def class_gradient(logits, labels, nodes_all):
    expd = jnp.exp(logits)
    probs = expd / jnp.sum(expd, axis=0, keepdims=True)
    classes = lax.broadcasted_iota(jnp.int32, logits.shape, 0)
    onehot = (classes == labels[None, :]).astype(jnp.float32)
    return ((probs - onehot) * (loss_scale / nodes_all)).astype(jnp.bfloat16)


def body(
    features,
    neighbours,
    hub_rows,
    send_rows,
    labels,
    inner_self,
    inner_neighbour,
    outer_self,
    outer_neighbour,
):
    rows = features.shape[1]
    nodes_all = rows * lax.axis_size("dom")
    full_input = feat_gather(features, "feat")
    mean_one = average(source_table(features, hub_rows, send_rows), neighbours, full_input)
    full_mean = lax.all_gather(mean_one, "feat", axis=0, tiled=True)
    pre_act = jnp.dot(inner_self, full_input, preferred_element_type=jnp.float32)
    pre_act = pre_act + jnp.dot(inner_neighbour, full_mean, preferred_element_type=jnp.float32)
    hidden = jnp.maximum(pre_act, 0.0).astype(jnp.bfloat16)
    mean_two = average(source_table(hidden, hub_rows, send_rows), neighbours, hidden)
    width = hidden.shape[0]
    offset = lax.axis_index("feat") * width
    self_cols = lax.dynamic_slice_in_dim(outer_self, offset, width, 1)
    neigh_cols = lax.dynamic_slice_in_dim(outer_neighbour, offset, width, 1)
    full_hidden, full_two = widen(hidden, mean_two)
    logits = jnp.dot(outer_self, full_hidden, preferred_element_type=jnp.float32)
    logits = logits + jnp.dot(outer_neighbour, full_two, preferred_element_type=jnp.float32)
    logit_grad = class_gradient(logits, labels, nodes_all)
    grad_outer_self = contract(logit_grad, hidden)
    grad_outer_neighbour = contract(logit_grad, mean_two)
    direct = transpose_times(self_cols, logit_grad)
    back_mean = transpose_times(neigh_cols, logit_grad).astype(jnp.bfloat16)
    degree = neighbours.shape[0]
    hub_count = lax.axis_size("dom") * hub_rows.shape[0]
    band = send_rows.shape[1]
    span = rows + hub_count + send_rows.shape[0] * band
    back_rows = back_mean.T.astype(jnp.float32)
    spread = scatter_mean(back_rows, neighbours, span)
    grad_rows = direct.T + spread[:rows]
    owners = lax.axis_size("dom")
    hub_parts = spread[rows : rows + hub_count].reshape(owners, hub_count // owners, width)
    hub_back = jnp.sum(
        lax.all_to_all(
            hub_parts.astype(jnp.bfloat16), "dom", split_axis=0, concat_axis=0, tiled=True
        ).astype(jnp.float32),
        axis=0,
    )
    base = rows + hub_count
    landed = [hub_back]
    for bit_index in range(send_rows.shape[0]):
        outgoing = spread[base + bit_index * band : base + (bit_index + 1) * band].astype(
            jnp.bfloat16
        )
        landed.append(trade(outgoing, bit_index).astype(jnp.float32))
    targets = jnp.concatenate([hub_rows, send_rows.reshape(-1)])
    grad_rows = land_rows(grad_rows, targets, jnp.concatenate(landed, axis=0))
    grad_hidden = grad_rows.T
    grad_pre = jnp.where(hidden > 0, grad_hidden, 0.0).astype(jnp.bfloat16)
    grad_inner_self = contract(grad_pre, full_input)
    grad_inner_neighbour = contract(grad_pre, full_mean)
    pieces = (grad_inner_self, grad_inner_neighbour, grad_outer_self, grad_outer_neighbour)
    summed = exchange_sum(jnp.concatenate([piece.reshape(-1) for piece in pieces]), "dom")
    results = []
    offset = 0
    for piece in pieces:
        results.append(summed[offset : offset + piece.size].reshape(piece.shape))
        offset += piece.size
    return tuple(results)


def solution(mesh):
    return jax.shard_map(
        body,
        mesh=mesh,
        in_specs=(
            P("feat", "dom"),
            P(None, "dom"),
            P("dom"),
            P("dom", None),
            P("dom"),
            P("feat", None),
            P("feat", None),
            P(),
            P(),
        ),
        out_specs=(P("feat", None), P("feat", None), P(None, "feat"), P(None, "feat")),
        check_vma=False,
    )
```

```python
import math

import jax
import jax.numpy as jnp
from jax import lax
from jax.sharding import PartitionSpec as P

from jax.experimental import pallas as pl
from jax.experimental.pallas import tpu as pltpu

loss_scale = 4096.0


def gather_mean(pieces, neighbours, after):
    width = pieces[0].shape[1]
    degree, nodes = neighbours.shape
    size = sum(piece.shape[0] for piece in pieces)
    chunk = 512
    for piece in pieces:
        chunk = math.gcd(chunk, piece.shape[0])

    def kernel(nb_ref, *refs):
        piece_refs = refs[: len(pieces)]
        out_ref = refs[len(pieces) + 1]
        tab_ref = refs[len(pieces) + 2]
        start = 0
        for piece_ref, piece in zip(piece_refs, pieces):

            def fill(c, carry, piece_ref=piece_ref, start=start):
                r = pl.multiple_of(c * chunk, chunk)
                tab_ref[pl.ds(start + r, chunk), :] = piece_ref[pl.ds(r, chunk), :].astype(jnp.float32)
                return carry

            lax.fori_loop(0, piece.shape[0] // chunk, fill, 0)
            start += piece.shape[0]

        def body(n, carry):
            acc = tab_ref[pl.ds(nb_ref[0, n], 1), :]
            for k in range(1, degree):
                acc = acc + tab_ref[pl.ds(nb_ref[k, n], 1), :]
            out_ref[pl.ds(n, 1), :] = acc / degree
            return carry

        lax.fori_loop(0, nodes, body, 0, unroll=8)

    return pl.pallas_call(
        kernel,
        in_specs=[pl.BlockSpec(memory_space=pltpu.SMEM)]
        + [pl.BlockSpec(memory_space=pltpu.VMEM) for _ in pieces]
        + [pl.BlockSpec(memory_space=pl.ANY)],
        out_specs=pl.BlockSpec(memory_space=pltpu.VMEM),
        out_shape=jax.ShapeDtypeStruct((nodes, width), jnp.float32),
        scratch_shapes=[pltpu.VMEM((size, width), jnp.float32)],
    )(neighbours, *pieces, after)


def scatter_mean(rows, neighbours, size, chains=4):
    nodes, width = rows.shape
    degree = neighbours.shape[0]
    per_chain = degree // chains

    def kernel(nb_ref, rows_ref, out_ref, *extra_refs):
        accumulators = (out_ref,) + extra_refs
        for acc_ref in accumulators:
            acc_ref[...] = jnp.zeros_like(acc_ref)

        def step(n, carry):
            x = rows_ref[pl.ds(n, 1), :]
            for k in range(per_chain):
                for chain, acc_ref in enumerate(accumulators):
                    s = nb_ref[chain * per_chain + k, n]
                    acc_ref[pl.ds(s, 1), :] = acc_ref[pl.ds(s, 1), :] + x
            return carry

        lax.fori_loop(0, nodes, step, 0, unroll=2)
        total = out_ref[...]
        for acc_ref in extra_refs:
            total = total + acc_ref[...]
        out_ref[...] = total * (1.0 / degree)

    return pl.pallas_call(
        kernel,
        in_specs=[
            pl.BlockSpec(memory_space=pltpu.SMEM),
            pl.BlockSpec(memory_space=pltpu.VMEM),
        ],
        out_specs=pl.BlockSpec(memory_space=pltpu.VMEM),
        out_shape=jax.ShapeDtypeStruct((size, width), jnp.float32),
        scratch_shapes=[pltpu.VMEM((size, width), jnp.float32) for _ in range(chains - 1)],
        compiler_params=pltpu.CompilerParams(vmem_limit_bytes=63 * 1024 * 1024),
    )(neighbours, rows)


def feat_gather(value, axis):
    count = lax.axis_size(axis)
    index = lax.axis_index(axis)
    got = [value] + [
        lax.ppermute(value, axis, [(source, (source + shift) % count) for source in range(count)])
        for shift in range(1, count)
    ]
    stacked = jnp.stack(got[::-1] * 2)
    full = lax.dynamic_slice_in_dim(stacked, (count - 1 - index) % count, count, axis=0)
    return full.reshape(count * value.shape[0], value.shape[1])


def land_rows(base, targets, updates):
    count, width = updates.shape
    half = count // 2

    def kernel(t_ref, base_ref, upd_ref, out_ref, extra_ref):
        out_ref[...] = base_ref[...]
        extra_ref[...] = jnp.zeros_like(extra_ref)

        def step(i, carry):
            s = t_ref[i]
            t = t_ref[i + half]
            out_ref[pl.ds(s, 1), :] = out_ref[pl.ds(s, 1), :] + upd_ref[pl.ds(i, 1), :]
            extra_ref[pl.ds(t, 1), :] = extra_ref[pl.ds(t, 1), :] + upd_ref[pl.ds(i + half, 1), :]
            return carry

        lax.fori_loop(0, half, step, 0, unroll=4)
        for i in range(2 * half, count):
            s = t_ref[i]
            out_ref[pl.ds(s, 1), :] = out_ref[pl.ds(s, 1), :] + upd_ref[pl.ds(i, 1), :]
        out_ref[...] = out_ref[...] + extra_ref[...]

    return pl.pallas_call(
        kernel,
        in_specs=[
            pl.BlockSpec(memory_space=pltpu.SMEM),
            pl.BlockSpec(memory_space=pltpu.VMEM),
            pl.BlockSpec(memory_space=pltpu.VMEM),
        ],
        out_specs=pl.BlockSpec(memory_space=pltpu.VMEM),
        out_shape=jax.ShapeDtypeStruct(base.shape, jnp.float32),
        scratch_shapes=[pltpu.VMEM(base.shape, jnp.float32)],
    )(targets, base, updates)


def tree_gather(value, axis):
    count = lax.axis_size(axis)
    index = lax.axis_index(axis)
    block = value
    stride = 1
    while stride < count:
        pairs = [(source, source ^ stride) for source in range(count)]
        other = lax.ppermute(block, axis, pairs)
        low = (index // stride) % 2 == 0
        block = jnp.where(
            low, jnp.concatenate([block, other], axis=0), jnp.concatenate([other, block], axis=0)
        )
        stride *= 2
    return block


def exchange_sum(flat, axis):
    count = lax.axis_size(axis)
    length = flat.shape[0]
    padded = jnp.pad(flat, (0, (-length) % count)).reshape(count, -1)
    reduced = jnp.sum(lax.all_to_all(padded, axis, 0, 0, tiled=True), axis=0)
    spread = jnp.broadcast_to(reduced[None], (count, reduced.shape[0]))
    return lax.all_to_all(spread, axis, 0, 0, tiled=True).reshape(-1)[:length]


def tree_sum(value, axis):
    count = lax.axis_size(axis)
    stride = 1
    while stride < count:
        pairs = [(source, source ^ stride) for source in range(count)]
        value = value + lax.ppermute(value, axis, pairs)
        stride *= 2
    return value


def tree_scatter(value, axis):
    count = lax.axis_size(axis)
    index = lax.axis_index(axis)
    width = value.shape[1]
    parts = value.reshape(count, -1, width)
    rows = parts.shape[1]
    stride = 1
    while stride < count:
        bit = (index // stride) % 2
        paired = parts.reshape(parts.shape[0] // 2, 2, rows, width)
        keep = lax.dynamic_index_in_dim(paired, bit, axis=1, keepdims=False)
        send = lax.dynamic_index_in_dim(paired, 1 - bit, axis=1, keepdims=False)
        pairs = [(source, source ^ stride) for source in range(count)]
        parts = keep + lax.ppermute(send, axis, pairs)
        stride *= 2
    return parts.reshape(rows, width)


def partner(value, axis, stride):
    mask = 2**stride
    pairs = [(source, source ^ mask) for source in range(lax.axis_size(axis))]
    return lax.ppermute(value, axis, pairs)


def trade(piece, bit_index):
    return partner(piece, "dom", bit_index)


def widen(first_rows, second_rows):
    return (
        lax.all_gather(first_rows, "feat", axis=0, tiled=True),
        lax.all_gather(second_rows, "feat", axis=0, tiled=True),
    )


def average(pieces, neighbours, after):
    summed = gather_mean(pieces, neighbours, after)
    return summed.T.astype(jnp.bfloat16)


def source_table(local, hub_rows, send_rows):
    local_rows = local.T
    hub_local = jnp.take(local_rows, hub_rows, axis=0)
    owners = lax.axis_size("dom")
    hub_all = lax.all_to_all(
        jnp.broadcast_to(hub_local[None], (owners,) + hub_local.shape), "dom", 0, 0, tiled=True
    ).reshape(owners * hub_local.shape[0], hub_local.shape[1])
    received = [
        trade(jnp.take(local_rows, send_rows[bit_index], axis=0), bit_index)
        for bit_index in range(send_rows.shape[0])
    ]
    return [local_rows, hub_all] + received


def contract(left, right):
    return lax.dot_general(
        left, right, (((1,), (1,)), ((), ())), preferred_element_type=jnp.float32
    )


def transpose_times(left, right):
    return lax.dot_general(
        left, right, (((0,), (0,)), ((), ())), preferred_element_type=jnp.float32
    )


def class_gradient(logits, labels, nodes_all):
    expd = jnp.exp(logits)
    probs = expd / jnp.sum(expd, axis=0, keepdims=True)
    classes = lax.broadcasted_iota(jnp.int32, logits.shape, 0)
    onehot = (classes == labels[None, :]).astype(jnp.float32)
    return ((probs - onehot) * (loss_scale / nodes_all)).astype(jnp.bfloat16)


def body(
    features,
    neighbours,
    hub_rows,
    send_rows,
    labels,
    inner_self,
    inner_neighbour,
    outer_self,
    outer_neighbour,
):
    rows = features.shape[1]
    nodes_all = rows * lax.axis_size("dom")
    full_input = feat_gather(features, "feat")
    mean_one = average(source_table(features, hub_rows, send_rows), neighbours, full_input)
    full_mean = lax.all_gather(mean_one, "feat", axis=0, tiled=True)
    pre_act = jnp.dot(inner_self, full_input, preferred_element_type=jnp.float32)
    pre_act = pre_act + jnp.dot(inner_neighbour, full_mean, preferred_element_type=jnp.float32)
    hidden = jnp.maximum(pre_act, 0.0).astype(jnp.bfloat16)
    mean_two = average(source_table(hidden, hub_rows, send_rows), neighbours, hidden)
    width = hidden.shape[0]
    offset = lax.axis_index("feat") * width
    self_cols = lax.dynamic_slice_in_dim(outer_self, offset, width, 1)
    neigh_cols = lax.dynamic_slice_in_dim(outer_neighbour, offset, width, 1)
    full_hidden, full_two = widen(hidden, mean_two)
    logits = jnp.dot(outer_self, full_hidden, preferred_element_type=jnp.float32)
    logits = logits + jnp.dot(outer_neighbour, full_two, preferred_element_type=jnp.float32)
    logit_grad = class_gradient(logits, labels, nodes_all)
    grad_outer_self = contract(logit_grad, hidden)
    grad_outer_neighbour = contract(logit_grad, mean_two)
    direct = transpose_times(self_cols, logit_grad)
    back_mean = transpose_times(neigh_cols, logit_grad).astype(jnp.bfloat16)
    degree = neighbours.shape[0]
    hub_count = lax.axis_size("dom") * hub_rows.shape[0]
    band = send_rows.shape[1]
    span = rows + hub_count + send_rows.shape[0] * band
    back_rows = back_mean.T.astype(jnp.float32)
    spread = scatter_mean(back_rows, neighbours, span)
    grad_rows = direct.T + spread[:rows]
    owners = lax.axis_size("dom")
    hub_flat = spread[rows : rows + hub_count].astype(jnp.bfloat16)
    hub_back = jnp.sum(
        lax.all_to_all(hub_flat, "dom", 0, 0, tiled=True)
        .astype(jnp.float32)
        .reshape(owners, hub_count // owners, width),
        axis=0,
    )
    base = rows + hub_count
    landed = [hub_back]
    for bit_index in range(send_rows.shape[0]):
        outgoing = spread[base + bit_index * band : base + (bit_index + 1) * band].astype(
            jnp.bfloat16
        )
        landed.append(trade(outgoing, bit_index).astype(jnp.float32))
    targets = jnp.concatenate([hub_rows, send_rows.reshape(-1)])
    grad_rows = land_rows(grad_rows, targets, jnp.concatenate(landed, axis=0))
    grad_hidden = grad_rows.T
    grad_pre = jnp.where(hidden > 0, grad_hidden, 0.0).astype(jnp.bfloat16)
    grad_inner_self = contract(grad_pre, full_input)
    grad_inner_neighbour = contract(grad_pre, full_mean)
    pieces = (grad_inner_self, grad_inner_neighbour, grad_outer_self, grad_outer_neighbour)
    summed = exchange_sum(jnp.concatenate([piece.reshape(-1) for piece in pieces]), "dom")
    results = []
    offset = 0
    for piece in pieces:
        results.append(summed[offset : offset + piece.size].reshape(piece.shape))
        offset += piece.size
    return tuple(results)


def solution(mesh):
    return jax.shard_map(
        body,
        mesh=mesh,
        in_specs=(
            P("feat", "dom"),
            P(None, "dom"),
            P("dom"),
            P("dom", None),
            P("dom"),
            P("feat", None),
            P("feat", None),
            P(),
            P(),
        ),
        out_specs=(P("feat", None), P("feat", None), P(None, "feat"), P(None, "feat")),
        check_vma=False,
    )
```

```python
import math

import jax
import jax.numpy as jnp
from jax import lax
from jax.sharding import PartitionSpec as P

from jax.experimental import pallas as pl
from jax.experimental.pallas import tpu as pltpu

loss_scale = 4096.0


def gather_mean(pieces, neighbours, after):
    width = pieces[0].shape[1]
    degree, nodes = neighbours.shape
    size = sum(piece.shape[0] for piece in pieces)
    chunk = 512
    for piece in pieces:
        chunk = math.gcd(chunk, piece.shape[0])

    def kernel(nb_ref, *refs):
        piece_refs = refs[: len(pieces)]
        out_ref = refs[len(pieces) + 1]
        tab_ref = refs[len(pieces) + 2]
        start = 0
        for piece_ref, piece in zip(piece_refs, pieces):

            def fill(c, carry, piece_ref=piece_ref, start=start):
                r = pl.multiple_of(c * chunk, chunk)
                tab_ref[pl.ds(start + r, chunk), :] = piece_ref[pl.ds(r, chunk), :].astype(jnp.float32)
                return carry

            lax.fori_loop(0, piece.shape[0] // chunk, fill, 0)
            start += piece.shape[0]

        def body(n, carry):
            acc = tab_ref[pl.ds(nb_ref[0, n], 1), :]
            for k in range(1, degree):
                acc = acc + tab_ref[pl.ds(nb_ref[k, n], 1), :]
            out_ref[pl.ds(n, 1), :] = acc / degree
            return carry

        lax.fori_loop(0, nodes, body, 0, unroll=8)

    return pl.pallas_call(
        kernel,
        in_specs=[pl.BlockSpec(memory_space=pltpu.SMEM)]
        + [pl.BlockSpec(memory_space=pltpu.VMEM) for _ in pieces]
        + [pl.BlockSpec(memory_space=pl.ANY)],
        out_specs=pl.BlockSpec(memory_space=pltpu.VMEM),
        out_shape=jax.ShapeDtypeStruct((nodes, width), jnp.float32),
        scratch_shapes=[pltpu.VMEM((size, width), jnp.float32)],
    )(neighbours, *pieces, after)


def scatter_mean(rows, neighbours, size, chains=4):
    nodes, width = rows.shape
    degree = neighbours.shape[0]
    per_chain = degree // chains

    def kernel(nb_ref, rows_ref, out_ref, *extra_refs):
        accumulators = (out_ref,) + extra_refs
        for acc_ref in accumulators:
            acc_ref[...] = jnp.zeros_like(acc_ref)

        def step(n, carry):
            x = rows_ref[pl.ds(n, 1), :]
            for k in range(per_chain):
                for chain, acc_ref in enumerate(accumulators):
                    s = nb_ref[chain * per_chain + k, n]
                    acc_ref[pl.ds(s, 1), :] = acc_ref[pl.ds(s, 1), :] + x
            return carry

        lax.fori_loop(0, nodes, step, 0, unroll=2)
        total = out_ref[...]
        for acc_ref in extra_refs:
            total = total + acc_ref[...]
        out_ref[...] = total * (1.0 / degree)

    return pl.pallas_call(
        kernel,
        in_specs=[
            pl.BlockSpec(memory_space=pltpu.SMEM),
            pl.BlockSpec(memory_space=pltpu.VMEM),
        ],
        out_specs=pl.BlockSpec(memory_space=pltpu.VMEM),
        out_shape=jax.ShapeDtypeStruct((size, width), jnp.float32),
        scratch_shapes=[pltpu.VMEM((size, width), jnp.float32) for _ in range(chains - 1)],
        compiler_params=pltpu.CompilerParams(vmem_limit_bytes=63 * 1024 * 1024),
    )(neighbours, rows)


def spread_gather(value, axis):
    count = lax.axis_size(axis)
    copies = jnp.broadcast_to(value[None], (count,) + value.shape)
    gathered = lax.all_to_all(copies, axis, 0, 0, tiled=True)
    return gathered.reshape(count * value.shape[0], value.shape[1])


def feat_gather(value, axis):
    count = lax.axis_size(axis)
    index = lax.axis_index(axis)
    got = [value] + [
        lax.ppermute(value, axis, [(source, (source + shift) % count) for source in range(count)])
        for shift in range(1, count)
    ]
    stacked = jnp.stack(got[::-1] * 2)
    full = lax.dynamic_slice_in_dim(stacked, (count - 1 - index) % count, count, axis=0)
    return full.reshape(count * value.shape[0], value.shape[1])


def land_rows(base, targets, updates):
    count, width = updates.shape
    half = count // 2

    def kernel(t_ref, base_ref, upd_ref, out_ref, extra_ref):
        out_ref[...] = base_ref[...]
        extra_ref[...] = jnp.zeros_like(extra_ref)

        def step(i, carry):
            s = t_ref[i]
            t = t_ref[i + half]
            out_ref[pl.ds(s, 1), :] = out_ref[pl.ds(s, 1), :] + upd_ref[pl.ds(i, 1), :]
            extra_ref[pl.ds(t, 1), :] = extra_ref[pl.ds(t, 1), :] + upd_ref[pl.ds(i + half, 1), :]
            return carry

        lax.fori_loop(0, half, step, 0, unroll=4)
        for i in range(2 * half, count):
            s = t_ref[i]
            out_ref[pl.ds(s, 1), :] = out_ref[pl.ds(s, 1), :] + upd_ref[pl.ds(i, 1), :]
        out_ref[...] = out_ref[...] + extra_ref[...]

    return pl.pallas_call(
        kernel,
        in_specs=[
            pl.BlockSpec(memory_space=pltpu.SMEM),
            pl.BlockSpec(memory_space=pltpu.VMEM),
            pl.BlockSpec(memory_space=pltpu.VMEM),
        ],
        out_specs=pl.BlockSpec(memory_space=pltpu.VMEM),
        out_shape=jax.ShapeDtypeStruct(base.shape, jnp.float32),
        scratch_shapes=[pltpu.VMEM(base.shape, jnp.float32)],
    )(targets, base, updates)


def tree_gather(value, axis):
    count = lax.axis_size(axis)
    index = lax.axis_index(axis)
    block = value
    stride = 1
    while stride < count:
        pairs = [(source, source ^ stride) for source in range(count)]
        other = lax.ppermute(block, axis, pairs)
        low = (index // stride) % 2 == 0
        block = jnp.where(
            low, jnp.concatenate([block, other], axis=0), jnp.concatenate([other, block], axis=0)
        )
        stride *= 2
    return block


def exchange_sum(flat, axis):
    count = lax.axis_size(axis)
    length = flat.shape[0]
    padded = jnp.pad(flat, (0, (-length) % count)).reshape(count, -1)
    reduced = jnp.sum(lax.all_to_all(padded, axis, 0, 0, tiled=True), axis=0)
    spread = jnp.broadcast_to(reduced[None], (count, reduced.shape[0]))
    return lax.all_to_all(spread, axis, 0, 0, tiled=True).reshape(-1)[:length]


def tree_sum(value, axis):
    count = lax.axis_size(axis)
    stride = 1
    while stride < count:
        pairs = [(source, source ^ stride) for source in range(count)]
        value = value + lax.ppermute(value, axis, pairs)
        stride *= 2
    return value


def tree_scatter(value, axis):
    count = lax.axis_size(axis)
    index = lax.axis_index(axis)
    width = value.shape[1]
    parts = value.reshape(count, -1, width)
    rows = parts.shape[1]
    stride = 1
    while stride < count:
        bit = (index // stride) % 2
        paired = parts.reshape(parts.shape[0] // 2, 2, rows, width)
        keep = lax.dynamic_index_in_dim(paired, bit, axis=1, keepdims=False)
        send = lax.dynamic_index_in_dim(paired, 1 - bit, axis=1, keepdims=False)
        pairs = [(source, source ^ stride) for source in range(count)]
        parts = keep + lax.ppermute(send, axis, pairs)
        stride *= 2
    return parts.reshape(rows, width)


def partner(value, axis, stride):
    mask = 2**stride
    pairs = [(source, source ^ mask) for source in range(lax.axis_size(axis))]
    return lax.ppermute(value, axis, pairs)


def trade(piece, bit_index):
    return partner(piece, "dom", bit_index)


def widen(first_rows, second_rows):
    return (
        lax.all_gather(first_rows, "feat", axis=0, tiled=True),
        lax.all_gather(second_rows, "feat", axis=0, tiled=True),
    )


def average(pieces, neighbours, after):
    summed = gather_mean(pieces, neighbours, after)
    return summed.T.astype(jnp.bfloat16)


def source_table(local, hub_rows, send_rows):
    local_rows = local.T
    hub_local = jnp.take(local_rows, hub_rows, axis=0)
    owners = lax.axis_size("dom")
    hub_all = lax.all_to_all(
        jnp.broadcast_to(hub_local[None], (owners,) + hub_local.shape), "dom", 0, 0, tiled=True
    ).reshape(owners * hub_local.shape[0], hub_local.shape[1])
    received = [
        trade(jnp.take(local_rows, send_rows[bit_index], axis=0), bit_index)
        for bit_index in range(send_rows.shape[0])
    ]
    return [local_rows, hub_all] + received


def contract(left, right):
    return lax.dot_general(
        left, right, (((1,), (1,)), ((), ())), preferred_element_type=jnp.float32
    )


def transpose_times(left, right):
    return lax.dot_general(
        left, right, (((0,), (0,)), ((), ())), preferred_element_type=jnp.float32
    )


def class_gradient(logits, labels, nodes_all):
    expd = jnp.exp(logits)
    probs = expd / jnp.sum(expd, axis=0, keepdims=True)
    classes = lax.broadcasted_iota(jnp.int32, logits.shape, 0)
    onehot = (classes == labels[None, :]).astype(jnp.float32)
    return ((probs - onehot) * (loss_scale / nodes_all)).astype(jnp.bfloat16)


def body(
    features,
    neighbours,
    hub_rows,
    send_rows,
    labels,
    inner_self,
    inner_neighbour,
    outer_self,
    outer_neighbour,
):
    rows = features.shape[1]
    nodes_all = rows * lax.axis_size("dom")
    full_input = feat_gather(features, "feat")
    mean_one = average(source_table(features, hub_rows, send_rows), neighbours, full_input)
    full_mean = spread_gather(mean_one, "feat")
    pre_act = jnp.dot(inner_self, full_input, preferred_element_type=jnp.float32)
    pre_act = pre_act + jnp.dot(inner_neighbour, full_mean, preferred_element_type=jnp.float32)
    hidden = jnp.maximum(pre_act, 0.0).astype(jnp.bfloat16)
    mean_two = average(source_table(hidden, hub_rows, send_rows), neighbours, hidden)
    width = hidden.shape[0]
    offset = lax.axis_index("feat") * width
    self_cols = lax.dynamic_slice_in_dim(outer_self, offset, width, 1)
    neigh_cols = lax.dynamic_slice_in_dim(outer_neighbour, offset, width, 1)
    full_hidden = lax.all_gather(hidden, "feat", axis=0, tiled=True)
    full_two = spread_gather(mean_two, "feat")
    logits = jnp.dot(outer_self, full_hidden, preferred_element_type=jnp.float32)
    logits = logits + jnp.dot(outer_neighbour, full_two, preferred_element_type=jnp.float32)
    logit_grad = class_gradient(logits, labels, nodes_all)
    grad_outer_self = contract(logit_grad, hidden)
    grad_outer_neighbour = contract(logit_grad, mean_two)
    direct = transpose_times(self_cols, logit_grad)
    back_mean = transpose_times(neigh_cols, logit_grad).astype(jnp.bfloat16)
    degree = neighbours.shape[0]
    hub_count = lax.axis_size("dom") * hub_rows.shape[0]
    band = send_rows.shape[1]
    span = rows + hub_count + send_rows.shape[0] * band
    back_rows = back_mean.T.astype(jnp.float32)
    spread = scatter_mean(back_rows, neighbours, span)
    grad_rows = direct.T + spread[:rows]
    owners = lax.axis_size("dom")
    hub_flat = spread[rows : rows + hub_count].astype(jnp.bfloat16)
    hub_back = jnp.sum(
        lax.all_to_all(hub_flat, "dom", 0, 0, tiled=True)
        .astype(jnp.float32)
        .reshape(owners, hub_count // owners, width),
        axis=0,
    )
    base = rows + hub_count
    landed = [hub_back]
    for bit_index in range(send_rows.shape[0]):
        outgoing = spread[base + bit_index * band : base + (bit_index + 1) * band].astype(
            jnp.bfloat16
        )
        landed.append(trade(outgoing, bit_index).astype(jnp.float32))
    targets = jnp.concatenate([hub_rows, send_rows.reshape(-1)])
    grad_rows = land_rows(grad_rows, targets, jnp.concatenate(landed, axis=0))
    grad_hidden = grad_rows.T
    grad_pre = jnp.where(hidden > 0, grad_hidden, 0.0).astype(jnp.bfloat16)
    grad_inner_self = contract(grad_pre, full_input)
    grad_inner_neighbour = contract(grad_pre, full_mean)
    pieces = (grad_inner_self, grad_inner_neighbour, grad_outer_self, grad_outer_neighbour)
    summed = exchange_sum(jnp.concatenate([piece.reshape(-1) for piece in pieces]), "dom")
    results = []
    offset = 0
    for piece in pieces:
        results.append(summed[offset : offset + piece.size].reshape(piece.shape))
        offset += piece.size
    return tuple(results)


def solution(mesh):
    return jax.shard_map(
        body,
        mesh=mesh,
        in_specs=(
            P("feat", "dom"),
            P(None, "dom"),
            P("dom"),
            P("dom", None),
            P("dom"),
            P("feat", None),
            P("feat", None),
            P(),
            P(),
        ),
        out_specs=(P("feat", None), P("feat", None), P(None, "feat"), P(None, "feat")),
        check_vma=False,
    )
```

```python
import math

import jax
import jax.numpy as jnp
from jax import lax
from jax.sharding import PartitionSpec as P

from jax.experimental import pallas as pl
from jax.experimental.pallas import tpu as pltpu

loss_scale = 4096.0


def gather_mean(pieces, neighbours, after):
    width = pieces[0].shape[1]
    degree, nodes = neighbours.shape
    size = sum(piece.shape[0] for piece in pieces)
    chunk = 512
    for piece in pieces:
        chunk = math.gcd(chunk, piece.shape[0])

    def kernel(nb_ref, *refs):
        piece_refs = refs[: len(pieces)]
        out_ref = refs[len(pieces) + 1]
        tab_ref = refs[len(pieces) + 2]
        start = 0
        for piece_ref, piece in zip(piece_refs, pieces):

            def fill(c, carry, piece_ref=piece_ref, start=start):
                r = pl.multiple_of(c * chunk, chunk)
                tab_ref[pl.ds(start + r, chunk), :] = piece_ref[pl.ds(r, chunk), :].astype(jnp.float32)
                return carry

            lax.fori_loop(0, piece.shape[0] // chunk, fill, 0)
            start += piece.shape[0]

        def body(n, carry):
            acc = tab_ref[pl.ds(nb_ref[0, n], 1), :]
            for k in range(1, degree):
                acc = acc + tab_ref[pl.ds(nb_ref[k, n], 1), :]
            out_ref[pl.ds(n, 1), :] = acc / degree
            return carry

        lax.fori_loop(0, nodes, body, 0, unroll=8)

    return pl.pallas_call(
        kernel,
        in_specs=[pl.BlockSpec(memory_space=pltpu.SMEM)]
        + [pl.BlockSpec(memory_space=pltpu.VMEM) for _ in pieces]
        + [pl.BlockSpec(memory_space=pl.ANY)],
        out_specs=pl.BlockSpec(memory_space=pltpu.VMEM),
        out_shape=jax.ShapeDtypeStruct((nodes, width), jnp.float32),
        scratch_shapes=[pltpu.VMEM((size, width), jnp.float32)],
    )(neighbours, *pieces, after)


def scatter_mean(rows, neighbours, size, chains=4):
    nodes, width = rows.shape
    degree = neighbours.shape[0]
    per_chain = degree // chains

    def kernel(nb_ref, rows_ref, out_ref, *extra_refs):
        accumulators = (out_ref,) + extra_refs
        for acc_ref in accumulators:
            acc_ref[...] = jnp.zeros_like(acc_ref)

        def step(n, carry):
            x = rows_ref[pl.ds(n, 1), :]
            for k in range(per_chain):
                for chain, acc_ref in enumerate(accumulators):
                    s = nb_ref[chain * per_chain + k, n]
                    acc_ref[pl.ds(s, 1), :] = acc_ref[pl.ds(s, 1), :] + x
            return carry

        lax.fori_loop(0, nodes, step, 0, unroll=2)
        total = out_ref[...]
        for acc_ref in extra_refs:
            total = total + acc_ref[...]
        out_ref[...] = total * (1.0 / degree)

    return pl.pallas_call(
        kernel,
        in_specs=[
            pl.BlockSpec(memory_space=pltpu.SMEM),
            pl.BlockSpec(memory_space=pltpu.VMEM),
        ],
        out_specs=pl.BlockSpec(memory_space=pltpu.VMEM),
        out_shape=jax.ShapeDtypeStruct((size, width), jnp.float32),
        scratch_shapes=[pltpu.VMEM((size, width), jnp.float32) for _ in range(chains - 1)],
        compiler_params=pltpu.CompilerParams(vmem_limit_bytes=63 * 1024 * 1024),
    )(neighbours, rows)


def spread_gather(value, axis):
    count = lax.axis_size(axis)
    copies = jnp.broadcast_to(value[None], (count,) + value.shape)
    gathered = lax.all_to_all(copies, axis, 0, 0, tiled=True)
    return gathered.reshape(count * value.shape[0], value.shape[1])


def feat_gather(value, axis):
    count = lax.axis_size(axis)
    index = lax.axis_index(axis)
    got = [value] + [
        lax.ppermute(value, axis, [(source, (source + shift) % count) for source in range(count)])
        for shift in range(1, count)
    ]
    stacked = jnp.stack(got[::-1] * 2)
    full = lax.dynamic_slice_in_dim(stacked, (count - 1 - index) % count, count, axis=0)
    return full.reshape(count * value.shape[0], value.shape[1])


def land_rows(base, targets, updates):
    count, width = updates.shape
    half = count // 2

    def kernel(t_ref, base_ref, upd_ref, out_ref, extra_ref):
        out_ref[...] = base_ref[...]
        extra_ref[...] = jnp.zeros_like(extra_ref)

        def step(i, carry):
            s = t_ref[i]
            t = t_ref[i + half]
            out_ref[pl.ds(s, 1), :] = out_ref[pl.ds(s, 1), :] + upd_ref[pl.ds(i, 1), :]
            extra_ref[pl.ds(t, 1), :] = extra_ref[pl.ds(t, 1), :] + upd_ref[pl.ds(i + half, 1), :]
            return carry

        lax.fori_loop(0, half, step, 0, unroll=4)
        for i in range(2 * half, count):
            s = t_ref[i]
            out_ref[pl.ds(s, 1), :] = out_ref[pl.ds(s, 1), :] + upd_ref[pl.ds(i, 1), :]
        out_ref[...] = out_ref[...] + extra_ref[...]

    return pl.pallas_call(
        kernel,
        in_specs=[
            pl.BlockSpec(memory_space=pltpu.SMEM),
            pl.BlockSpec(memory_space=pltpu.VMEM),
            pl.BlockSpec(memory_space=pltpu.VMEM),
        ],
        out_specs=pl.BlockSpec(memory_space=pltpu.VMEM),
        out_shape=jax.ShapeDtypeStruct(base.shape, jnp.float32),
        scratch_shapes=[pltpu.VMEM(base.shape, jnp.float32)],
    )(targets, base, updates)


def tree_gather(value, axis):
    count = lax.axis_size(axis)
    index = lax.axis_index(axis)
    block = value
    stride = 1
    while stride < count:
        pairs = [(source, source ^ stride) for source in range(count)]
        other = lax.ppermute(block, axis, pairs)
        low = (index // stride) % 2 == 0
        block = jnp.where(
            low, jnp.concatenate([block, other], axis=0), jnp.concatenate([other, block], axis=0)
        )
        stride *= 2
    return block


def exchange_sum(flat, axis):
    count = lax.axis_size(axis)
    length = flat.shape[0]
    padded = jnp.pad(flat, (0, (-length) % count)).reshape(count, -1)
    reduced = jnp.sum(lax.all_to_all(padded, axis, 0, 0, tiled=True), axis=0)
    spread = jnp.broadcast_to(reduced[None], (count, reduced.shape[0]))
    return lax.all_to_all(spread, axis, 0, 0, tiled=True).reshape(-1)[:length]


def tree_sum(value, axis):
    count = lax.axis_size(axis)
    stride = 1
    while stride < count:
        pairs = [(source, source ^ stride) for source in range(count)]
        value = value + lax.ppermute(value, axis, pairs)
        stride *= 2
    return value


def tree_scatter(value, axis):
    count = lax.axis_size(axis)
    index = lax.axis_index(axis)
    width = value.shape[1]
    parts = value.reshape(count, -1, width)
    rows = parts.shape[1]
    stride = 1
    while stride < count:
        bit = (index // stride) % 2
        paired = parts.reshape(parts.shape[0] // 2, 2, rows, width)
        keep = lax.dynamic_index_in_dim(paired, bit, axis=1, keepdims=False)
        send = lax.dynamic_index_in_dim(paired, 1 - bit, axis=1, keepdims=False)
        pairs = [(source, source ^ stride) for source in range(count)]
        parts = keep + lax.ppermute(send, axis, pairs)
        stride *= 2
    return parts.reshape(rows, width)


def partner(value, axis, stride):
    mask = 2**stride
    pairs = [(source, source ^ mask) for source in range(lax.axis_size(axis))]
    return lax.ppermute(value, axis, pairs)


def trade(piece, bit_index):
    return partner(piece, "dom", bit_index)


def widen(first_rows, second_rows):
    return (
        lax.all_gather(first_rows, "feat", axis=0, tiled=True),
        lax.all_gather(second_rows, "feat", axis=0, tiled=True),
    )


def average(pieces, neighbours, after):
    summed = gather_mean(pieces, neighbours, after)
    return summed.T.astype(jnp.bfloat16)


def source_table(local, hub_rows, send_rows):
    local_rows = local.T
    hub_count = hub_rows.shape[0]
    band = send_rows.shape[1]
    picked = jnp.take(local_rows, jnp.concatenate([hub_rows, send_rows.reshape(-1)]), axis=0)
    hub_local = picked[:hub_count]
    owners = lax.axis_size("dom")
    hub_all = lax.all_to_all(
        jnp.broadcast_to(hub_local[None], (owners,) + hub_local.shape), "dom", 0, 0, tiled=True
    ).reshape(owners * hub_local.shape[0], hub_local.shape[1])
    received = [
        trade(picked[hub_count + bit_index * band : hub_count + (bit_index + 1) * band], bit_index)
        for bit_index in range(send_rows.shape[0])
    ]
    return [local_rows, hub_all] + received


def contract(left, right):
    return lax.dot_general(
        left, right, (((1,), (1,)), ((), ())), preferred_element_type=jnp.float32
    )


def transpose_times(left, right):
    return lax.dot_general(
        left, right, (((0,), (0,)), ((), ())), preferred_element_type=jnp.float32
    )


def class_gradient(logits, labels, nodes_all):
    expd = jnp.exp(logits)
    probs = expd / jnp.sum(expd, axis=0, keepdims=True)
    classes = lax.broadcasted_iota(jnp.int32, logits.shape, 0)
    onehot = (classes == labels[None, :]).astype(jnp.float32)
    return ((probs - onehot) * (loss_scale / nodes_all)).astype(jnp.bfloat16)


def body(
    features,
    neighbours,
    hub_rows,
    send_rows,
    labels,
    inner_self,
    inner_neighbour,
    outer_self,
    outer_neighbour,
):
    rows = features.shape[1]
    nodes_all = rows * lax.axis_size("dom")
    full_input = feat_gather(features, "feat")
    mean_one = average(source_table(features, hub_rows, send_rows), neighbours, full_input)
    full_mean = spread_gather(mean_one, "feat")
    pre_act = jnp.dot(inner_self, full_input, preferred_element_type=jnp.float32)
    pre_act = pre_act + jnp.dot(inner_neighbour, full_mean, preferred_element_type=jnp.float32)
    hidden = jnp.maximum(pre_act, 0.0).astype(jnp.bfloat16)
    mean_two = average(source_table(hidden, hub_rows, send_rows), neighbours, hidden)
    width = hidden.shape[0]
    offset = lax.axis_index("feat") * width
    self_cols = lax.dynamic_slice_in_dim(outer_self, offset, width, 1)
    neigh_cols = lax.dynamic_slice_in_dim(outer_neighbour, offset, width, 1)
    full_hidden = lax.all_gather(hidden, "feat", axis=0, tiled=True)
    full_two = spread_gather(mean_two, "feat")
    logits = jnp.dot(outer_self, full_hidden, preferred_element_type=jnp.float32)
    logits = logits + jnp.dot(outer_neighbour, full_two, preferred_element_type=jnp.float32)
    logit_grad = class_gradient(logits, labels, nodes_all)
    grad_outer_self = contract(logit_grad, hidden)
    grad_outer_neighbour = contract(logit_grad, mean_two)
    direct = transpose_times(self_cols, logit_grad)
    back_mean = transpose_times(neigh_cols, logit_grad).astype(jnp.bfloat16)
    degree = neighbours.shape[0]
    hub_count = lax.axis_size("dom") * hub_rows.shape[0]
    band = send_rows.shape[1]
    span = rows + hub_count + send_rows.shape[0] * band
    back_rows = back_mean.T.astype(jnp.float32)
    spread = scatter_mean(back_rows, neighbours, span)
    grad_rows = direct.T + spread[:rows]
    owners = lax.axis_size("dom")
    hub_flat = spread[rows : rows + hub_count].astype(jnp.bfloat16)
    hub_back = jnp.sum(
        lax.all_to_all(hub_flat, "dom", 0, 0, tiled=True)
        .astype(jnp.float32)
        .reshape(owners, hub_count // owners, width),
        axis=0,
    )
    base = rows + hub_count
    landed = [hub_back]
    for bit_index in range(send_rows.shape[0]):
        outgoing = spread[base + bit_index * band : base + (bit_index + 1) * band].astype(
            jnp.bfloat16
        )
        landed.append(trade(outgoing, bit_index).astype(jnp.float32))
    targets = jnp.concatenate([hub_rows, send_rows.reshape(-1)])
    grad_rows = land_rows(grad_rows, targets, jnp.concatenate(landed, axis=0))
    grad_hidden = grad_rows.T
    grad_pre = jnp.where(hidden > 0, grad_hidden, 0.0).astype(jnp.bfloat16)
    grad_inner_self = contract(grad_pre, full_input)
    grad_inner_neighbour = contract(grad_pre, full_mean)
    pieces = (grad_inner_self, grad_inner_neighbour, grad_outer_self, grad_outer_neighbour)
    summed = exchange_sum(jnp.concatenate([piece.reshape(-1) for piece in pieces]), "dom")
    results = []
    offset = 0
    for piece in pieces:
        results.append(summed[offset : offset + piece.size].reshape(piece.shape))
        offset += piece.size
    return tuple(results)


def solution(mesh):
    return jax.shard_map(
        body,
        mesh=mesh,
        in_specs=(
            P("feat", "dom"),
            P(None, "dom"),
            P("dom"),
            P("dom", None),
            P("dom"),
            P("feat", None),
            P("feat", None),
            P(),
            P(),
        ),
        out_specs=(P("feat", None), P("feat", None), P(None, "feat"), P(None, "feat")),
        check_vma=False,
    )
```

```python
import math

import jax
import jax.numpy as jnp
from jax import lax
from jax.sharding import PartitionSpec as P

from jax.experimental import pallas as pl
from jax.experimental.pallas import tpu as pltpu

loss_scale = 4096.0


def gather_mean(pieces, neighbours, after):
    width = pieces[0].shape[1]
    degree, nodes = neighbours.shape
    size = sum(piece.shape[0] for piece in pieces)
    chunk = 512
    for piece in pieces:
        chunk = math.gcd(chunk, piece.shape[0])

    def kernel(nb_ref, *refs):
        piece_refs = refs[: len(pieces)]
        out_ref = refs[len(pieces) + 1]
        tab_ref = refs[len(pieces) + 2]
        start = 0
        for piece_ref, piece in zip(piece_refs, pieces):

            def fill(c, carry, piece_ref=piece_ref, start=start):
                r = pl.multiple_of(c * chunk, chunk)
                tab_ref[pl.ds(start + r, chunk), :] = piece_ref[pl.ds(r, chunk), :].astype(jnp.float32)
                return carry

            lax.fori_loop(0, piece.shape[0] // chunk, fill, 0)
            start += piece.shape[0]

        def body(n, carry):
            acc = tab_ref[pl.ds(nb_ref[0, n], 1), :]
            for k in range(1, degree):
                acc = acc + tab_ref[pl.ds(nb_ref[k, n], 1), :]
            out_ref[pl.ds(n, 1), :] = acc / degree
            return carry

        lax.fori_loop(0, nodes, body, 0, unroll=8)

    return pl.pallas_call(
        kernel,
        in_specs=[pl.BlockSpec(memory_space=pltpu.SMEM)]
        + [pl.BlockSpec(memory_space=pltpu.VMEM) for _ in pieces]
        + [pl.BlockSpec(memory_space=pl.ANY)],
        out_specs=pl.BlockSpec(memory_space=pltpu.VMEM),
        out_shape=jax.ShapeDtypeStruct((nodes, width), jnp.float32),
        scratch_shapes=[pltpu.VMEM((size, width), jnp.float32)],
    )(neighbours, *pieces, after)


def scatter_mean(rows, neighbours, size):
    nodes, width = rows.shape
    degree = neighbours.shape[0]
    pack = 128 // width
    lanes = pack * width
    doubled = jnp.concatenate([rows] * pack, axis=1)

    def kernel(nb_ref, rows_ref, out_ref, *extra_refs):
        accumulators = (out_ref,) + extra_refs
        for acc_ref in accumulators:
            acc_ref[...] = jnp.zeros_like(acc_ref)
        part = lax.broadcasted_iota(jnp.int32, (1, lanes), 1) // width

        def step(n, carry):
            x = rows_ref[pl.ds(n, 1), :]
            for k, acc_ref in enumerate(accumulators):
                s = nb_ref[k, n]
                row = s // pack
                placed = jnp.where(part == s % pack, x, 0.0)
                acc_ref[pl.ds(row, 1), :] = acc_ref[pl.ds(row, 1), :] + placed
            return carry

        lax.fori_loop(0, nodes, step, 0, unroll=2)
        total = out_ref[...]
        for acc_ref in extra_refs:
            total = total + acc_ref[...]
        out_ref[...] = total * (1.0 / degree)

    packed = pl.pallas_call(
        kernel,
        in_specs=[
            pl.BlockSpec(memory_space=pltpu.SMEM),
            pl.BlockSpec(memory_space=pltpu.VMEM),
        ],
        out_specs=pl.BlockSpec(memory_space=pltpu.VMEM),
        out_shape=jax.ShapeDtypeStruct((size // pack, lanes), jnp.float32),
        scratch_shapes=[pltpu.VMEM((size // pack, lanes), jnp.float32) for _ in range(degree - 1)],
        compiler_params=pltpu.CompilerParams(vmem_limit_bytes=63 * 1024 * 1024),
    )(neighbours, doubled)
    return packed.reshape(size, width)


def spread_gather(value, axis):
    count = lax.axis_size(axis)
    copies = jnp.broadcast_to(value[None], (count,) + value.shape)
    gathered = lax.all_to_all(copies, axis, 0, 0, tiled=True)
    return gathered.reshape(count * value.shape[0], value.shape[1])


def feat_gather(value, axis):
    count = lax.axis_size(axis)
    index = lax.axis_index(axis)
    got = [value] + [
        lax.ppermute(value, axis, [(source, (source + shift) % count) for source in range(count)])
        for shift in range(1, count)
    ]
    stacked = jnp.stack(got[::-1] * 2)
    full = lax.dynamic_slice_in_dim(stacked, (count - 1 - index) % count, count, axis=0)
    return full.reshape(count * value.shape[0], value.shape[1])


def land_rows(base, targets, updates):
    count, width = updates.shape
    half = count // 2

    def kernel(t_ref, base_ref, upd_ref, out_ref, extra_ref):
        out_ref[...] = base_ref[...]
        extra_ref[...] = jnp.zeros_like(extra_ref)

        def step(i, carry):
            s = t_ref[i]
            t = t_ref[i + half]
            out_ref[pl.ds(s, 1), :] = out_ref[pl.ds(s, 1), :] + upd_ref[pl.ds(i, 1), :]
            extra_ref[pl.ds(t, 1), :] = extra_ref[pl.ds(t, 1), :] + upd_ref[pl.ds(i + half, 1), :]
            return carry

        lax.fori_loop(0, half, step, 0, unroll=4)
        for i in range(2 * half, count):
            s = t_ref[i]
            out_ref[pl.ds(s, 1), :] = out_ref[pl.ds(s, 1), :] + upd_ref[pl.ds(i, 1), :]
        out_ref[...] = out_ref[...] + extra_ref[...]

    return pl.pallas_call(
        kernel,
        in_specs=[
            pl.BlockSpec(memory_space=pltpu.SMEM),
            pl.BlockSpec(memory_space=pltpu.VMEM),
            pl.BlockSpec(memory_space=pltpu.VMEM),
        ],
        out_specs=pl.BlockSpec(memory_space=pltpu.VMEM),
        out_shape=jax.ShapeDtypeStruct(base.shape, jnp.float32),
        scratch_shapes=[pltpu.VMEM(base.shape, jnp.float32)],
    )(targets, base, updates)


def tree_gather(value, axis):
    count = lax.axis_size(axis)
    index = lax.axis_index(axis)
    block = value
    stride = 1
    while stride < count:
        pairs = [(source, source ^ stride) for source in range(count)]
        other = lax.ppermute(block, axis, pairs)
        low = (index // stride) % 2 == 0
        block = jnp.where(
            low, jnp.concatenate([block, other], axis=0), jnp.concatenate([other, block], axis=0)
        )
        stride *= 2
    return block


def exchange_sum(flat, axis):
    count = lax.axis_size(axis)
    length = flat.shape[0]
    padded = jnp.pad(flat, (0, (-length) % count)).reshape(count, -1)
    reduced = jnp.sum(lax.all_to_all(padded, axis, 0, 0, tiled=True), axis=0)
    spread = jnp.broadcast_to(reduced[None], (count, reduced.shape[0]))
    return lax.all_to_all(spread, axis, 0, 0, tiled=True).reshape(-1)[:length]


def tree_sum(value, axis):
    count = lax.axis_size(axis)
    stride = 1
    while stride < count:
        pairs = [(source, source ^ stride) for source in range(count)]
        value = value + lax.ppermute(value, axis, pairs)
        stride *= 2
    return value


def tree_scatter(value, axis):
    count = lax.axis_size(axis)
    index = lax.axis_index(axis)
    width = value.shape[1]
    parts = value.reshape(count, -1, width)
    rows = parts.shape[1]
    stride = 1
    while stride < count:
        bit = (index // stride) % 2
        paired = parts.reshape(parts.shape[0] // 2, 2, rows, width)
        keep = lax.dynamic_index_in_dim(paired, bit, axis=1, keepdims=False)
        send = lax.dynamic_index_in_dim(paired, 1 - bit, axis=1, keepdims=False)
        pairs = [(source, source ^ stride) for source in range(count)]
        parts = keep + lax.ppermute(send, axis, pairs)
        stride *= 2
    return parts.reshape(rows, width)


def partner(value, axis, stride):
    mask = 2**stride
    pairs = [(source, source ^ mask) for source in range(lax.axis_size(axis))]
    return lax.ppermute(value, axis, pairs)


def trade(piece, bit_index):
    return partner(piece, "dom", bit_index)


def widen(first_rows, second_rows):
    return (
        lax.all_gather(first_rows, "feat", axis=0, tiled=True),
        lax.all_gather(second_rows, "feat", axis=0, tiled=True),
    )


def average(pieces, neighbours, after):
    summed = gather_mean(pieces, neighbours, after)
    return summed.T.astype(jnp.bfloat16)


def source_table(local, hub_rows, send_rows):
    local_rows = local.T
    hub_local = jnp.take(local_rows, hub_rows, axis=0)
    owners = lax.axis_size("dom")
    hub_all = lax.all_to_all(
        jnp.broadcast_to(hub_local[None], (owners,) + hub_local.shape), "dom", 0, 0, tiled=True
    ).reshape(owners * hub_local.shape[0], hub_local.shape[1])
    received = [
        trade(jnp.take(local_rows, send_rows[bit_index], axis=0), bit_index)
        for bit_index in range(send_rows.shape[0])
    ]
    return [local_rows, hub_all] + received


def contract(left, right):
    return lax.dot_general(
        left, right, (((1,), (1,)), ((), ())), preferred_element_type=jnp.float32
    )


def transpose_times(left, right):
    return lax.dot_general(
        left, right, (((0,), (0,)), ((), ())), preferred_element_type=jnp.float32
    )


def class_gradient(logits, labels, nodes_all):
    expd = jnp.exp(logits)
    probs = expd / jnp.sum(expd, axis=0, keepdims=True)
    classes = lax.broadcasted_iota(jnp.int32, logits.shape, 0)
    onehot = (classes == labels[None, :]).astype(jnp.float32)
    return ((probs - onehot) * (loss_scale / nodes_all)).astype(jnp.bfloat16)


def body(
    features,
    neighbours,
    hub_rows,
    send_rows,
    labels,
    inner_self,
    inner_neighbour,
    outer_self,
    outer_neighbour,
):
    rows = features.shape[1]
    nodes_all = rows * lax.axis_size("dom")
    full_input = feat_gather(features, "feat")
    mean_one = average(source_table(features, hub_rows, send_rows), neighbours, full_input)
    full_mean = spread_gather(mean_one, "feat")
    pre_act = jnp.dot(inner_self, full_input, preferred_element_type=jnp.float32)
    pre_act = pre_act + jnp.dot(inner_neighbour, full_mean, preferred_element_type=jnp.float32)
    hidden = jnp.maximum(pre_act, 0.0).astype(jnp.bfloat16)
    mean_two = average(source_table(hidden, hub_rows, send_rows), neighbours, hidden)
    width = hidden.shape[0]
    offset = lax.axis_index("feat") * width
    self_cols = lax.dynamic_slice_in_dim(outer_self, offset, width, 1)
    neigh_cols = lax.dynamic_slice_in_dim(outer_neighbour, offset, width, 1)
    full_hidden = lax.all_gather(hidden, "feat", axis=0, tiled=True)
    full_two = spread_gather(mean_two, "feat")
    logits = jnp.dot(outer_self, full_hidden, preferred_element_type=jnp.float32)
    logits = logits + jnp.dot(outer_neighbour, full_two, preferred_element_type=jnp.float32)
    logit_grad = class_gradient(logits, labels, nodes_all)
    grad_outer_self = contract(logit_grad, hidden)
    grad_outer_neighbour = contract(logit_grad, mean_two)
    direct = transpose_times(self_cols, logit_grad)
    back_mean = transpose_times(neigh_cols, logit_grad).astype(jnp.bfloat16)
    degree = neighbours.shape[0]
    hub_count = lax.axis_size("dom") * hub_rows.shape[0]
    band = send_rows.shape[1]
    span = rows + hub_count + send_rows.shape[0] * band
    back_rows = back_mean.T.astype(jnp.float32)
    spread = scatter_mean(back_rows, neighbours, span)
    grad_rows = direct.T + spread[:rows]
    owners = lax.axis_size("dom")
    hub_flat = spread[rows : rows + hub_count].astype(jnp.bfloat16)
    hub_back = jnp.sum(
        lax.all_to_all(hub_flat, "dom", 0, 0, tiled=True)
        .astype(jnp.float32)
        .reshape(owners, hub_count // owners, width),
        axis=0,
    )
    base = rows + hub_count
    landed = [hub_back]
    for bit_index in range(send_rows.shape[0]):
        outgoing = spread[base + bit_index * band : base + (bit_index + 1) * band].astype(
            jnp.bfloat16
        )
        landed.append(trade(outgoing, bit_index).astype(jnp.float32))
    targets = jnp.concatenate([hub_rows, send_rows.reshape(-1)])
    grad_rows = land_rows(grad_rows, targets, jnp.concatenate(landed, axis=0))
    grad_hidden = grad_rows.T
    grad_pre = jnp.where(hidden > 0, grad_hidden, 0.0).astype(jnp.bfloat16)
    grad_inner_self = contract(grad_pre, full_input)
    grad_inner_neighbour = contract(grad_pre, full_mean)
    pieces = (grad_inner_self, grad_inner_neighbour, grad_outer_self, grad_outer_neighbour)
    summed = exchange_sum(jnp.concatenate([piece.reshape(-1) for piece in pieces]), "dom")
    results = []
    offset = 0
    for piece in pieces:
        results.append(summed[offset : offset + piece.size].reshape(piece.shape))
        offset += piece.size
    return tuple(results)


def solution(mesh):
    return jax.shard_map(
        body,
        mesh=mesh,
        in_specs=(
            P("feat", "dom"),
            P(None, "dom"),
            P("dom"),
            P("dom", None),
            P("dom"),
            P("feat", None),
            P("feat", None),
            P(),
            P(),
        ),
        out_specs=(P("feat", None), P("feat", None), P(None, "feat"), P(None, "feat")),
        check_vma=False,
    )
```

```python
import math

import jax
import jax.numpy as jnp
from jax import lax
from jax.sharding import PartitionSpec as P

from jax.experimental import pallas as pl
from jax.experimental.pallas import tpu as pltpu

loss_scale = 4096.0


def gather_mean(pieces, neighbours, after):
    width = pieces[0].shape[1]
    degree, nodes = neighbours.shape
    size = sum(piece.shape[0] for piece in pieces)
    chunk = 512
    for piece in pieces:
        chunk = math.gcd(chunk, piece.shape[0])

    def kernel(nb_ref, *refs):
        piece_refs = refs[: len(pieces)]
        out_ref = refs[len(pieces) + 1]
        tab_ref = refs[len(pieces) + 2]
        start = 0
        for piece_ref, piece in zip(piece_refs, pieces):

            def fill(c, carry, piece_ref=piece_ref, start=start):
                r = pl.multiple_of(c * chunk, chunk)
                tab_ref[pl.ds(start + r, chunk), :] = piece_ref[pl.ds(r, chunk), :].astype(jnp.float32)
                return carry

            lax.fori_loop(0, piece.shape[0] // chunk, fill, 0)
            start += piece.shape[0]

        def body(n, carry):
            acc = tab_ref[pl.ds(nb_ref[0, n], 1), :]
            for k in range(1, degree):
                acc = acc + tab_ref[pl.ds(nb_ref[k, n], 1), :]
            out_ref[pl.ds(n, 1), :] = acc / degree
            return carry

        lax.fori_loop(0, nodes, body, 0, unroll=16)

    return pl.pallas_call(
        kernel,
        in_specs=[pl.BlockSpec(memory_space=pltpu.SMEM)]
        + [pl.BlockSpec(memory_space=pltpu.VMEM) for _ in pieces]
        + [pl.BlockSpec(memory_space=pl.ANY)],
        out_specs=pl.BlockSpec(memory_space=pltpu.VMEM),
        out_shape=jax.ShapeDtypeStruct((nodes, width), jnp.float32),
        scratch_shapes=[pltpu.VMEM((size, width), jnp.float32)],
    )(neighbours, *pieces, after)


def scatter_mean(rows, neighbours, size, chains=4):
    nodes, width = rows.shape
    degree = neighbours.shape[0]
    per_chain = degree // chains

    def kernel(nb_ref, rows_ref, out_ref, *extra_refs):
        accumulators = (out_ref,) + extra_refs
        for acc_ref in accumulators:
            acc_ref[...] = jnp.zeros_like(acc_ref)

        def step(n, carry):
            x = rows_ref[pl.ds(n, 1), :]
            for k in range(per_chain):
                for chain, acc_ref in enumerate(accumulators):
                    s = nb_ref[chain * per_chain + k, n]
                    acc_ref[pl.ds(s, 1), :] = acc_ref[pl.ds(s, 1), :] + x
            return carry

        lax.fori_loop(0, nodes, step, 0, unroll=2)
        total = out_ref[...]
        for acc_ref in extra_refs:
            total = total + acc_ref[...]
        out_ref[...] = total * (1.0 / degree)

    return pl.pallas_call(
        kernel,
        in_specs=[
            pl.BlockSpec(memory_space=pltpu.SMEM),
            pl.BlockSpec(memory_space=pltpu.VMEM),
        ],
        out_specs=pl.BlockSpec(memory_space=pltpu.VMEM),
        out_shape=jax.ShapeDtypeStruct((size, width), jnp.float32),
        scratch_shapes=[pltpu.VMEM((size, width), jnp.float32) for _ in range(chains - 1)],
        compiler_params=pltpu.CompilerParams(vmem_limit_bytes=63 * 1024 * 1024),
    )(neighbours, rows)


def spread_gather(value, axis):
    count = lax.axis_size(axis)
    copies = jnp.broadcast_to(value[None], (count,) + value.shape)
    gathered = lax.all_to_all(copies, axis, 0, 0, tiled=True)
    return gathered.reshape(count * value.shape[0], value.shape[1])


def feat_gather(value, axis):
    count = lax.axis_size(axis)
    index = lax.axis_index(axis)
    got = [value] + [
        lax.ppermute(value, axis, [(source, (source + shift) % count) for source in range(count)])
        for shift in range(1, count)
    ]
    stacked = jnp.stack(got[::-1] * 2)
    full = lax.dynamic_slice_in_dim(stacked, (count - 1 - index) % count, count, axis=0)
    return full.reshape(count * value.shape[0], value.shape[1])


def land_rows(base, targets, updates):
    count, width = updates.shape
    half = count // 2

    def kernel(t_ref, base_ref, upd_ref, out_ref, extra_ref):
        out_ref[...] = base_ref[...]
        extra_ref[...] = jnp.zeros_like(extra_ref)

        def step(i, carry):
            s = t_ref[i]
            t = t_ref[i + half]
            out_ref[pl.ds(s, 1), :] = out_ref[pl.ds(s, 1), :] + upd_ref[pl.ds(i, 1), :]
            extra_ref[pl.ds(t, 1), :] = extra_ref[pl.ds(t, 1), :] + upd_ref[pl.ds(i + half, 1), :]
            return carry

        lax.fori_loop(0, half, step, 0, unroll=4)
        for i in range(2 * half, count):
            s = t_ref[i]
            out_ref[pl.ds(s, 1), :] = out_ref[pl.ds(s, 1), :] + upd_ref[pl.ds(i, 1), :]
        out_ref[...] = out_ref[...] + extra_ref[...]

    return pl.pallas_call(
        kernel,
        in_specs=[
            pl.BlockSpec(memory_space=pltpu.SMEM),
            pl.BlockSpec(memory_space=pltpu.VMEM),
            pl.BlockSpec(memory_space=pltpu.VMEM),
        ],
        out_specs=pl.BlockSpec(memory_space=pltpu.VMEM),
        out_shape=jax.ShapeDtypeStruct(base.shape, jnp.float32),
        scratch_shapes=[pltpu.VMEM(base.shape, jnp.float32)],
    )(targets, base, updates)


def tree_gather(value, axis):
    count = lax.axis_size(axis)
    index = lax.axis_index(axis)
    block = value
    stride = 1
    while stride < count:
        pairs = [(source, source ^ stride) for source in range(count)]
        other = lax.ppermute(block, axis, pairs)
        low = (index // stride) % 2 == 0
        block = jnp.where(
            low, jnp.concatenate([block, other], axis=0), jnp.concatenate([other, block], axis=0)
        )
        stride *= 2
    return block


def exchange_sum(flat, axis):
    count = lax.axis_size(axis)
    length = flat.shape[0]
    padded = jnp.pad(flat, (0, (-length) % count)).reshape(count, -1)
    reduced = jnp.sum(lax.all_to_all(padded, axis, 0, 0, tiled=True), axis=0)
    spread = jnp.broadcast_to(reduced[None], (count, reduced.shape[0]))
    return lax.all_to_all(spread, axis, 0, 0, tiled=True).reshape(-1)[:length]


def tree_sum(value, axis):
    count = lax.axis_size(axis)
    stride = 1
    while stride < count:
        pairs = [(source, source ^ stride) for source in range(count)]
        value = value + lax.ppermute(value, axis, pairs)
        stride *= 2
    return value


def tree_scatter(value, axis):
    count = lax.axis_size(axis)
    index = lax.axis_index(axis)
    width = value.shape[1]
    parts = value.reshape(count, -1, width)
    rows = parts.shape[1]
    stride = 1
    while stride < count:
        bit = (index // stride) % 2
        paired = parts.reshape(parts.shape[0] // 2, 2, rows, width)
        keep = lax.dynamic_index_in_dim(paired, bit, axis=1, keepdims=False)
        send = lax.dynamic_index_in_dim(paired, 1 - bit, axis=1, keepdims=False)
        pairs = [(source, source ^ stride) for source in range(count)]
        parts = keep + lax.ppermute(send, axis, pairs)
        stride *= 2
    return parts.reshape(rows, width)


def partner(value, axis, stride):
    mask = 2**stride
    pairs = [(source, source ^ mask) for source in range(lax.axis_size(axis))]
    return lax.ppermute(value, axis, pairs)


def trade(piece, bit_index):
    return partner(piece, "dom", bit_index)


def widen(first_rows, second_rows):
    return (
        lax.all_gather(first_rows, "feat", axis=0, tiled=True),
        lax.all_gather(second_rows, "feat", axis=0, tiled=True),
    )


def average(pieces, neighbours, after):
    summed = gather_mean(pieces, neighbours, after)
    return summed.T.astype(jnp.bfloat16)


def source_table(local, hub_rows, send_rows):
    local_rows = local.T
    hub_local = jnp.take(local_rows, hub_rows, axis=0)
    owners = lax.axis_size("dom")
    hub_all = lax.all_to_all(
        jnp.broadcast_to(hub_local[None], (owners,) + hub_local.shape), "dom", 0, 0, tiled=True
    ).reshape(owners * hub_local.shape[0], hub_local.shape[1])
    received = [
        trade(jnp.take(local_rows, send_rows[bit_index], axis=0), bit_index)
        for bit_index in range(send_rows.shape[0])
    ]
    return [local_rows, hub_all] + received


def contract(left, right):
    return lax.dot_general(
        left, right, (((1,), (1,)), ((), ())), preferred_element_type=jnp.float32
    )


def transpose_times(left, right):
    return lax.dot_general(
        left, right, (((0,), (0,)), ((), ())), preferred_element_type=jnp.float32
    )


def class_gradient(logits, labels, nodes_all):
    expd = jnp.exp(logits)
    probs = expd / jnp.sum(expd, axis=0, keepdims=True)
    classes = lax.broadcasted_iota(jnp.int32, logits.shape, 0)
    onehot = (classes == labels[None, :]).astype(jnp.float32)
    return ((probs - onehot) * (loss_scale / nodes_all)).astype(jnp.bfloat16)


def body(
    features,
    neighbours,
    hub_rows,
    send_rows,
    labels,
    inner_self,
    inner_neighbour,
    outer_self,
    outer_neighbour,
):
    rows = features.shape[1]
    nodes_all = rows * lax.axis_size("dom")
    full_input = feat_gather(features, "feat")
    mean_one = average(source_table(features, hub_rows, send_rows), neighbours, full_input)
    full_mean = spread_gather(mean_one, "feat")
    pre_act = jnp.dot(inner_self, full_input, preferred_element_type=jnp.float32)
    pre_act = pre_act + jnp.dot(inner_neighbour, full_mean, preferred_element_type=jnp.float32)
    hidden = jnp.maximum(pre_act, 0.0).astype(jnp.bfloat16)
    mean_two = average(source_table(hidden, hub_rows, send_rows), neighbours, hidden)
    width = hidden.shape[0]
    offset = lax.axis_index("feat") * width
    self_cols = lax.dynamic_slice_in_dim(outer_self, offset, width, 1)
    neigh_cols = lax.dynamic_slice_in_dim(outer_neighbour, offset, width, 1)
    full_hidden = lax.all_gather(hidden, "feat", axis=0, tiled=True)
    full_two = spread_gather(mean_two, "feat")
    logits = jnp.dot(outer_self, full_hidden, preferred_element_type=jnp.float32)
    logits = logits + jnp.dot(outer_neighbour, full_two, preferred_element_type=jnp.float32)
    logit_grad = class_gradient(logits, labels, nodes_all)
    grad_outer_self = contract(logit_grad, hidden)
    grad_outer_neighbour = contract(logit_grad, mean_two)
    direct = transpose_times(self_cols, logit_grad)
    back_mean = transpose_times(neigh_cols, logit_grad).astype(jnp.bfloat16)
    degree = neighbours.shape[0]
    hub_count = lax.axis_size("dom") * hub_rows.shape[0]
    band = send_rows.shape[1]
    span = rows + hub_count + send_rows.shape[0] * band
    back_rows = back_mean.T.astype(jnp.float32)
    spread = scatter_mean(back_rows, neighbours, span)
    grad_rows = direct.T + spread[:rows]
    owners = lax.axis_size("dom")
    hub_flat = spread[rows : rows + hub_count].astype(jnp.bfloat16)
    hub_back = jnp.sum(
        lax.all_to_all(hub_flat, "dom", 0, 0, tiled=True)
        .astype(jnp.float32)
        .reshape(owners, hub_count // owners, width),
        axis=0,
    )
    base = rows + hub_count
    landed = [hub_back]
    for bit_index in range(send_rows.shape[0]):
        outgoing = spread[base + bit_index * band : base + (bit_index + 1) * band].astype(
            jnp.bfloat16
        )
        landed.append(trade(outgoing, bit_index).astype(jnp.float32))
    targets = jnp.concatenate([hub_rows, send_rows.reshape(-1)])
    grad_rows = land_rows(grad_rows, targets, jnp.concatenate(landed, axis=0))
    grad_hidden = grad_rows.T
    grad_pre = jnp.where(hidden > 0, grad_hidden, 0.0).astype(jnp.bfloat16)
    grad_inner_self = contract(grad_pre, full_input)
    grad_inner_neighbour = contract(grad_pre, full_mean)
    pieces = (grad_inner_self, grad_inner_neighbour, grad_outer_self, grad_outer_neighbour)
    summed = exchange_sum(jnp.concatenate([piece.reshape(-1) for piece in pieces]), "dom")
    results = []
    offset = 0
    for piece in pieces:
        results.append(summed[offset : offset + piece.size].reshape(piece.shape))
        offset += piece.size
    return tuple(results)


def solution(mesh):
    return jax.shard_map(
        body,
        mesh=mesh,
        in_specs=(
            P("feat", "dom"),
            P(None, "dom"),
            P("dom"),
            P("dom", None),
            P("dom"),
            P("feat", None),
            P("feat", None),
            P(),
            P(),
        ),
        out_specs=(P("feat", None), P("feat", None), P(None, "feat"), P(None, "feat")),
        check_vma=False,
    )
```

```python
import math

import jax
import jax.numpy as jnp
from jax import lax
from jax.sharding import PartitionSpec as P

from jax.experimental import pallas as pl
from jax.experimental.pallas import tpu as pltpu

loss_scale = 4096.0


def gather_mean(pieces, neighbours, after):
    width = pieces[0].shape[1]
    degree, nodes = neighbours.shape
    size = sum(piece.shape[0] for piece in pieces)
    chunk = 512
    for piece in pieces:
        chunk = math.gcd(chunk, piece.shape[0])

    def kernel(nb_ref, *refs):
        piece_refs = refs[: len(pieces)]
        out_ref = refs[len(pieces) + 1]
        tab_ref = refs[len(pieces) + 2]
        start = 0
        for piece_ref, piece in zip(piece_refs, pieces):

            def fill(c, carry, piece_ref=piece_ref, start=start):
                r = pl.multiple_of(c * chunk, chunk)
                tab_ref[pl.ds(start + r, chunk), :] = piece_ref[pl.ds(r, chunk), :].astype(jnp.float32)
                return carry

            lax.fori_loop(0, piece.shape[0] // chunk, fill, 0)
            start += piece.shape[0]

        def body(n, carry):
            acc = tab_ref[pl.ds(nb_ref[0, n], 1), :]
            for k in range(1, degree):
                acc = acc + tab_ref[pl.ds(nb_ref[k, n], 1), :]
            out_ref[pl.ds(n, 1), :] = acc / degree
            return carry

        lax.fori_loop(0, nodes, body, 0, unroll=16)

    return pl.pallas_call(
        kernel,
        in_specs=[pl.BlockSpec(memory_space=pltpu.SMEM)]
        + [pl.BlockSpec(memory_space=pltpu.VMEM) for _ in pieces]
        + [pl.BlockSpec(memory_space=pl.ANY)],
        out_specs=pl.BlockSpec(memory_space=pltpu.VMEM),
        out_shape=jax.ShapeDtypeStruct((nodes, width), jnp.float32),
        scratch_shapes=[pltpu.VMEM((size, width), jnp.float32)],
    )(neighbours, *pieces, after)


def scatter_mean(rows, neighbours, size, chains=4):
    nodes, width = rows.shape
    degree = neighbours.shape[0]
    per_chain = degree // chains

    def kernel(nb_ref, rows_ref, out_ref, *extra_refs):
        accumulators = (out_ref,) + extra_refs
        for acc_ref in accumulators:
            acc_ref[...] = jnp.zeros_like(acc_ref)

        def step(n, carry):
            x = rows_ref[pl.ds(n, 1), :]
            for k in range(per_chain):
                for chain, acc_ref in enumerate(accumulators):
                    s = nb_ref[chain * per_chain + k, n]
                    acc_ref[pl.ds(s, 1), :] = acc_ref[pl.ds(s, 1), :] + x
            return carry

        lax.fori_loop(0, nodes, step, 0, unroll=4)
        total = out_ref[...]
        for acc_ref in extra_refs:
            total = total + acc_ref[...]
        out_ref[...] = total * (1.0 / degree)

    return pl.pallas_call(
        kernel,
        in_specs=[
            pl.BlockSpec(memory_space=pltpu.SMEM),
            pl.BlockSpec(memory_space=pltpu.VMEM),
        ],
        out_specs=pl.BlockSpec(memory_space=pltpu.VMEM),
        out_shape=jax.ShapeDtypeStruct((size, width), jnp.float32),
        scratch_shapes=[pltpu.VMEM((size, width), jnp.float32) for _ in range(chains - 1)],
        compiler_params=pltpu.CompilerParams(vmem_limit_bytes=63 * 1024 * 1024),
    )(neighbours, rows)


def spread_gather(value, axis):
    count = lax.axis_size(axis)
    copies = jnp.broadcast_to(value[None], (count,) + value.shape)
    gathered = lax.all_to_all(copies, axis, 0, 0, tiled=True)
    return gathered.reshape(count * value.shape[0], value.shape[1])


def feat_gather(value, axis):
    count = lax.axis_size(axis)
    index = lax.axis_index(axis)
    got = [value] + [
        lax.ppermute(value, axis, [(source, (source + shift) % count) for source in range(count)])
        for shift in range(1, count)
    ]
    stacked = jnp.stack(got[::-1] * 2)
    full = lax.dynamic_slice_in_dim(stacked, (count - 1 - index) % count, count, axis=0)
    return full.reshape(count * value.shape[0], value.shape[1])


def land_rows(base, targets, updates):
    count, width = updates.shape
    half = count // 2

    def kernel(t_ref, base_ref, upd_ref, out_ref, extra_ref):
        out_ref[...] = base_ref[...]
        extra_ref[...] = jnp.zeros_like(extra_ref)

        def step(i, carry):
            s = t_ref[i]
            t = t_ref[i + half]
            out_ref[pl.ds(s, 1), :] = out_ref[pl.ds(s, 1), :] + upd_ref[pl.ds(i, 1), :]
            extra_ref[pl.ds(t, 1), :] = extra_ref[pl.ds(t, 1), :] + upd_ref[pl.ds(i + half, 1), :]
            return carry

        lax.fori_loop(0, half, step, 0, unroll=4)
        for i in range(2 * half, count):
            s = t_ref[i]
            out_ref[pl.ds(s, 1), :] = out_ref[pl.ds(s, 1), :] + upd_ref[pl.ds(i, 1), :]
        out_ref[...] = out_ref[...] + extra_ref[...]

    return pl.pallas_call(
        kernel,
        in_specs=[
            pl.BlockSpec(memory_space=pltpu.SMEM),
            pl.BlockSpec(memory_space=pltpu.VMEM),
            pl.BlockSpec(memory_space=pltpu.VMEM),
        ],
        out_specs=pl.BlockSpec(memory_space=pltpu.VMEM),
        out_shape=jax.ShapeDtypeStruct(base.shape, jnp.float32),
        scratch_shapes=[pltpu.VMEM(base.shape, jnp.float32)],
    )(targets, base, updates)


def tree_gather(value, axis):
    count = lax.axis_size(axis)
    index = lax.axis_index(axis)
    block = value
    stride = 1
    while stride < count:
        pairs = [(source, source ^ stride) for source in range(count)]
        other = lax.ppermute(block, axis, pairs)
        low = (index // stride) % 2 == 0
        block = jnp.where(
            low, jnp.concatenate([block, other], axis=0), jnp.concatenate([other, block], axis=0)
        )
        stride *= 2
    return block


def exchange_sum(flat, axis):
    count = lax.axis_size(axis)
    length = flat.shape[0]
    padded = jnp.pad(flat, (0, (-length) % count)).reshape(count, -1)
    reduced = jnp.sum(lax.all_to_all(padded, axis, 0, 0, tiled=True), axis=0)
    spread = jnp.broadcast_to(reduced[None], (count, reduced.shape[0]))
    return lax.all_to_all(spread, axis, 0, 0, tiled=True).reshape(-1)[:length]


def tree_sum(value, axis):
    count = lax.axis_size(axis)
    stride = 1
    while stride < count:
        pairs = [(source, source ^ stride) for source in range(count)]
        value = value + lax.ppermute(value, axis, pairs)
        stride *= 2
    return value


def tree_scatter(value, axis):
    count = lax.axis_size(axis)
    index = lax.axis_index(axis)
    width = value.shape[1]
    parts = value.reshape(count, -1, width)
    rows = parts.shape[1]
    stride = 1
    while stride < count:
        bit = (index // stride) % 2
        paired = parts.reshape(parts.shape[0] // 2, 2, rows, width)
        keep = lax.dynamic_index_in_dim(paired, bit, axis=1, keepdims=False)
        send = lax.dynamic_index_in_dim(paired, 1 - bit, axis=1, keepdims=False)
        pairs = [(source, source ^ stride) for source in range(count)]
        parts = keep + lax.ppermute(send, axis, pairs)
        stride *= 2
    return parts.reshape(rows, width)


def partner(value, axis, stride):
    mask = 2**stride
    pairs = [(source, source ^ mask) for source in range(lax.axis_size(axis))]
    return lax.ppermute(value, axis, pairs)


def trade(piece, bit_index):
    return partner(piece, "dom", bit_index)


def widen(first_rows, second_rows):
    return (
        lax.all_gather(first_rows, "feat", axis=0, tiled=True),
        lax.all_gather(second_rows, "feat", axis=0, tiled=True),
    )


def average(pieces, neighbours, after):
    summed = gather_mean(pieces, neighbours, after)
    return summed.T.astype(jnp.bfloat16)


def source_table(local, hub_rows, send_rows):
    local_rows = local.T
    hub_local = jnp.take(local_rows, hub_rows, axis=0)
    owners = lax.axis_size("dom")
    hub_all = lax.all_to_all(
        jnp.broadcast_to(hub_local[None], (owners,) + hub_local.shape), "dom", 0, 0, tiled=True
    ).reshape(owners * hub_local.shape[0], hub_local.shape[1])
    received = [
        trade(jnp.take(local_rows, send_rows[bit_index], axis=0), bit_index)
        for bit_index in range(send_rows.shape[0])
    ]
    return [local_rows, hub_all] + received


def contract(left, right):
    return lax.dot_general(
        left, right, (((1,), (1,)), ((), ())), preferred_element_type=jnp.float32
    )


def transpose_times(left, right):
    return lax.dot_general(
        left, right, (((0,), (0,)), ((), ())), preferred_element_type=jnp.float32
    )


def class_gradient(logits, labels, nodes_all):
    expd = jnp.exp(logits)
    probs = expd / jnp.sum(expd, axis=0, keepdims=True)
    classes = lax.broadcasted_iota(jnp.int32, logits.shape, 0)
    onehot = (classes == labels[None, :]).astype(jnp.float32)
    return ((probs - onehot) * (loss_scale / nodes_all)).astype(jnp.bfloat16)


def body(
    features,
    neighbours,
    hub_rows,
    send_rows,
    labels,
    inner_self,
    inner_neighbour,
    outer_self,
    outer_neighbour,
):
    rows = features.shape[1]
    nodes_all = rows * lax.axis_size("dom")
    full_input = feat_gather(features, "feat")
    mean_one = average(source_table(features, hub_rows, send_rows), neighbours, full_input)
    full_mean = spread_gather(mean_one, "feat")
    pre_act = jnp.dot(inner_self, full_input, preferred_element_type=jnp.float32)
    pre_act = pre_act + jnp.dot(inner_neighbour, full_mean, preferred_element_type=jnp.float32)
    hidden = jnp.maximum(pre_act, 0.0).astype(jnp.bfloat16)
    mean_two = average(source_table(hidden, hub_rows, send_rows), neighbours, hidden)
    width = hidden.shape[0]
    offset = lax.axis_index("feat") * width
    self_cols = lax.dynamic_slice_in_dim(outer_self, offset, width, 1)
    neigh_cols = lax.dynamic_slice_in_dim(outer_neighbour, offset, width, 1)
    full_hidden = lax.all_gather(hidden, "feat", axis=0, tiled=True)
    full_two = spread_gather(mean_two, "feat")
    logits = jnp.dot(outer_self, full_hidden, preferred_element_type=jnp.float32)
    logits = logits + jnp.dot(outer_neighbour, full_two, preferred_element_type=jnp.float32)
    logit_grad = class_gradient(logits, labels, nodes_all)
    grad_outer_self = contract(logit_grad, hidden)
    grad_outer_neighbour = contract(logit_grad, mean_two)
    direct = transpose_times(self_cols, logit_grad)
    back_mean = transpose_times(neigh_cols, logit_grad).astype(jnp.bfloat16)
    degree = neighbours.shape[0]
    hub_count = lax.axis_size("dom") * hub_rows.shape[0]
    band = send_rows.shape[1]
    span = rows + hub_count + send_rows.shape[0] * band
    back_rows = back_mean.T.astype(jnp.float32)
    spread = scatter_mean(back_rows, neighbours, span)
    grad_rows = direct.T + spread[:rows]
    owners = lax.axis_size("dom")
    hub_flat = spread[rows : rows + hub_count].astype(jnp.bfloat16)
    hub_back = jnp.sum(
        lax.all_to_all(hub_flat, "dom", 0, 0, tiled=True)
        .astype(jnp.float32)
        .reshape(owners, hub_count // owners, width),
        axis=0,
    )
    base = rows + hub_count
    landed = [hub_back]
    for bit_index in range(send_rows.shape[0]):
        outgoing = spread[base + bit_index * band : base + (bit_index + 1) * band].astype(
            jnp.bfloat16
        )
        landed.append(trade(outgoing, bit_index).astype(jnp.float32))
    targets = jnp.concatenate([hub_rows, send_rows.reshape(-1)])
    grad_rows = land_rows(grad_rows, targets, jnp.concatenate(landed, axis=0))
    grad_hidden = grad_rows.T
    grad_pre = jnp.where(hidden > 0, grad_hidden, 0.0).astype(jnp.bfloat16)
    grad_inner_self = contract(grad_pre, full_input)
    grad_inner_neighbour = contract(grad_pre, full_mean)
    pieces = (grad_inner_self, grad_inner_neighbour, grad_outer_self, grad_outer_neighbour)
    summed = exchange_sum(jnp.concatenate([piece.reshape(-1) for piece in pieces]), "dom")
    results = []
    offset = 0
    for piece in pieces:
        results.append(summed[offset : offset + piece.size].reshape(piece.shape))
        offset += piece.size
    return tuple(results)


def solution(mesh):
    return jax.shard_map(
        body,
        mesh=mesh,
        in_specs=(
            P("feat", "dom"),
            P(None, "dom"),
            P("dom"),
            P("dom", None),
            P("dom"),
            P("feat", None),
            P("feat", None),
            P(),
            P(),
        ),
        out_specs=(P("feat", None), P("feat", None), P(None, "feat"), P(None, "feat")),
        check_vma=False,
    )
```

```python
import math

import jax
import jax.numpy as jnp
from jax import lax
from jax.sharding import PartitionSpec as P

from jax.experimental import pallas as pl
from jax.experimental.pallas import tpu as pltpu

loss_scale = 4096.0


def gather_mean(pieces, neighbours, after):
    width = pieces[0].shape[1]
    degree, nodes = neighbours.shape
    size = sum(piece.shape[0] for piece in pieces)
    chunk = 512
    for piece in pieces:
        chunk = math.gcd(chunk, piece.shape[0])

    def kernel(nb_ref, *refs):
        piece_refs = refs[: len(pieces)]
        out_ref = refs[len(pieces) + 1]
        tab_ref = refs[len(pieces) + 2]
        start = 0
        for piece_ref, piece in zip(piece_refs, pieces):

            def fill(c, carry, piece_ref=piece_ref, start=start):
                r = pl.multiple_of(c * chunk, chunk)
                tab_ref[pl.ds(start + r, chunk), :] = piece_ref[pl.ds(r, chunk), :].astype(jnp.float32)
                return carry

            lax.fori_loop(0, piece.shape[0] // chunk, fill, 0)
            start += piece.shape[0]

        def body(n, carry):
            acc = tab_ref[pl.ds(nb_ref[0, n], 1), :]
            for k in range(1, degree):
                acc = acc + tab_ref[pl.ds(nb_ref[k, n], 1), :]
            out_ref[pl.ds(n, 1), :] = acc / degree
            return carry

        lax.fori_loop(0, nodes, body, 0, unroll=16)

    return pl.pallas_call(
        kernel,
        in_specs=[pl.BlockSpec(memory_space=pltpu.SMEM)]
        + [pl.BlockSpec(memory_space=pltpu.VMEM) for _ in pieces]
        + [pl.BlockSpec(memory_space=pl.ANY)],
        out_specs=pl.BlockSpec(memory_space=pltpu.VMEM),
        out_shape=jax.ShapeDtypeStruct((nodes, width), jnp.float32),
        scratch_shapes=[pltpu.VMEM((size, width), jnp.float32)],
    )(neighbours, *pieces, after)


def scatter_mean(rows, neighbours, size, chains=4):
    nodes, width = rows.shape
    degree = neighbours.shape[0]
    per_chain = degree // chains

    def kernel(nb_ref, rows_ref, out_ref, *extra_refs):
        accumulators = (out_ref,) + extra_refs
        for acc_ref in accumulators:
            acc_ref[...] = jnp.zeros_like(acc_ref)

        def step(n, carry):
            x = rows_ref[pl.ds(n, 1), :]
            for k in range(per_chain):
                for chain, acc_ref in enumerate(accumulators):
                    s = nb_ref[chain * per_chain + k, n]
                    acc_ref[pl.ds(s, 1), :] = acc_ref[pl.ds(s, 1), :] + x
            return carry

        lax.fori_loop(0, nodes, step, 0, unroll=8)
        total = out_ref[...]
        for acc_ref in extra_refs:
            total = total + acc_ref[...]
        out_ref[...] = total * (1.0 / degree)

    return pl.pallas_call(
        kernel,
        in_specs=[
            pl.BlockSpec(memory_space=pltpu.SMEM),
            pl.BlockSpec(memory_space=pltpu.VMEM),
        ],
        out_specs=pl.BlockSpec(memory_space=pltpu.VMEM),
        out_shape=jax.ShapeDtypeStruct((size, width), jnp.float32),
        scratch_shapes=[pltpu.VMEM((size, width), jnp.float32) for _ in range(chains - 1)],
        compiler_params=pltpu.CompilerParams(vmem_limit_bytes=63 * 1024 * 1024),
    )(neighbours, rows)


def spread_gather(value, axis):
    count = lax.axis_size(axis)
    copies = jnp.broadcast_to(value[None], (count,) + value.shape)
    gathered = lax.all_to_all(copies, axis, 0, 0, tiled=True)
    return gathered.reshape(count * value.shape[0], value.shape[1])


def feat_gather(value, axis):
    count = lax.axis_size(axis)
    index = lax.axis_index(axis)
    got = [value] + [
        lax.ppermute(value, axis, [(source, (source + shift) % count) for source in range(count)])
        for shift in range(1, count)
    ]
    stacked = jnp.stack(got[::-1] * 2)
    full = lax.dynamic_slice_in_dim(stacked, (count - 1 - index) % count, count, axis=0)
    return full.reshape(count * value.shape[0], value.shape[1])


def land_rows(base, targets, updates):
    count, width = updates.shape
    half = count // 2

    def kernel(t_ref, base_ref, upd_ref, out_ref, extra_ref):
        out_ref[...] = base_ref[...]
        extra_ref[...] = jnp.zeros_like(extra_ref)

        def step(i, carry):
            s = t_ref[i]
            t = t_ref[i + half]
            out_ref[pl.ds(s, 1), :] = out_ref[pl.ds(s, 1), :] + upd_ref[pl.ds(i, 1), :]
            extra_ref[pl.ds(t, 1), :] = extra_ref[pl.ds(t, 1), :] + upd_ref[pl.ds(i + half, 1), :]
            return carry

        lax.fori_loop(0, half, step, 0, unroll=4)
        for i in range(2 * half, count):
            s = t_ref[i]
            out_ref[pl.ds(s, 1), :] = out_ref[pl.ds(s, 1), :] + upd_ref[pl.ds(i, 1), :]
        out_ref[...] = out_ref[...] + extra_ref[...]

    return pl.pallas_call(
        kernel,
        in_specs=[
            pl.BlockSpec(memory_space=pltpu.SMEM),
            pl.BlockSpec(memory_space=pltpu.VMEM),
            pl.BlockSpec(memory_space=pltpu.VMEM),
        ],
        out_specs=pl.BlockSpec(memory_space=pltpu.VMEM),
        out_shape=jax.ShapeDtypeStruct(base.shape, jnp.float32),
        scratch_shapes=[pltpu.VMEM(base.shape, jnp.float32)],
    )(targets, base, updates)


def tree_gather(value, axis):
    count = lax.axis_size(axis)
    index = lax.axis_index(axis)
    block = value
    stride = 1
    while stride < count:
        pairs = [(source, source ^ stride) for source in range(count)]
        other = lax.ppermute(block, axis, pairs)
        low = (index // stride) % 2 == 0
        block = jnp.where(
            low, jnp.concatenate([block, other], axis=0), jnp.concatenate([other, block], axis=0)
        )
        stride *= 2
    return block


def exchange_sum(flat, axis):
    count = lax.axis_size(axis)
    length = flat.shape[0]
    padded = jnp.pad(flat, (0, (-length) % count)).reshape(count, -1)
    reduced = jnp.sum(lax.all_to_all(padded, axis, 0, 0, tiled=True), axis=0)
    spread = jnp.broadcast_to(reduced[None], (count, reduced.shape[0]))
    return lax.all_to_all(spread, axis, 0, 0, tiled=True).reshape(-1)[:length]


def tree_sum(value, axis):
    count = lax.axis_size(axis)
    stride = 1
    while stride < count:
        pairs = [(source, source ^ stride) for source in range(count)]
        value = value + lax.ppermute(value, axis, pairs)
        stride *= 2
    return value


def tree_scatter(value, axis):
    count = lax.axis_size(axis)
    index = lax.axis_index(axis)
    width = value.shape[1]
    parts = value.reshape(count, -1, width)
    rows = parts.shape[1]
    stride = 1
    while stride < count:
        bit = (index // stride) % 2
        paired = parts.reshape(parts.shape[0] // 2, 2, rows, width)
        keep = lax.dynamic_index_in_dim(paired, bit, axis=1, keepdims=False)
        send = lax.dynamic_index_in_dim(paired, 1 - bit, axis=1, keepdims=False)
        pairs = [(source, source ^ stride) for source in range(count)]
        parts = keep + lax.ppermute(send, axis, pairs)
        stride *= 2
    return parts.reshape(rows, width)


def partner(value, axis, stride):
    mask = 2**stride
    pairs = [(source, source ^ mask) for source in range(lax.axis_size(axis))]
    return lax.ppermute(value, axis, pairs)


def trade(piece, bit_index):
    return partner(piece, "dom", bit_index)


def widen(first_rows, second_rows):
    return (
        lax.all_gather(first_rows, "feat", axis=0, tiled=True),
        lax.all_gather(second_rows, "feat", axis=0, tiled=True),
    )


def average(pieces, neighbours, after):
    summed = gather_mean(pieces, neighbours, after)
    return summed.T.astype(jnp.bfloat16)


def source_table(local, hub_rows, send_rows):
    local_rows = local.T
    hub_local = jnp.take(local_rows, hub_rows, axis=0)
    owners = lax.axis_size("dom")
    hub_all = lax.all_to_all(
        jnp.broadcast_to(hub_local[None], (owners,) + hub_local.shape), "dom", 0, 0, tiled=True
    ).reshape(owners * hub_local.shape[0], hub_local.shape[1])
    received = [
        trade(jnp.take(local_rows, send_rows[bit_index], axis=0), bit_index)
        for bit_index in range(send_rows.shape[0])
    ]
    return [local_rows, hub_all] + received


def contract(left, right):
    return lax.dot_general(
        left, right, (((1,), (1,)), ((), ())), preferred_element_type=jnp.float32
    )


def transpose_times(left, right):
    return lax.dot_general(
        left, right, (((0,), (0,)), ((), ())), preferred_element_type=jnp.float32
    )


def class_gradient(logits, labels, nodes_all):
    expd = jnp.exp(logits)
    probs = expd / jnp.sum(expd, axis=0, keepdims=True)
    classes = lax.broadcasted_iota(jnp.int32, logits.shape, 0)
    onehot = (classes == labels[None, :]).astype(jnp.float32)
    return ((probs - onehot) * (loss_scale / nodes_all)).astype(jnp.bfloat16)


def body(
    features,
    neighbours,
    hub_rows,
    send_rows,
    labels,
    inner_self,
    inner_neighbour,
    outer_self,
    outer_neighbour,
):
    rows = features.shape[1]
    nodes_all = rows * lax.axis_size("dom")
    full_input = feat_gather(features, "feat")
    mean_one = average(source_table(features, hub_rows, send_rows), neighbours, full_input)
    full_mean = spread_gather(mean_one, "feat")
    pre_act = jnp.dot(inner_self, full_input, preferred_element_type=jnp.float32)
    pre_act = pre_act + jnp.dot(inner_neighbour, full_mean, preferred_element_type=jnp.float32)
    hidden = jnp.maximum(pre_act, 0.0).astype(jnp.bfloat16)
    mean_two = average(source_table(hidden, hub_rows, send_rows), neighbours, hidden)
    width = hidden.shape[0]
    offset = lax.axis_index("feat") * width
    self_cols = lax.dynamic_slice_in_dim(outer_self, offset, width, 1)
    neigh_cols = lax.dynamic_slice_in_dim(outer_neighbour, offset, width, 1)
    full_hidden = lax.all_gather(hidden, "feat", axis=0, tiled=True)
    full_two = spread_gather(mean_two, "feat")
    logits = jnp.dot(outer_self, full_hidden, preferred_element_type=jnp.float32)
    logits = logits + jnp.dot(outer_neighbour, full_two, preferred_element_type=jnp.float32)
    logit_grad = class_gradient(logits, labels, nodes_all)
    grad_outer_self = contract(logit_grad, hidden)
    grad_outer_neighbour = contract(logit_grad, mean_two)
    direct = transpose_times(self_cols, logit_grad)
    back_mean = transpose_times(neigh_cols, logit_grad).astype(jnp.bfloat16)
    degree = neighbours.shape[0]
    hub_count = lax.axis_size("dom") * hub_rows.shape[0]
    band = send_rows.shape[1]
    span = rows + hub_count + send_rows.shape[0] * band
    back_rows = back_mean.T.astype(jnp.float32)
    spread = scatter_mean(back_rows, neighbours, span)
    grad_rows = direct.T + spread[:rows]
    owners = lax.axis_size("dom")
    hub_flat = spread[rows : rows + hub_count].astype(jnp.bfloat16)
    hub_back = jnp.sum(
        lax.all_to_all(hub_flat, "dom", 0, 0, tiled=True)
        .astype(jnp.float32)
        .reshape(owners, hub_count // owners, width),
        axis=0,
    )
    base = rows + hub_count
    landed = [hub_back]
    for bit_index in range(send_rows.shape[0]):
        outgoing = spread[base + bit_index * band : base + (bit_index + 1) * band].astype(
            jnp.bfloat16
        )
        landed.append(trade(outgoing, bit_index).astype(jnp.float32))
    targets = jnp.concatenate([hub_rows, send_rows.reshape(-1)])
    grad_rows = land_rows(grad_rows, targets, jnp.concatenate(landed, axis=0))
    grad_hidden = grad_rows.T
    grad_pre = jnp.where(hidden > 0, grad_hidden, 0.0).astype(jnp.bfloat16)
    grad_inner_self = contract(grad_pre, full_input)
    grad_inner_neighbour = contract(grad_pre, full_mean)
    pieces = (grad_inner_self, grad_inner_neighbour, grad_outer_self, grad_outer_neighbour)
    summed = exchange_sum(jnp.concatenate([piece.reshape(-1) for piece in pieces]), "dom")
    results = []
    offset = 0
    for piece in pieces:
        results.append(summed[offset : offset + piece.size].reshape(piece.shape))
        offset += piece.size
    return tuple(results)


def solution(mesh):
    return jax.shard_map(
        body,
        mesh=mesh,
        in_specs=(
            P("feat", "dom"),
            P(None, "dom"),
            P("dom"),
            P("dom", None),
            P("dom"),
            P("feat", None),
            P("feat", None),
            P(),
            P(),
        ),
        out_specs=(P("feat", None), P("feat", None), P(None, "feat"), P(None, "feat")),
        check_vma=False,
    )
```
